128 devices in a mesh: seq: 32 (over y, x, core), head: 4 (over z).
Axes of the slice: x: 4, y: 4, z: 4, core: 2. Of those that a mesh axis runs over, the one named last changes fastest.
Arguments:
- value_rows: bfloat16 [8192, 4096], P('seq', 'head'), may hold values from -6 to 6
- key_rows: bfloat16 [8192, 4096], P('seq', 'head'), may hold values from -6 to 6
- query_rows: bfloat16 [8192, 4096], P('seq', 'head'), may hold values from -6 to 6
- cotangent: bfloat16 [8192, 4096], P('seq', 'head'), may hold values from -6 to 6
- filter_taps: float32 [16, 2048], replicated, may hold values from -0.125 to 0.125
- doc_blocks: int32 [64], replicated, may hold values from 0 to 15, never falling along the last dimension, each value on 1 to 12 neighbouring positions
Outputs:
- output_rows: bfloat16 [8192, 4096], P('seq', 'head')
- grad_query: bfloat16 [8192, 4096], P('seq', 'head')
- grad_key: bfloat16 [8192, 4096], P('seq', 'head')
- grad_value: bfloat16 [8192, 4096], P('seq', 'head')
- grad_filter: float32 [16, 2048], replicated
The draws below stay inside these ranges and needn't reach their ends.
Inputs may be any that keep to these rules, and one draw needn't show every extreme that they name: doc_blocks gives each 128-token block its document number; numbers never fall, each document spans 1 to 12 blocks, and one spans exactly 12.
All inputs are finite; a program needn't handle non-finite values.
Results may differ from the reference program's by a relative error of at most 0.0058.
Values may be sent and summed in bfloat16 or wider, within the bound.
No kernel may reach another device: no remote copies, remote signals or barrier semaphores. Data moves between devices by JAX's collectives and lax.ppermute only.
A program may use at most 384 MiB of HBM per device.

```python
import math
import jax
import jax.numpy as jnp
import numpy as np

H = 64
DH = 64
FILTERS = 16
K = 2048
BLK = 128
TOKENS = 8192
CH = 4096
NBLK = 64
DOCS = 16
MOST = 12


def levels(key, dims, shards, low, high):
    loudness, own = 1.0, jax.random.fold_in(key, 6)
    for axis_at, parts in shards:
        draws = jnp.exp(jax.random.uniform(jax.random.fold_in(own, axis_at), (parts,), jnp.float32, low / len(shards), high / len(shards)))
        loudness = loudness * jnp.repeat(draws, dims[axis_at] // parts).reshape([-1 if axis == axis_at else 1 for axis in range(len(dims))])
    return loudness


def split_up(amount, total, bound, skew):
    portions = [(1 << 20) // math.isqrt(rank ** skew) + 1 for rank in range(2, amount + 1)]
    rest, counts = total - bound - (amount - 1), [1] * (amount - 1)
    while rest > 0:
        free = [i for i in range(amount - 1) if counts[i] < bound]
        whole, remaining = sum([portions[i] for i in free]), rest
        for i in free:
            more = min(bound - counts[i], max(1, remaining * portions[i] // whole), rest)
            counts[i] = counts[i] + more
            rest = rest - more
    return np.array([bound] + counts)


def uneven_parts(key, number_of, total, bound, slope):
    if number_of == 2:
        one = jax.random.randint(key, (), max(1, total - bound), min(bound, total - 1) + 1)
        return jnp.stack([one, total - one])
    sizes = jnp.asarray(split_up(number_of, total, bound, slope), jnp.int32)
    couples = (number_of - 1) // 2
    donor, receiver = sizes[1:1 + 2 * couples:2], sizes[2:2 + 2 * couples:2]
    margin = jnp.minimum(donor - 1, bound - receiver)
    moved = jax.random.randint(jax.random.fold_in(key, 1), (couples,), 0, 1 << 20) % (margin + 1)
    sizes = sizes.at[1:1 + 2 * couples:2].set(donor - moved).at[2:2 + 2 * couples:2].set(receiver + moved)
    return sizes[jax.random.permutation(jax.random.fold_in(key, 2), number_of)]


def bell_draw(rng, dims, width, limit, split=(), held_as=jnp.bfloat16):
    values = jax.random.normal(rng, dims, jnp.float32) * width
    if len(split) > 0:
        values = levels(rng, dims, split, -0.22, 0.18) * values
    return jnp.clip(values, min=-limit, max=limit).astype(held_as)


def setup_inputs(seed: int = 0) -> dict:
    splits = jax.random.split(jax.random.key(seed), 7)
    value_rows = bell_draw(splits[0], (TOKENS, CH), 1.0, 6.0, ((0, 32), (1, 4)))
    key_rows = bell_draw(splits[1], (TOKENS, CH), 1.0, 6.0, ((0, 32), (1, 4)))
    query_rows = bell_draw(splits[2], (TOKENS, CH), 1.0, 6.0, ((0, 32), (1, 4)))
    cotangent = bell_draw(splits[3], (TOKENS, CH), 1.0, 6.0, ((0, 32), (1, 4)))
    filter_taps = bell_draw(splits[4], (FILTERS, K), K ** -0.5, 0.125, (), jnp.float32)
    doc_blocks = jnp.searchsorted(jnp.cumsum(uneven_parts(splits[5], DOCS, NBLK, MOST, 1)), jnp.arange(NBLK), side="right").astype(jnp.int32)
    return dict(value_rows=value_rows, key_rows=key_rows, query_rows=query_rows, cotangent=cotangent, filter_taps=filter_taps, doc_blocks=doc_blocks)


def toeplitz_blocks(filter_taps):
    lags_count = K // BLK + 1
    offsets = (jnp.arange(lags_count)[:, None, None] * BLK + jnp.arange(BLK)[None, :, None] - jnp.arange(BLK)[None, None, :]).astype(jnp.int32)
    inside = (offsets >= 0) & (offsets < K)
    safe_index = jnp.clip(offsets, 0, K - 1).astype(jnp.int32)
    rounded = filter_taps.astype(jnp.bfloat16)
    table = jnp.take(rounded, safe_index.reshape(-1), axis=1).reshape(FILTERS, lags_count, BLK, BLK)
    table = jnp.where(inside[None], table, jnp.zeros_like(table))
    return table, safe_index, inside


def reference(value_rows, key_rows, query_rows, cotangent, filter_taps, doc_blocks):
    blocks = TOKENS // BLK
    groups = H // FILTERS
    channels = H * DH
    lags_count = K // BLK + 1
    toeplitz, safe_index, inside = toeplitz_blocks(filter_taps)
    toeplitz_wide = toeplitz.astype(jnp.float32)
    product = (key_rows.astype(jnp.float32) * value_rows.astype(jnp.float32)).astype(jnp.bfloat16)
    scaled = (cotangent.astype(jnp.float32) * query_rows.astype(jnp.float32)).astype(jnp.bfloat16)
    shape5 = (blocks, BLK, groups, FILTERS, DH)
    past_blocks = product.astype(jnp.float32).reshape(shape5)
    fore_blocks = scaled.astype(jnp.float32).reshape(shape5)
    convolved = jnp.zeros(shape5, jnp.float32)
    adjoint = jnp.zeros(shape5, jnp.float32)
    grad_list = []
    for b in range(lags_count):
        filler = jnp.zeros((b, BLK, groups, FILTERS, DH), jnp.float32)
        source = jnp.concatenate([filler, past_blocks[:blocks - b]], 0)
        earlier = jnp.concatenate([jnp.full((b,), -1, jnp.int32), doc_blocks[:blocks - b]], 0)
        keep = (earlier == doc_blocks).astype(jnp.float32)
        source = source * keep[:, None, None, None, None]
        convolved = convolved + jnp.einsum('frs,nsgfd->nrgfd', toeplitz_wide[:, b], source)
        grad_list.append(jnp.einsum('nrgfd,nsgfd->frs', fore_blocks, source))
        later = jnp.concatenate([fore_blocks[b:], filler], 0)
        later_docs = jnp.concatenate([doc_blocks[b:], jnp.full((b,), -2, jnp.int32)], 0)
        keep_back = (later_docs == doc_blocks).astype(jnp.float32)
        later = later * keep_back[:, None, None, None, None]
        adjoint = adjoint + jnp.einsum('frs,nrgfd->nsgfd', toeplitz_wide[:, b], later)
    grad_blocks = jnp.stack(grad_list, 1)
    weighted = jnp.where(inside[None], grad_blocks, jnp.zeros_like(grad_blocks))
    grad_filter = jnp.zeros((FILTERS, K), jnp.float32).at[:, safe_index.reshape(-1)].add(weighted.reshape(FILTERS, -1))
    grad_filter = grad_filter / TOKENS
    convolved = convolved.reshape(TOKENS, channels)
    adjoint = adjoint.reshape(TOKENS, channels)
    output_rows = (query_rows.astype(jnp.float32) * convolved).astype(jnp.bfloat16)
    grad_query = (cotangent.astype(jnp.float32) * convolved).astype(jnp.bfloat16)
    grad_key = (adjoint * value_rows.astype(jnp.float32)).astype(jnp.bfloat16)
    grad_value = (adjoint * key_rows.astype(jnp.float32)).astype(jnp.bfloat16)
    return (output_rows, grad_query, grad_key, grad_value, grad_filter)
```

```python
import numpy as np
import jax
import jax.numpy as jnp
from jax import lax
from jax.experimental import pallas as pl
from jax.experimental.pallas import tpu as pltpu
from jax.sharding import PartitionSpec as P

DH = 64
BLK = 128


def passed_along(value, axis, by):
    length = lax.axis_size(axis)
    pairs = [(i, i + by) for i in range(length) if 0 <= i + by < length]
    return lax.ppermute(value, axis, pairs)


def tap_rows(rounded, index):
    filters, taps_total = rounded.shape
    padded = jnp.concatenate([rounded, jnp.zeros((filters, 1), jnp.float32)], 1)
    safe = np.where((index >= 0) & (index < taps_total), index, taps_total)
    return jnp.take(padded, jnp.asarray(safe, jnp.int32), axis=1)


def make_kernel(nb, lags, width, span, conv_start):
    def kernel(qc_ref, qa_ref, cm_ref, pext_ref, sext_ref, srev_ref, q_ref, ct_ref,
               k_ref, v_ref, out_ref, gq_ref, gk_ref, gv_ref, gd_ref):
        step = pl.program_id(0)
        lo = lax.broadcasted_iota(jnp.int32, (BLK, BLK), 1) < DH

        def table(ref, i, shift):
            row = ref[pl.ds(2 * step + i, 1), :]
            full = jnp.broadcast_to(row, (BLK, span))
            rolled = pltpu.roll(full, shift, 1, stride=1, stride_axis=0)
            return rolled[:, :width]

        tc = jnp.concatenate(
            [table(qc_ref, 0, span - (BLK - 1)), table(qc_ref, 1, span - (BLK - 1))], 0
        )
        ta = jnp.concatenate([table(qa_ref, 0, span - BLK), table(qa_ref, 1, span - BLK)], 0)
        gsum = jnp.zeros((2 * BLK, width), jnp.float32)
        for n in range(nb):
            rows = pl.ds(n * BLK, BLK)
            cmask = cm_ref[n : n + 1, :]
            amask = cm_ref[nb + n : nb + n + 1, :]
            pw = pext_ref[pl.ds(conv_start + n * BLK, width), :]
            sw = sext_ref[pl.ds(n * BLK, width), :]
            conv2 = jnp.dot(
                (tc * cmask).astype(jnp.bfloat16), pw, preferred_element_type=jnp.float32
            )
            conv = jnp.where(lo, conv2[:BLK], conv2[BLK:])
            adj2 = jnp.dot(
                (ta * amask).astype(jnp.bfloat16), sw, preferred_element_type=jnp.float32
            )
            adj = jnp.where(lo, adj2[:BLK], adj2[BLK:])
            out_ref[rows, :] = (q_ref[rows, :].astype(jnp.float32) * conv).astype(jnp.bfloat16)
            gq_ref[rows, :] = (ct_ref[rows, :].astype(jnp.float32) * conv).astype(jnp.bfloat16)
            gk_ref[rows, :] = (adj * v_ref[rows, :].astype(jnp.float32)).astype(jnp.bfloat16)
            gv_ref[rows, :] = (adj * k_ref[rows, :].astype(jnp.float32)).astype(jnp.bfloat16)
            sr = srev_ref[rows, :]
            zero = jnp.zeros_like(sr)
            a = jnp.concatenate([jnp.where(lo, sr, zero), jnp.where(lo, zero, sr)], 0)
            g = lax.dot_general(
                a, pw, (((1,), (1,)), ((), ())), preferred_element_type=jnp.float32
            )
            gsum = gsum + g * cmask
        d0 = pltpu.roll(gsum[:BLK], 0, 1, stride=1, stride_axis=0).sum(0, keepdims=True)
        d1 = pltpu.roll(gsum[BLK:], 0, 1, stride=1, stride_axis=0).sum(0, keepdims=True)
        gd_ref[0] = jnp.concatenate([d0, d1], 0)

    return kernel


def per_device(value_rows, key_rows, query_rows, cotangent, filter_taps, doc_blocks):
    tok_rows, channels = value_rows.shape
    filters, taps_total = filter_taps.shape
    nb = tok_rows // BLK
    reach = -(-taps_total // tok_rows)
    lags = taps_total // BLK + 1
    width = lags * BLK
    span = width + BLK
    base = (lags - 1) * BLK
    steps = channels // BLK
    product = (key_rows.astype(jnp.float32) * value_rows.astype(jnp.float32)).astype(jnp.bfloat16)
    scaled = (cotangent.astype(jnp.float32) * query_rows.astype(jnp.float32)).astype(jnp.bfloat16)
    earlier = [passed_along(product, "seq", d) for d in range(reach, 0, -1)]
    later = [passed_along(scaled, "seq", -d) for d in range(1, reach + 1)]
    pext = jnp.concatenate(earlier + [product], 0)
    sext = jnp.concatenate([scaled] + later, 0)
    srev = scaled.reshape(nb, BLK, channels)[:, ::-1].reshape(tok_rows, channels)
    own0 = reach * nb
    conv_start = (own0 - (lags - 1)) * BLK

    rounded = filter_taps.astype(jnp.bfloat16).astype(jnp.float32)
    k_idx = np.arange(span)
    qc = tap_rows(rounded, base + BLK - 1 - k_idx)
    qa = tap_rows(rounded, k_idx - BLK)

    nblk = doc_blocks.shape[0]
    margin = lags + nb
    padded = jnp.concatenate(
        [jnp.full((margin,), -1, jnp.int32), doc_blocks, jnp.full((margin,), -2, jnp.int32)], 0
    )
    shard = lax.axis_index("seq")
    window = lax.dynamic_slice_in_dim(padded, shard * nb + margin - (lags - 1), 2 * (lags - 1) + nb)
    own = jnp.stack([window[lags - 1 + n] for n in range(nb)])
    conv_docs = jnp.stack([window[n : n + lags] for n in range(nb)])
    adj_docs = jnp.stack([window[lags - 1 + n : lags - 1 + n + lags] for n in range(nb)])
    links = jnp.concatenate([conv_docs == own[:, None], adj_docs == own[:, None]], 0)
    cm = jnp.repeat(links.astype(jnp.float32), BLK, axis=1)

    ext_rows = pext.shape[0]
    whole = lambda shape: pl.BlockSpec(shape, lambda s: (0, 0))
    lanes = lambda r: pl.BlockSpec((r, BLK), lambda s: (0, s))
    kernel = make_kernel(nb, lags, width, span, conv_start)
    outs = pl.pallas_call(
        kernel,
        grid=(steps,),
        in_specs=[
            whole((filters, span)),
            whole((filters, span)),
            whole((2 * nb, width)),
            lanes(ext_rows),
            lanes(ext_rows),
            lanes(tok_rows),
            lanes(tok_rows),
            lanes(tok_rows),
            lanes(tok_rows),
            lanes(tok_rows),
        ],
        out_specs=[
            lanes(tok_rows),
            lanes(tok_rows),
            lanes(tok_rows),
            lanes(tok_rows),
            pl.BlockSpec((1, 2, width), lambda s: (s, 0, 0)),
        ],
        out_shape=[
            jax.ShapeDtypeStruct((tok_rows, channels), jnp.bfloat16),
            jax.ShapeDtypeStruct((tok_rows, channels), jnp.bfloat16),
            jax.ShapeDtypeStruct((tok_rows, channels), jnp.bfloat16),
            jax.ShapeDtypeStruct((tok_rows, channels), jnp.bfloat16),
            jax.ShapeDtypeStruct((steps, 2, width), jnp.float32),
        ],
        compiler_params=pltpu.CompilerParams(
            dimension_semantics=("arbitrary",), vmem_limit_bytes=48 * 1024 * 1024
        ),
    )(qc, qa, cm, pext, sext, srev, query_rows, cotangent, key_rows, value_rows)
    output_rows, grad_query, grad_key, grad_value, diag = outs
    diag = diag.reshape(filters, width)
    j_idx = base + BLK - 1 - np.arange(taps_total)
    taps_grad = tap_rows_any(diag, j_idx) * (1.0 / (tok_rows * lax.axis_size("seq")))
    grad_filter = lax.psum(taps_grad, ("seq", "head"))
    return (output_rows, grad_query, grad_key, grad_value, grad_filter)


def tap_rows_any(values, index):
    rows, cols = values.shape
    padded = jnp.concatenate([values, jnp.zeros((rows, 1), values.dtype)], 1)
    safe = np.where((index >= 0) & (index < cols), index, cols)
    return jnp.take(padded, jnp.asarray(safe, jnp.int32), axis=1)


def solution(mesh):
    in_specs = (P("seq", "head"), P("seq", "head"), P("seq", "head"), P("seq", "head"), P(), P())
    out_specs = (P("seq", "head"), P("seq", "head"), P("seq", "head"), P("seq", "head"), P())
    return jax.shard_map(
        per_device, mesh=mesh, in_specs=in_specs, out_specs=out_specs, check_vma=False
    )
```

```python
import numpy as np
import jax
import jax.numpy as jnp
from jax import lax
from jax.experimental import pallas as pl
from jax.experimental.pallas import tpu as pltpu
from jax.sharding import PartitionSpec as P

DH = 64
BLK = 128


def passed_along(value, axis, by):
    length = lax.axis_size(axis)
    pairs = [(i, i + by) for i in range(length) if 0 <= i + by < length]
    return lax.ppermute(value, axis, pairs)


def tap_rows(rounded, index):
    filters, taps_total = rounded.shape
    padded = jnp.concatenate([rounded, jnp.zeros((filters, 1), jnp.float32)], 1)
    safe = np.where((index >= 0) & (index < taps_total), index, taps_total)
    return jnp.take(padded, jnp.asarray(safe, jnp.int32), axis=1)


def make_kernel(nb, lags, width, span, conv_start):
    def kernel(qc_ref, qa_ref, cm_ref, pext_ref, sext_ref, srev_ref, q_ref, ct_ref,
               k_ref, v_ref, out_ref, gq_ref, gk_ref, gv_ref, gd_ref):
        step = pl.program_id(0)
        lo = lax.broadcasted_iota(jnp.int32, (BLK, BLK), 1) < DH

        def table(ref, i, shift):
            row = ref[pl.ds(2 * step + i, 1), :]
            full = jnp.broadcast_to(row, (BLK, span))
            rolled = pltpu.roll(full, shift, 1, stride=1, stride_axis=0)
            return rolled[:, :width]

        tc = jnp.concatenate(
            [table(qc_ref, 0, span - (BLK - 1)), table(qc_ref, 1, span - (BLK - 1))], 0
        )
        ta = jnp.concatenate([table(qa_ref, 0, span - BLK), table(qa_ref, 1, span - BLK)], 0)
        gsum = jnp.zeros((2 * BLK, width), jnp.float32)
        for n in range(nb):
            rows = pl.ds(n * BLK, BLK)
            cmask = cm_ref[n : n + 1, :]
            amask = cm_ref[nb + n : nb + n + 1, :]
            pw = pext_ref[pl.ds(conv_start + n * BLK, width), :]
            sw = sext_ref[pl.ds(n * BLK, width), :]
            conv2 = jnp.dot(
                (tc * cmask).astype(jnp.bfloat16), pw, preferred_element_type=jnp.float32
            )
            conv = jnp.where(lo, conv2[:BLK], conv2[BLK:])
            adj2 = jnp.dot(
                (ta * amask).astype(jnp.bfloat16), sw, preferred_element_type=jnp.float32
            )
            adj = jnp.where(lo, adj2[:BLK], adj2[BLK:])
            out_ref[rows, :] = (q_ref[rows, :].astype(jnp.float32) * conv).astype(jnp.bfloat16)
            gq_ref[rows, :] = (ct_ref[rows, :].astype(jnp.float32) * conv).astype(jnp.bfloat16)
            gk_ref[rows, :] = (adj * v_ref[rows, :].astype(jnp.float32)).astype(jnp.bfloat16)
            gv_ref[rows, :] = (adj * k_ref[rows, :].astype(jnp.float32)).astype(jnp.bfloat16)
            sr = srev_ref[rows, :]
            zero = jnp.zeros_like(sr)
            a = jnp.concatenate([jnp.where(lo, sr, zero), jnp.where(lo, zero, sr)], 0)
            g = lax.dot_general(
                a, pw, (((1,), (1,)), ((), ())), preferred_element_type=jnp.float32
            )
            gsum = gsum + g * cmask
        d0 = pltpu.roll(gsum[:BLK], 0, 1, stride=1, stride_axis=0).sum(0, keepdims=True)
        d1 = pltpu.roll(gsum[BLK:], 0, 1, stride=1, stride_axis=0).sum(0, keepdims=True)
        gd_ref[0] = jnp.concatenate([d0, d1], 0)

    return kernel


def per_device(value_rows, key_rows, query_rows, cotangent, filter_taps, doc_blocks):
    tok_rows, channels = value_rows.shape
    filters, taps_total = filter_taps.shape
    nb = tok_rows // BLK
    reach = -(-taps_total // tok_rows)
    lags = taps_total // BLK + 1
    width = lags * BLK
    span = width + BLK
    base = (lags - 1) * BLK
    steps = channels // BLK
    product = (key_rows.astype(jnp.float32) * value_rows.astype(jnp.float32)).astype(jnp.bfloat16)
    scaled = (cotangent.astype(jnp.float32) * query_rows.astype(jnp.float32)).astype(jnp.bfloat16)
    earlier = [passed_along(product, "seq", d) for d in range(reach, 0, -1)]
    later = [passed_along(scaled, "seq", -d) for d in range(1, reach + 1)]
    pext = jnp.concatenate(earlier + [product], 0)
    sext = jnp.concatenate([scaled] + later, 0)
    srev = scaled.reshape(nb, BLK, channels)[:, ::-1].reshape(tok_rows, channels)
    own0 = reach * nb
    conv_start = (own0 - (lags - 1)) * BLK

    rounded = filter_taps.astype(jnp.bfloat16).astype(jnp.float32)
    k_idx = np.arange(span)
    qc = tap_rows(rounded, base + BLK - 1 - k_idx)
    qa = tap_rows(rounded, k_idx - BLK)

    nblk = doc_blocks.shape[0]
    margin = lags + nb
    padded = jnp.concatenate(
        [jnp.full((margin,), -1, jnp.int32), doc_blocks, jnp.full((margin,), -2, jnp.int32)], 0
    )
    shard = lax.axis_index("seq")
    window = lax.dynamic_slice_in_dim(padded, shard * nb + margin - (lags - 1), 2 * (lags - 1) + nb)
    own = jnp.stack([window[lags - 1 + n] for n in range(nb)])
    conv_docs = jnp.stack([window[n : n + lags] for n in range(nb)])
    adj_docs = jnp.stack([window[lags - 1 + n : lags - 1 + n + lags] for n in range(nb)])
    links = jnp.concatenate([conv_docs == own[:, None], adj_docs == own[:, None]], 0)
    cm = jnp.repeat(links.astype(jnp.float32), BLK, axis=1)

    ext_rows = pext.shape[0]
    whole = lambda shape: pl.BlockSpec(shape, lambda s: (0, 0))
    lanes = lambda r: pl.BlockSpec((r, BLK), lambda s: (0, s))
    kernel = make_kernel(nb, lags, width, span, conv_start)
    outs = pl.pallas_call(
        kernel,
        grid=(steps,),
        in_specs=[
            whole((filters, span)),
            whole((filters, span)),
            whole((2 * nb, width)),
            lanes(ext_rows),
            lanes(ext_rows),
            lanes(tok_rows),
            lanes(tok_rows),
            lanes(tok_rows),
            lanes(tok_rows),
            lanes(tok_rows),
        ],
        out_specs=[
            lanes(tok_rows),
            lanes(tok_rows),
            lanes(tok_rows),
            lanes(tok_rows),
            pl.BlockSpec((1, 2, width), lambda s: (s, 0, 0)),
        ],
        out_shape=[
            jax.ShapeDtypeStruct((tok_rows, channels), jnp.bfloat16),
            jax.ShapeDtypeStruct((tok_rows, channels), jnp.bfloat16),
            jax.ShapeDtypeStruct((tok_rows, channels), jnp.bfloat16),
            jax.ShapeDtypeStruct((tok_rows, channels), jnp.bfloat16),
            jax.ShapeDtypeStruct((steps, 2, width), jnp.float32),
        ],
        compiler_params=pltpu.CompilerParams(
            dimension_semantics=("arbitrary",), vmem_limit_bytes=48 * 1024 * 1024
        ),
    )(qc, qa, cm, pext, sext, srev, query_rows, cotangent, key_rows, value_rows)
    output_rows, grad_query, grad_key, grad_value, diag = outs
    diag = diag.reshape(filters, width)
    j_idx = base + BLK - 1 - np.arange(taps_total)
    taps_grad = tap_rows_any(diag, j_idx) * (1.0 / (tok_rows * lax.axis_size("seq")))
    grad_filter = doubled_total(taps_grad, ("head", "seq"))
    return (output_rows, grad_query, grad_key, grad_value, grad_filter)


def doubled_total(value, axes):
    for axis in axes:
        length = lax.axis_size(axis)
        bit = 1
        while bit < length:
            pairs = [(i, i ^ bit) for i in range(length)]
            value = value + lax.ppermute(value, axis, pairs)
            bit *= 2
    return value


def tap_rows_any(values, index):
    rows, cols = values.shape
    padded = jnp.concatenate([values, jnp.zeros((rows, 1), values.dtype)], 1)
    safe = np.where((index >= 0) & (index < cols), index, cols)
    return jnp.take(padded, jnp.asarray(safe, jnp.int32), axis=1)


def solution(mesh):
    in_specs = (P("seq", "head"), P("seq", "head"), P("seq", "head"), P("seq", "head"), P(), P())
    out_specs = (P("seq", "head"), P("seq", "head"), P("seq", "head"), P("seq", "head"), P())
    return jax.shard_map(
        per_device, mesh=mesh, in_specs=in_specs, out_specs=out_specs, check_vma=False
    )
```

```python
import numpy as np
import jax
import jax.numpy as jnp
from jax import lax
from jax.experimental import pallas as pl
from jax.experimental.pallas import tpu as pltpu
from jax.sharding import PartitionSpec as P

DH = 64
BLK = 128
MOST = 12


def passed_along(value, axis, by):
    length = lax.axis_size(axis)
    pairs = [(i, i + by) for i in range(length) if 0 <= i + by < length]
    return lax.ppermute(value, axis, pairs)


def tap_rows(rounded, index):
    filters, taps_total = rounded.shape
    padded = jnp.concatenate([rounded, jnp.zeros((filters, 1), jnp.float32)], 1)
    safe = np.where((index >= 0) & (index < taps_total), index, taps_total)
    return jnp.take(padded, jnp.asarray(safe, jnp.int32), axis=1)


def make_kernel(nb, lags, width, span, conv_start):
    def kernel(qc_ref, qa_ref, cm_ref, pext_ref, sext_ref, srev_ref, q_ref, ct_ref,
               k_ref, v_ref, out_ref, gq_ref, gk_ref, gv_ref, gd_ref):
        step = pl.program_id(0)
        lo = lax.broadcasted_iota(jnp.int32, (BLK, BLK), 1) < DH

        def table(ref, i, shift):
            row = ref[pl.ds(2 * step + i, 1), :]
            full = jnp.broadcast_to(row, (BLK, span))
            rolled = pltpu.roll(full, shift, 1, stride=1, stride_axis=0)
            return rolled[:, :width]

        tc = jnp.concatenate(
            [table(qc_ref, 0, span - (BLK - 1)), table(qc_ref, 1, span - (BLK - 1))], 0
        )
        ta = jnp.concatenate([table(qa_ref, 0, span - BLK), table(qa_ref, 1, span - BLK)], 0)
        gsum = jnp.zeros((2 * BLK, width), jnp.float32)
        for n in range(nb):
            rows = pl.ds(n * BLK, BLK)
            cmask = cm_ref[n : n + 1, :]
            amask = cm_ref[nb + n : nb + n + 1, :]
            pw = pext_ref[pl.ds(conv_start + n * BLK, width), :]
            sw = sext_ref[pl.ds(n * BLK, width), :]
            conv2 = jnp.dot(
                (tc * cmask).astype(jnp.bfloat16), pw, preferred_element_type=jnp.float32
            )
            conv = jnp.where(lo, conv2[:BLK], conv2[BLK:])
            adj2 = jnp.dot(
                (ta * amask).astype(jnp.bfloat16), sw, preferred_element_type=jnp.float32
            )
            adj = jnp.where(lo, adj2[:BLK], adj2[BLK:])
            out_ref[rows, :] = (q_ref[rows, :].astype(jnp.float32) * conv).astype(jnp.bfloat16)
            gq_ref[rows, :] = (ct_ref[rows, :].astype(jnp.float32) * conv).astype(jnp.bfloat16)
            gk_ref[rows, :] = (adj * v_ref[rows, :].astype(jnp.float32)).astype(jnp.bfloat16)
            gv_ref[rows, :] = (adj * k_ref[rows, :].astype(jnp.float32)).astype(jnp.bfloat16)
            sr = srev_ref[rows, :]
            zero = jnp.zeros_like(sr)
            a = jnp.concatenate([jnp.where(lo, sr, zero), jnp.where(lo, zero, sr)], 0)
            g = lax.dot_general(
                a, pw, (((1,), (1,)), ((), ())), preferred_element_type=jnp.float32
            )
            gsum = gsum + g * cmask
        pad = jnp.zeros((BLK, BLK), jnp.float32)

        def diagonals(half):
            wide = jnp.concatenate([half, pad], 1)
            rolled = pltpu.roll(wide, 0, 1, stride=1, stride_axis=0)
            return rolled[:, :width].sum(0, keepdims=True)

        gd_ref[0] = jnp.concatenate([diagonals(gsum[:BLK]), diagonals(gsum[BLK:])], 0)

    return kernel


def convolve_all(value_rows, key_rows, query_rows, cotangent, filter_taps, doc_blocks, lags):
    tok_rows, channels = value_rows.shape
    filters, taps_total = filter_taps.shape
    nb = tok_rows // BLK
    width = lags * BLK
    span = width + BLK
    base = (lags - 1) * BLK
    steps = channels // BLK
    far = -(-(lags - 1) // nb)
    part = (lags - 1) - (far - 1) * nb
    product = (key_rows.astype(jnp.float32) * value_rows.astype(jnp.float32)).astype(jnp.bfloat16)
    scaled = (cotangent.astype(jnp.float32) * query_rows.astype(jnp.float32)).astype(jnp.bfloat16)
    earlier = [passed_along(product[(nb - part) * BLK :], "seq", far)]
    earlier += [passed_along(product, "seq", d) for d in range(far - 1, 0, -1)]
    later = [passed_along(scaled, "seq", -d) for d in range(1, far)]
    later += [passed_along(scaled[: part * BLK], "seq", -far)]
    pext = jnp.concatenate(earlier + [product], 0)
    sext = jnp.concatenate([scaled] + later, 0)
    srev = scaled.reshape(nb, BLK, channels)[:, ::-1].reshape(tok_rows, channels)
    conv_start = 0

    rounded = filter_taps.astype(jnp.bfloat16).astype(jnp.float32)
    k_idx = np.arange(span)
    qc = tap_rows(rounded, base + BLK - 1 - k_idx)
    qa = tap_rows(rounded, k_idx - BLK)

    margin = lags + nb
    padded = jnp.concatenate(
        [jnp.full((margin,), -1, jnp.int32), doc_blocks, jnp.full((margin,), -2, jnp.int32)], 0
    )
    shard = lax.axis_index("seq")
    window = lax.dynamic_slice_in_dim(padded, shard * nb + margin - (lags - 1), 2 * (lags - 1) + nb)
    own = jnp.stack([window[lags - 1 + n] for n in range(nb)])
    conv_docs = jnp.stack([window[n : n + lags] for n in range(nb)])
    adj_docs = jnp.stack([window[lags - 1 + n : lags - 1 + n + lags] for n in range(nb)])
    links = jnp.concatenate([conv_docs == own[:, None], adj_docs == own[:, None]], 0)
    cm = jnp.repeat(links.astype(jnp.float32), BLK, axis=1)

    whole = lambda shape: pl.BlockSpec(shape, lambda s: (0, 0))
    lanes = lambda r: pl.BlockSpec((r, BLK), lambda s: (0, s))
    kernel = make_kernel(nb, lags, width, span, conv_start)
    outs = pl.pallas_call(
        kernel,
        grid=(steps,),
        in_specs=[
            whole((filters, span)),
            whole((filters, span)),
            whole((2 * nb, width)),
            lanes(pext.shape[0]),
            lanes(sext.shape[0]),
            lanes(tok_rows),
            lanes(tok_rows),
            lanes(tok_rows),
            lanes(tok_rows),
            lanes(tok_rows),
        ],
        out_specs=[
            lanes(tok_rows),
            lanes(tok_rows),
            lanes(tok_rows),
            lanes(tok_rows),
            pl.BlockSpec((1, 2, width), lambda s: (s, 0, 0)),
        ],
        out_shape=[
            jax.ShapeDtypeStruct((tok_rows, channels), jnp.bfloat16),
            jax.ShapeDtypeStruct((tok_rows, channels), jnp.bfloat16),
            jax.ShapeDtypeStruct((tok_rows, channels), jnp.bfloat16),
            jax.ShapeDtypeStruct((tok_rows, channels), jnp.bfloat16),
            jax.ShapeDtypeStruct((steps, 2, width), jnp.float32),
        ],
        compiler_params=pltpu.CompilerParams(
            dimension_semantics=("arbitrary",), vmem_limit_bytes=48 * 1024 * 1024
        ),
    )(qc, qa, cm, pext, sext, srev, query_rows, cotangent, key_rows, value_rows)
    output_rows, grad_query, grad_key, grad_value, diag = outs
    diag = diag.reshape(filters, width)
    top = min(taps_total, base + BLK)
    taps_grad = jnp.flip(diag[:, base + BLK - top : base + BLK], 1)
    if top < taps_total:
        taps_grad = jnp.pad(taps_grad, ((0, 0), (0, taps_total - top)))
    return output_rows, grad_query, grad_key, grad_value, taps_grad


def per_device(value_rows, key_rows, query_rows, cotangent, filter_taps, doc_blocks):
    tok_rows = value_rows.shape[0]
    taps_total = filter_taps.shape[1]
    full_lags = taps_total // BLK + 1
    short_lags = min(MOST, full_lags)
    args = (value_rows, key_rows, query_rows, cotangent, filter_taps, doc_blocks)
    long_links = jnp.zeros((), jnp.bool_)
    for b in range(short_lags, full_lags):
        long_links = long_links | jnp.any(doc_blocks[b:] == doc_blocks[:-b])
    outs = lax.cond(
        long_links,
        lambda a: convolve_all(*a, full_lags),
        lambda a: convolve_all(*a, short_lags),
        args,
    )
    output_rows, grad_query, grad_key, grad_value, taps_grad = outs
    taps_grad = taps_grad * (1.0 / (tok_rows * lax.axis_size("seq")))
    grad_filter = doubled_total(taps_grad, ("head", "seq"))
    return (output_rows, grad_query, grad_key, grad_value, grad_filter)


def doubled_total(value, axes):
    for axis in axes:
        length = lax.axis_size(axis)
        bit = 1
        while bit < length:
            pairs = [(i, i ^ bit) for i in range(length)]
            value = value + lax.ppermute(value, axis, pairs)
            bit *= 2
    return value


def solution(mesh):
    in_specs = (P("seq", "head"), P("seq", "head"), P("seq", "head"), P("seq", "head"), P(), P())
    out_specs = (P("seq", "head"), P("seq", "head"), P("seq", "head"), P("seq", "head"), P())
    return jax.shard_map(
        per_device, mesh=mesh, in_specs=in_specs, out_specs=out_specs, check_vma=False
    )
```

```python
import numpy as np
import jax
import jax.numpy as jnp
from jax import lax
from jax.experimental import pallas as pl
from jax.experimental.pallas import tpu as pltpu
from jax.sharding import PartitionSpec as P

DH = 64
BLK = 128
MOST = 12


def passed_along(value, axis, by):
    length = lax.axis_size(axis)
    pairs = [(i, i + by) for i in range(length) if 0 <= i + by < length]
    return lax.ppermute(value, axis, pairs)


def tap_rows(rounded, index):
    filters, taps_total = rounded.shape
    padded = jnp.concatenate([rounded, jnp.zeros((filters, 1), jnp.float32)], 1)
    safe = np.where((index >= 0) & (index < taps_total), index, taps_total)
    return jnp.take(padded, jnp.asarray(safe, jnp.int32), axis=1)


def shifted_pairs(length, by, parity=None):
    return [
        (i, i + by)
        for i in range(length)
        if 0 <= i + by < length and (parity is None or (i + by) % 2 == parity)
    ]


def gathered_earlier(product, far, part, nb):
    length = lax.axis_size("seq")
    rounds = far // 2
    core = lax.axis_index("seq") % 2
    chain = [product]
    for r in range(1, rounds):
        chain.append(lax.ppermute(chain[-1], "seq", shifted_pairs(length, 2)))
    if part == nb:
        last_full = lax.ppermute(chain[-1], "seq", shifted_pairs(length, 2))
        last_part = last_full
    else:
        last_full = lax.ppermute(chain[-1], "seq", shifted_pairs(length, 2, 1))
        last_part = lax.ppermute(
            chain[-1][(nb - part) * BLK :], "seq", shifted_pairs(length, 2, 0)
        )
        last_part = jnp.where(core == 0, last_part, last_full[(nb - part) * BLK :])
    rows = product.shape[0]
    stacked = jnp.concatenate(chain + [last_full], 0)
    offer = lax.dynamic_slice_in_dim(stacked, core * rows, rounds * rows)
    swap = [(i, i ^ 1) for i in range(length)]
    odd = lax.ppermute(offer, "seq", swap)
    parts = [last_part if part != nb else last_full[(nb - part) * BLK :]]
    for r in range(rounds, 0, -1):
        parts.append(odd[(r - 1) * rows : r * rows])
        parts.append(chain[r - 1] if r > 1 else None)
    parts = [p for p in parts if p is not None]
    return jnp.concatenate(parts + [product], 0)


def gathered_later(scaled, far, part, nb):
    length = lax.axis_size("seq")
    rounds = far // 2
    core = lax.axis_index("seq") % 2
    chain = [scaled]
    for r in range(1, rounds):
        chain.append(lax.ppermute(chain[-1], "seq", shifted_pairs(length, -2)))
    if part == nb:
        last_full = lax.ppermute(chain[-1], "seq", shifted_pairs(length, -2))
        last_part = last_full
    else:
        last_full = lax.ppermute(chain[-1], "seq", shifted_pairs(length, -2, 0))
        last_part = lax.ppermute(chain[-1][: part * BLK], "seq", shifted_pairs(length, -2, 1))
        last_part = jnp.where(core == 1, last_part, last_full[: part * BLK])
    rows = scaled.shape[0]
    stacked = jnp.concatenate(chain + [last_full], 0)
    offer = lax.dynamic_slice_in_dim(stacked, (1 - core) * rows, rounds * rows)
    swap = [(i, i ^ 1) for i in range(length)]
    odd = lax.ppermute(offer, "seq", swap)
    parts = [scaled]
    for r in range(1, rounds + 1):
        parts.append(odd[(r - 1) * rows : r * rows])
        if r < rounds:
            parts.append(chain[r])
    parts.append(last_part if part != nb else last_full[: part * BLK])
    return jnp.concatenate(parts, 0)


def make_kernel(nb, lags, width, span, conv_start):
    def kernel(qc_ref, qa_ref, cm_ref, pext_ref, sext_ref, srev_ref, q_ref, ct_ref,
               k_ref, v_ref, out_ref, gq_ref, gk_ref, gv_ref, gd_ref):
        step = pl.program_id(0)
        lo = lax.broadcasted_iota(jnp.int32, (BLK, BLK), 1) < DH

        def table(ref, i, shift):
            row = ref[pl.ds(2 * step + i, 1), :]
            full = jnp.broadcast_to(row, (BLK, span))
            rolled = pltpu.roll(full, shift, 1, stride=1, stride_axis=0)
            return rolled[:, :width]

        tc = jnp.concatenate(
            [table(qc_ref, 0, span - (BLK - 1)), table(qc_ref, 1, span - (BLK - 1))], 0
        )
        ta = jnp.concatenate([table(qa_ref, 0, span - BLK), table(qa_ref, 1, span - BLK)], 0)
        gsum = jnp.zeros((2 * BLK, width), jnp.float32)
        for n in range(nb):
            rows = pl.ds(n * BLK, BLK)
            cmask = cm_ref[n : n + 1, :]
            amask = cm_ref[nb + n : nb + n + 1, :]
            pw = pext_ref[pl.ds(conv_start + n * BLK, width), :]
            sw = sext_ref[pl.ds(n * BLK, width), :]
            conv2 = jnp.dot(
                (tc * cmask).astype(jnp.bfloat16), pw, preferred_element_type=jnp.float32
            )
            conv = jnp.where(lo, conv2[:BLK], conv2[BLK:])
            adj2 = jnp.dot(
                (ta * amask).astype(jnp.bfloat16), sw, preferred_element_type=jnp.float32
            )
            adj = jnp.where(lo, adj2[:BLK], adj2[BLK:])
            out_ref[rows, :] = (q_ref[rows, :].astype(jnp.float32) * conv).astype(jnp.bfloat16)
            gq_ref[rows, :] = (ct_ref[rows, :].astype(jnp.float32) * conv).astype(jnp.bfloat16)
            gk_ref[rows, :] = (adj * v_ref[rows, :].astype(jnp.float32)).astype(jnp.bfloat16)
            gv_ref[rows, :] = (adj * k_ref[rows, :].astype(jnp.float32)).astype(jnp.bfloat16)
            sr = srev_ref[rows, :]
            zero = jnp.zeros_like(sr)
            a = jnp.concatenate([jnp.where(lo, sr, zero), jnp.where(lo, zero, sr)], 0)
            g = lax.dot_general(
                a, pw, (((1,), (1,)), ((), ())), preferred_element_type=jnp.float32
            )
            gsum = gsum + g * cmask
        pad = jnp.zeros((BLK, BLK), jnp.float32)

        def diagonals(half):
            wide = jnp.concatenate([half, pad], 1)
            rolled = pltpu.roll(wide, 0, 1, stride=1, stride_axis=0)
            return rolled[:, :width].sum(0, keepdims=True)

        gd_ref[0] = jnp.concatenate([diagonals(gsum[:BLK]), diagonals(gsum[BLK:])], 0)

    return kernel


def convolve_all(value_rows, key_rows, query_rows, cotangent, filter_taps, doc_blocks, lags):
    tok_rows, channels = value_rows.shape
    filters, taps_total = filter_taps.shape
    nb = tok_rows // BLK
    width = lags * BLK
    span = width + BLK
    base = (lags - 1) * BLK
    steps = channels // BLK
    far = -(-(lags - 1) // nb)
    part = (lags - 1) - (far - 1) * nb
    product = (key_rows.astype(jnp.float32) * value_rows.astype(jnp.float32)).astype(jnp.bfloat16)
    scaled = (cotangent.astype(jnp.float32) * query_rows.astype(jnp.float32)).astype(jnp.bfloat16)
    pext = gathered_earlier(product, far, part, nb)
    sext = gathered_later(scaled, far, part, nb)
    srev = scaled.reshape(nb, BLK, channels)[:, ::-1].reshape(tok_rows, channels)
    conv_start = 0

    rounded = filter_taps.astype(jnp.bfloat16).astype(jnp.float32)
    k_idx = np.arange(span)
    qc = tap_rows(rounded, base + BLK - 1 - k_idx)
    qa = tap_rows(rounded, k_idx - BLK)

    margin = lags + nb
    padded = jnp.concatenate(
        [jnp.full((margin,), -1, jnp.int32), doc_blocks, jnp.full((margin,), -2, jnp.int32)], 0
    )
    shard = lax.axis_index("seq")
    window = lax.dynamic_slice_in_dim(padded, shard * nb + margin - (lags - 1), 2 * (lags - 1) + nb)
    own = jnp.stack([window[lags - 1 + n] for n in range(nb)])
    conv_docs = jnp.stack([window[n : n + lags] for n in range(nb)])
    adj_docs = jnp.stack([window[lags - 1 + n : lags - 1 + n + lags] for n in range(nb)])
    links = jnp.concatenate([conv_docs == own[:, None], adj_docs == own[:, None]], 0)
    cm = jnp.repeat(links.astype(jnp.float32), BLK, axis=1)

    whole = lambda shape: pl.BlockSpec(shape, lambda s: (0, 0))
    lanes = lambda r: pl.BlockSpec((r, BLK), lambda s: (0, s))
    kernel = make_kernel(nb, lags, width, span, conv_start)
    outs = pl.pallas_call(
        kernel,
        grid=(steps,),
        in_specs=[
            whole((filters, span)),
            whole((filters, span)),
            whole((2 * nb, width)),
            lanes(pext.shape[0]),
            lanes(sext.shape[0]),
            lanes(tok_rows),
            lanes(tok_rows),
            lanes(tok_rows),
            lanes(tok_rows),
            lanes(tok_rows),
        ],
        out_specs=[
            lanes(tok_rows),
            lanes(tok_rows),
            lanes(tok_rows),
            lanes(tok_rows),
            pl.BlockSpec((1, 2, width), lambda s: (s, 0, 0)),
        ],
        out_shape=[
            jax.ShapeDtypeStruct((tok_rows, channels), jnp.bfloat16),
            jax.ShapeDtypeStruct((tok_rows, channels), jnp.bfloat16),
            jax.ShapeDtypeStruct((tok_rows, channels), jnp.bfloat16),
            jax.ShapeDtypeStruct((tok_rows, channels), jnp.bfloat16),
            jax.ShapeDtypeStruct((steps, 2, width), jnp.float32),
        ],
        compiler_params=pltpu.CompilerParams(
            dimension_semantics=("arbitrary",), vmem_limit_bytes=48 * 1024 * 1024
        ),
    )(qc, qa, cm, pext, sext, srev, query_rows, cotangent, key_rows, value_rows)
    output_rows, grad_query, grad_key, grad_value, diag = outs
    diag = diag.reshape(filters, width)
    top = min(taps_total, base + BLK)
    taps_grad = jnp.flip(diag[:, base + BLK - top : base + BLK], 1)
    if top < taps_total:
        taps_grad = jnp.pad(taps_grad, ((0, 0), (0, taps_total - top)))
    return output_rows, grad_query, grad_key, grad_value, taps_grad


def per_device(value_rows, key_rows, query_rows, cotangent, filter_taps, doc_blocks):
    tok_rows = value_rows.shape[0]
    taps_total = filter_taps.shape[1]
    full_lags = taps_total // BLK + 1
    short_lags = min(MOST, full_lags)
    args = (value_rows, key_rows, query_rows, cotangent, filter_taps, doc_blocks)
    nblk = doc_blocks.shape[0]
    apart = np.abs(np.arange(nblk)[:, None] - np.arange(nblk)[None, :])
    far_pairs = jnp.asarray((apart >= short_lags) & (apart < full_lags))
    same = doc_blocks[:, None] == doc_blocks[None, :]
    long_links = jnp.any(same & far_pairs)
    outs = lax.cond(
        long_links,
        lambda a: convolve_all(*a, full_lags),
        lambda a: convolve_all(*a, short_lags),
        args,
    )
    output_rows, grad_query, grad_key, grad_value, taps_grad = outs
    taps_grad = taps_grad * (1.0 / (tok_rows * lax.axis_size("seq")))
    grad_filter = doubled_total(taps_grad, ("head", "seq"))
    return (output_rows, grad_query, grad_key, grad_value, grad_filter)


def doubled_total(value, axes):
    for axis in axes:
        length = lax.axis_size(axis)
        bit = 1
        while bit < length:
            pairs = [(i, i ^ bit) for i in range(length)]
            value = value + lax.ppermute(value, axis, pairs)
            bit *= 2
    return value


def solution(mesh):
    in_specs = (P("seq", "head"), P("seq", "head"), P("seq", "head"), P("seq", "head"), P(), P())
    out_specs = (P("seq", "head"), P("seq", "head"), P("seq", "head"), P("seq", "head"), P())
    return jax.shard_map(
        per_device, mesh=mesh, in_specs=in_specs, out_specs=out_specs, check_vma=False
    )
```

```python
import numpy as np
import jax
import jax.numpy as jnp
from jax import lax
from jax.experimental import pallas as pl
from jax.experimental.pallas import tpu as pltpu
from jax.sharding import PartitionSpec as P

DH = 64
BLK = 128
MOST = 12


def passed_along(value, axis, by):
    length = lax.axis_size(axis)
    pairs = [(i, i + by) for i in range(length) if 0 <= i + by < length]
    return lax.ppermute(value, axis, pairs)


def shifted_pairs(length, by, parity=None):
    return [
        (i, i + by)
        for i in range(length)
        if 0 <= i + by < length and (parity is None or (i + by) % 2 == parity)
    ]


def earlier_pieces(product, far, part, nb):
    length = lax.axis_size("seq")
    rounds = far // 2
    rows = product.shape[0]
    chain = [product]
    for r in range(1, rounds):
        chain.append(lax.ppermute(chain[-1], "seq", shifted_pairs(length, 2)))
    if part == nb:
        last_full = lax.ppermute(chain[-1], "seq", shifted_pairs(length, 2))
        tail = [(last_full, 0, rows)]
    else:
        last_full = lax.ppermute(chain[-1], "seq", shifted_pairs(length, 2, 1))
        last_part = lax.ppermute(
            chain[-1][(nb - part) * BLK :], "seq", shifted_pairs(length, 2, 0)
        )
        tail = [(last_part, 0, part * BLK), (last_full, (nb - part) * BLK, part * BLK)]
    offers = chain[1:] + [last_full]
    to_odd = [(i, i + 1) for i in range(0, length, 2)]
    to_even = [(i, i - 1) for i in range(1, length, 2)]
    odd = [
        [(lax.ppermute(chain[k], "seq", to_odd), 0, rows),
         (lax.ppermute(offers[k], "seq", to_even), 0, rows)]
        for k in range(rounds)
    ]
    pieces = [tail]
    for r in range(rounds, 0, -1):
        pieces.append(odd[r - 1])
        if r > 1:
            pieces.append([(chain[r - 1], 0, rows)])
    pieces.append([(product, 0, rows)])
    return pieces


def later_pieces(scaled, far, part, nb):
    length = lax.axis_size("seq")
    rounds = far // 2
    rows = scaled.shape[0]
    chain = [scaled]
    for r in range(1, rounds):
        chain.append(lax.ppermute(chain[-1], "seq", shifted_pairs(length, -2)))
    if part == nb:
        last_full = lax.ppermute(chain[-1], "seq", shifted_pairs(length, -2))
        tail = [(last_full, 0, rows)]
    else:
        last_full = lax.ppermute(chain[-1], "seq", shifted_pairs(length, -2, 0))
        last_part = lax.ppermute(chain[-1][: part * BLK], "seq", shifted_pairs(length, -2, 1))
        tail = [(last_part, 0, part * BLK), (last_full, 0, part * BLK)]
    offers = chain[1:] + [last_full]
    to_even = [(i, i - 1) for i in range(1, length, 2)]
    to_odd = [(i, i + 1) for i in range(0, length, 2)]
    odd = [
        [(lax.ppermute(chain[k], "seq", to_even), 0, rows),
         (lax.ppermute(offers[k], "seq", to_odd), 0, rows)]
        for k in range(rounds)
    ]
    pieces = [[(scaled, 0, rows)]]
    for r in range(1, rounds + 1):
        pieces.append(odd[r - 1])
        if r < rounds:
            pieces.append([(chain[r], 0, rows)])
    pieces.append(tail)
    return pieces


def flatten_pieces(pieces, arrays):
    layout = []
    for piece in pieces:
        terms = []
        for arr, start, rows in piece:
            for idx, known in enumerate(arrays):
                if known is arr:
                    break
            else:
                arrays.append(arr)
                idx = len(arrays) - 1
            terms.append((idx, start, rows))
        layout.append(terms)
    return layout


def make_kernel(nb, lags, width, span, conv_start, p_layout, s_layout, n_halo):
    def kernel(*refs):
        qc_ref, qa_ref, cm_ref = refs[:3]
        halo = refs[3 : 3 + n_halo]
        srev_ref, q_ref, ct_ref, k_ref, v_ref = refs[3 + n_halo : 8 + n_halo]
        out_ref, gq_ref, gk_ref, gv_ref, gd_ref = refs[8 + n_halo :]
        step = pl.program_id(0)

        def assemble(layout):
            pieces = []
            for terms in layout:
                total = None
                for idx, start, rows in terms:
                    term = halo[idx][start : start + rows, :]
                    total = term if total is None else total + term
                pieces.append(total)
            return jnp.concatenate(pieces, 0)

        pext = assemble(p_layout)
        sext = assemble(s_layout)
        lo = lax.broadcasted_iota(jnp.int32, (BLK, BLK), 1) < DH

        def table(ref, i, shift):
            row = ref[pl.ds(2 * step + i, 1), :]
            full = jnp.broadcast_to(row, (BLK, span))
            rolled = pltpu.roll(full, shift, 1, stride=1, stride_axis=0)
            return rolled[:, :width]

        tc = jnp.concatenate(
            [table(qc_ref, 0, span - (BLK - 1)), table(qc_ref, 1, span - (BLK - 1))], 0
        )
        ta = jnp.concatenate([table(qa_ref, 0, span - BLK), table(qa_ref, 1, span - BLK)], 0)
        gsum = jnp.zeros((2 * BLK, width), jnp.float32)
        for n in range(nb):
            rows = pl.ds(n * BLK, BLK)
            cmask = cm_ref[n : n + 1, :]
            amask = cm_ref[nb + n : nb + n + 1, :]
            pw = pext[conv_start + n * BLK : conv_start + n * BLK + width]
            sw = sext[n * BLK : n * BLK + width]
            conv2 = jnp.dot(
                (tc * cmask).astype(jnp.bfloat16), pw, preferred_element_type=jnp.float32
            )
            conv = jnp.where(lo, conv2[:BLK], conv2[BLK:])
            adj2 = jnp.dot(
                (ta * amask).astype(jnp.bfloat16), sw, preferred_element_type=jnp.float32
            )
            adj = jnp.where(lo, adj2[:BLK], adj2[BLK:])
            out_ref[rows, :] = (q_ref[rows, :].astype(jnp.float32) * conv).astype(jnp.bfloat16)
            gq_ref[rows, :] = (ct_ref[rows, :].astype(jnp.float32) * conv).astype(jnp.bfloat16)
            gk_ref[rows, :] = (adj * v_ref[rows, :].astype(jnp.float32)).astype(jnp.bfloat16)
            gv_ref[rows, :] = (adj * k_ref[rows, :].astype(jnp.float32)).astype(jnp.bfloat16)
            sr = srev_ref[rows, :]
            zero = jnp.zeros_like(sr)
            a = jnp.concatenate([jnp.where(lo, sr, zero), jnp.where(lo, zero, sr)], 0)
            g = lax.dot_general(
                a, pw, (((1,), (1,)), ((), ())), preferred_element_type=jnp.float32
            )
            gsum = gsum + g * cmask
        pad = jnp.zeros((BLK, BLK), jnp.float32)

        def diagonals(half):
            wide = jnp.concatenate([half, pad], 1)
            rolled = pltpu.roll(wide, 0, 1, stride=1, stride_axis=0)
            return rolled[:, :width].sum(0, keepdims=True)

        gd_ref[0] = jnp.concatenate([diagonals(gsum[:BLK]), diagonals(gsum[BLK:])], 0)

    return kernel


def convolve_all(value_rows, key_rows, query_rows, cotangent, filter_taps, doc_blocks, lags):
    tok_rows, channels = value_rows.shape
    filters, taps_total = filter_taps.shape
    nb = tok_rows // BLK
    width = lags * BLK
    span = width + BLK
    base = (lags - 1) * BLK
    steps = channels // BLK
    far = -(-(lags - 1) // nb)
    part = (lags - 1) - (far - 1) * nb
    product = (key_rows.astype(jnp.float32) * value_rows.astype(jnp.float32)).astype(jnp.bfloat16)
    scaled = (cotangent.astype(jnp.float32) * query_rows.astype(jnp.float32)).astype(jnp.bfloat16)
    halo = []
    p_layout = flatten_pieces(earlier_pieces(product, far, part, nb), halo)
    s_layout = flatten_pieces(later_pieces(scaled, far, part, nb), halo)
    srev = scaled.reshape(nb, BLK, channels)[:, ::-1].reshape(tok_rows, channels)
    conv_start = 0

    rounded = filter_taps.astype(jnp.bfloat16).astype(jnp.float32)
    kept = min(taps_total, span - BLK)
    qa = jnp.pad(rounded[:, :kept], ((0, 0), (BLK, span - BLK - kept)))
    qc = jnp.flip(qa, 1)

    margin = lags + nb
    padded = jnp.concatenate(
        [jnp.full((margin,), -1, jnp.int32), doc_blocks, jnp.full((margin,), -2, jnp.int32)], 0
    )
    shard = lax.axis_index("seq")
    window = lax.dynamic_slice_in_dim(padded, shard * nb + margin - (lags - 1), 2 * (lags - 1) + nb)
    own = jnp.stack([window[lags - 1 + n] for n in range(nb)])
    conv_docs = jnp.stack([window[n : n + lags] for n in range(nb)])
    adj_docs = jnp.stack([window[lags - 1 + n : lags - 1 + n + lags] for n in range(nb)])
    links = jnp.concatenate([conv_docs == own[:, None], adj_docs == own[:, None]], 0)
    cm = jnp.repeat(links.astype(jnp.float32), BLK, axis=1)

    whole = lambda shape: pl.BlockSpec(shape, lambda s: (0, 0))
    lanes = lambda r: pl.BlockSpec((r, BLK), lambda s: (0, s))
    kernel = make_kernel(nb, lags, width, span, conv_start, p_layout, s_layout, len(halo))
    outs = pl.pallas_call(
        kernel,
        grid=(steps,),
        in_specs=[
            whole((filters, span)),
            whole((filters, span)),
            whole((2 * nb, width)),
            *[lanes(h.shape[0]) for h in halo],
            lanes(tok_rows),
            lanes(tok_rows),
            lanes(tok_rows),
            lanes(tok_rows),
            lanes(tok_rows),
        ],
        out_specs=[
            lanes(tok_rows),
            lanes(tok_rows),
            lanes(tok_rows),
            lanes(tok_rows),
            pl.BlockSpec((1, 2, width), lambda s: (s, 0, 0)),
        ],
        out_shape=[
            jax.ShapeDtypeStruct((tok_rows, channels), jnp.bfloat16),
            jax.ShapeDtypeStruct((tok_rows, channels), jnp.bfloat16),
            jax.ShapeDtypeStruct((tok_rows, channels), jnp.bfloat16),
            jax.ShapeDtypeStruct((tok_rows, channels), jnp.bfloat16),
            jax.ShapeDtypeStruct((steps, 2, width), jnp.float32),
        ],
        compiler_params=pltpu.CompilerParams(
            dimension_semantics=("arbitrary",), vmem_limit_bytes=48 * 1024 * 1024
        ),
    )(qc, qa, cm, *halo, srev, query_rows, cotangent, key_rows, value_rows)
    output_rows, grad_query, grad_key, grad_value, diag = outs
    diag = diag.reshape(filters, width)
    top = min(taps_total, base + BLK)
    taps_grad = jnp.flip(diag[:, base + BLK - top : base + BLK], 1)
    if top < taps_total:
        taps_grad = jnp.pad(taps_grad, ((0, 0), (0, taps_total - top)))
    return output_rows, grad_query, grad_key, grad_value, taps_grad


def per_device(value_rows, key_rows, query_rows, cotangent, filter_taps, doc_blocks):
    tok_rows = value_rows.shape[0]
    taps_total = filter_taps.shape[1]
    full_lags = taps_total // BLK + 1
    short_lags = min(MOST, full_lags)
    args = (value_rows, key_rows, query_rows, cotangent, filter_taps, doc_blocks)
    nblk = doc_blocks.shape[0]
    apart = np.abs(np.arange(nblk)[:, None] - np.arange(nblk)[None, :])
    far_pairs = jnp.asarray((apart >= short_lags) & (apart < full_lags))
    same = doc_blocks[:, None] == doc_blocks[None, :]
    long_links = jnp.any(same & far_pairs)
    outs = lax.cond(
        long_links,
        lambda a: convolve_all(*a, full_lags),
        lambda a: convolve_all(*a, short_lags),
        args,
    )
    output_rows, grad_query, grad_key, grad_value, taps_grad = outs
    taps_grad = taps_grad * (1.0 / (tok_rows * lax.axis_size("seq")))
    grad_filter = doubled_total(taps_grad, ("head", "seq"))
    return (output_rows, grad_query, grad_key, grad_value, grad_filter)


def doubled_total(value, axes):
    for axis in axes:
        length = lax.axis_size(axis)
        bit = 1
        while bit < length:
            pairs = [(i, i ^ bit) for i in range(length)]
            value = value + lax.ppermute(value, axis, pairs)
            bit *= 2
    return value


def solution(mesh):
    in_specs = (P("seq", "head"), P("seq", "head"), P("seq", "head"), P("seq", "head"), P(), P())
    out_specs = (P("seq", "head"), P("seq", "head"), P("seq", "head"), P("seq", "head"), P())
    return jax.shard_map(
        per_device, mesh=mesh, in_specs=in_specs, out_specs=out_specs, check_vma=False
    )
```

```python
import numpy as np
import jax
import jax.numpy as jnp
from jax import lax
from jax.experimental import pallas as pl
from jax.experimental.pallas import tpu as pltpu
from jax.sharding import PartitionSpec as P

DH = 64
BLK = 128
MOST = 12


def passed_along(value, axis, by):
    length = lax.axis_size(axis)
    pairs = [(i, i + by) for i in range(length) if 0 <= i + by < length]
    return lax.ppermute(value, axis, pairs)


def shifted_pairs(length, by, parity=None):
    return [
        (i, i + by)
        for i in range(length)
        if 0 <= i + by < length and (parity is None or (i + by) % 2 == parity)
    ]


def earlier_pieces(product, far, part, nb):
    length = lax.axis_size("seq")
    rounds = far // 2
    rows = product.shape[0]
    chain = [product]
    for r in range(1, rounds):
        chain.append(lax.ppermute(chain[-1], "seq", shifted_pairs(length, 2)))
    if part == nb:
        last_full = lax.ppermute(chain[-1], "seq", shifted_pairs(length, 2))
        tail = [(last_full, 0, rows)]
    else:
        last_full = lax.ppermute(chain[-1], "seq", shifted_pairs(length, 2, 1))
        last_part = lax.ppermute(
            chain[-1][(nb - part) * BLK :], "seq", shifted_pairs(length, 2, 0)
        )
        tail = [(last_part, 0, part * BLK), (last_full, (nb - part) * BLK, part * BLK)]
    offers = chain[1:] + [last_full]
    to_odd = [(i, i + 1) for i in range(0, length, 2)]
    to_even = [(i, i - 1) for i in range(1, length, 2)]
    odd = [
        [(lax.ppermute(chain[k], "seq", to_odd), 0, rows),
         (lax.ppermute(offers[k], "seq", to_even), 0, rows)]
        for k in range(rounds)
    ]
    pieces = [tail]
    for r in range(rounds, 0, -1):
        pieces.append(odd[r - 1])
        if r > 1:
            pieces.append([(chain[r - 1], 0, rows)])
    pieces.append([(product, 0, rows)])
    return pieces


def later_pieces(scaled, far, part, nb):
    length = lax.axis_size("seq")
    rounds = far // 2
    rows = scaled.shape[0]
    chain = [scaled]
    for r in range(1, rounds):
        chain.append(lax.ppermute(chain[-1], "seq", shifted_pairs(length, -2)))
    if part == nb:
        last_full = lax.ppermute(chain[-1], "seq", shifted_pairs(length, -2))
        tail = [(last_full, 0, rows)]
    else:
        last_full = lax.ppermute(chain[-1], "seq", shifted_pairs(length, -2, 0))
        last_part = lax.ppermute(chain[-1][: part * BLK], "seq", shifted_pairs(length, -2, 1))
        tail = [(last_part, 0, part * BLK), (last_full, 0, part * BLK)]
    offers = chain[1:] + [last_full]
    to_even = [(i, i - 1) for i in range(1, length, 2)]
    to_odd = [(i, i + 1) for i in range(0, length, 2)]
    odd = [
        [(lax.ppermute(chain[k], "seq", to_even), 0, rows),
         (lax.ppermute(offers[k], "seq", to_odd), 0, rows)]
        for k in range(rounds)
    ]
    pieces = [[(scaled, 0, rows)]]
    for r in range(1, rounds + 1):
        pieces.append(odd[r - 1])
        if r < rounds:
            pieces.append([(chain[r], 0, rows)])
    pieces.append(tail)
    return pieces


def flatten_pieces(pieces, arrays):
    layout = []
    for piece in pieces:
        terms = []
        for arr, start, rows in piece:
            for idx, known in enumerate(arrays):
                if known is arr:
                    break
            else:
                arrays.append(arr)
                idx = len(arrays) - 1
            terms.append((idx, start, rows))
        layout.append(terms)
    return layout


def make_kernel(nb, lags, width, span, conv_start, p_layout, s_layout, n_halo):
    def kernel(*refs):
        qc_ref, qa_ref, cm_ref = refs[:3]
        halo = refs[3 : 3 + n_halo]
        q_ref, ct_ref, k_ref, v_ref = refs[3 + n_halo : 7 + n_halo]
        out_ref, gq_ref, gk_ref, gv_ref, gd_ref = refs[7 + n_halo :]
        step = pl.program_id(0)

        def assemble(layout):
            pieces = []
            for terms in layout:
                total = None
                for idx, start, rows in terms:
                    term = halo[idx][start : start + rows, :]
                    total = term if total is None else total + term
                pieces.append(total)
            return jnp.concatenate(pieces, 0)

        pext = assemble(p_layout)
        sext = assemble(s_layout)
        lane = lax.broadcasted_iota(jnp.int32, (BLK, BLK), 1)
        lo = lane < DH
        flip = (lane + lax.broadcasted_iota(jnp.int32, (BLK, BLK), 0) == BLK - 1).astype(
            jnp.bfloat16
        )

        def table(ref, i, shift):
            row = ref[pl.ds(2 * step + i, 1), :]
            full = jnp.broadcast_to(row, (BLK, span))
            rolled = pltpu.roll(full, shift, 1, stride=1, stride_axis=0)
            return rolled[:, :width]

        tc = jnp.concatenate(
            [table(qc_ref, 0, span - (BLK - 1)), table(qc_ref, 1, span - (BLK - 1))], 0
        )
        ta = jnp.concatenate([table(qa_ref, 0, span - BLK), table(qa_ref, 1, span - BLK)], 0)
        gsum = jnp.zeros((2 * BLK, width), jnp.float32)
        for n in range(nb):
            rows = pl.ds(n * BLK, BLK)
            cmask = cm_ref[n : n + 1, :]
            amask = cm_ref[nb + n : nb + n + 1, :]
            pw = pext[conv_start + n * BLK : conv_start + n * BLK + width]
            sw = sext[n * BLK : n * BLK + width]
            conv2 = jnp.dot(
                (tc * cmask).astype(jnp.bfloat16), pw, preferred_element_type=jnp.float32
            )
            conv = jnp.where(lo, conv2[:BLK], conv2[BLK:])
            adj2 = jnp.dot(
                (ta * amask).astype(jnp.bfloat16), sw, preferred_element_type=jnp.float32
            )
            adj = jnp.where(lo, adj2[:BLK], adj2[BLK:])
            out_ref[rows, :] = (q_ref[rows, :].astype(jnp.float32) * conv).astype(jnp.bfloat16)
            gq_ref[rows, :] = (ct_ref[rows, :].astype(jnp.float32) * conv).astype(jnp.bfloat16)
            gk_ref[rows, :] = (adj * v_ref[rows, :].astype(jnp.float32)).astype(jnp.bfloat16)
            gv_ref[rows, :] = (adj * k_ref[rows, :].astype(jnp.float32)).astype(jnp.bfloat16)
            sr = jnp.dot(
                flip, sext[n * BLK : (n + 1) * BLK], preferred_element_type=jnp.float32
            ).astype(jnp.bfloat16)
            zero = jnp.zeros_like(sr)
            a = jnp.concatenate([jnp.where(lo, sr, zero), jnp.where(lo, zero, sr)], 0)
            g = lax.dot_general(
                a, pw, (((1,), (1,)), ((), ())), preferred_element_type=jnp.float32
            )
            gsum = gsum + g * cmask
        pad = jnp.zeros((BLK, BLK), jnp.float32)

        def diagonals(half):
            wide = jnp.concatenate([half, pad], 1)
            rolled = pltpu.roll(wide, 0, 1, stride=1, stride_axis=0)
            return rolled[:, :width].sum(0, keepdims=True)

        gd_ref[0] = jnp.concatenate([diagonals(gsum[:BLK]), diagonals(gsum[BLK:])], 0)

    return kernel


def convolve_all(value_rows, key_rows, query_rows, cotangent, filter_taps, doc_blocks, lags):
    tok_rows, channels = value_rows.shape
    filters, taps_total = filter_taps.shape
    nb = tok_rows // BLK
    width = lags * BLK
    span = width + BLK
    base = (lags - 1) * BLK
    steps = channels // BLK
    far = -(-(lags - 1) // nb)
    part = (lags - 1) - (far - 1) * nb
    product = (key_rows.astype(jnp.float32) * value_rows.astype(jnp.float32)).astype(jnp.bfloat16)
    scaled = (cotangent.astype(jnp.float32) * query_rows.astype(jnp.float32)).astype(jnp.bfloat16)
    halo = []
    p_layout = flatten_pieces(earlier_pieces(product, far, part, nb), halo)
    s_layout = flatten_pieces(later_pieces(scaled, far, part, nb), halo)
    conv_start = 0

    rounded = filter_taps.astype(jnp.bfloat16).astype(jnp.float32)
    kept = min(taps_total, span - BLK)
    qa = jnp.pad(rounded[:, :kept], ((0, 0), (BLK, span - BLK - kept)))
    qc = jnp.flip(qa, 1)

    margin = lags + nb
    padded = jnp.concatenate(
        [jnp.full((margin,), -1, jnp.int32), doc_blocks, jnp.full((margin,), -2, jnp.int32)], 0
    )
    shard = lax.axis_index("seq")
    window = lax.dynamic_slice_in_dim(padded, shard * nb + margin - (lags - 1), 2 * (lags - 1) + nb)
    own = jnp.stack([window[lags - 1 + n] for n in range(nb)])
    conv_docs = jnp.stack([window[n : n + lags] for n in range(nb)])
    adj_docs = jnp.stack([window[lags - 1 + n : lags - 1 + n + lags] for n in range(nb)])
    links = jnp.concatenate([conv_docs == own[:, None], adj_docs == own[:, None]], 0)
    cm = jnp.repeat(links.astype(jnp.float32), BLK, axis=1)

    whole = lambda shape: pl.BlockSpec(shape, lambda s: (0, 0))
    lanes = lambda r: pl.BlockSpec((r, BLK), lambda s: (0, s))
    kernel = make_kernel(nb, lags, width, span, conv_start, p_layout, s_layout, len(halo))
    outs = pl.pallas_call(
        kernel,
        grid=(steps,),
        in_specs=[
            whole((filters, span)),
            whole((filters, span)),
            whole((2 * nb, width)),
            *[lanes(h.shape[0]) for h in halo],
            lanes(tok_rows),
            lanes(tok_rows),
            lanes(tok_rows),
            lanes(tok_rows),
        ],
        out_specs=[
            lanes(tok_rows),
            lanes(tok_rows),
            lanes(tok_rows),
            lanes(tok_rows),
            pl.BlockSpec((1, 2, width), lambda s: (s, 0, 0)),
        ],
        out_shape=[
            jax.ShapeDtypeStruct((tok_rows, channels), jnp.bfloat16),
            jax.ShapeDtypeStruct((tok_rows, channels), jnp.bfloat16),
            jax.ShapeDtypeStruct((tok_rows, channels), jnp.bfloat16),
            jax.ShapeDtypeStruct((tok_rows, channels), jnp.bfloat16),
            jax.ShapeDtypeStruct((steps, 2, width), jnp.float32),
        ],
        compiler_params=pltpu.CompilerParams(
            dimension_semantics=("arbitrary",), vmem_limit_bytes=48 * 1024 * 1024
        ),
    )(qc, qa, cm, *halo, query_rows, cotangent, key_rows, value_rows)
    output_rows, grad_query, grad_key, grad_value, diag = outs
    diag = diag.reshape(filters, width)
    top = min(taps_total, base + BLK)
    taps_grad = jnp.flip(diag[:, base + BLK - top : base + BLK], 1)
    if top < taps_total:
        taps_grad = jnp.pad(taps_grad, ((0, 0), (0, taps_total - top)))
    return output_rows, grad_query, grad_key, grad_value, taps_grad


def per_device(value_rows, key_rows, query_rows, cotangent, filter_taps, doc_blocks):
    tok_rows = value_rows.shape[0]
    taps_total = filter_taps.shape[1]
    full_lags = taps_total // BLK + 1
    short_lags = min(MOST, full_lags)
    args = (value_rows, key_rows, query_rows, cotangent, filter_taps, doc_blocks)
    nblk = doc_blocks.shape[0]
    apart = np.abs(np.arange(nblk)[:, None] - np.arange(nblk)[None, :])
    far_pairs = jnp.asarray((apart >= short_lags) & (apart < full_lags))
    same = doc_blocks[:, None] == doc_blocks[None, :]
    long_links = jnp.any(same & far_pairs)
    outs = lax.cond(
        long_links,
        lambda a: convolve_all(*a, full_lags),
        lambda a: convolve_all(*a, short_lags),
        args,
    )
    output_rows, grad_query, grad_key, grad_value, taps_grad = outs
    taps_grad = taps_grad * (1.0 / (tok_rows * lax.axis_size("seq")))
    grad_filter = doubled_total(taps_grad, ("head", "seq"))
    return (output_rows, grad_query, grad_key, grad_value, grad_filter)


def doubled_total(value, axes):
    for axis in axes:
        length = lax.axis_size(axis)
        bits = (length - 1).bit_length()
        for low in range(0, bits, 2):
            group = [1 << low] + ([1 << (low + 1)] if low + 1 < bits else [])
            swap = lambda m: lax.ppermute(value, axis, [(i, i ^ m) for i in range(length)])
            if len(group) == 1:
                value = value + swap(group[0])
            else:
                a, b = group
                value = (value + swap(a)) + (swap(b) + swap(a | b))
    return value


def solution(mesh):
    in_specs = (P("seq", "head"), P("seq", "head"), P("seq", "head"), P("seq", "head"), P(), P())
    out_specs = (P("seq", "head"), P("seq", "head"), P("seq", "head"), P("seq", "head"), P())
    return jax.shard_map(
        per_device, mesh=mesh, in_specs=in_specs, out_specs=out_specs, check_vma=False
    )
```

```python
import numpy as np
import jax
import jax.numpy as jnp
from jax import lax
from jax.experimental import pallas as pl
from jax.experimental.pallas import tpu as pltpu
from jax.sharding import PartitionSpec as P

DH = 64
BLK = 128
MOST = 12


def passed_along(value, axis, by):
    length = lax.axis_size(axis)
    pairs = [(i, i + by) for i in range(length) if 0 <= i + by < length]
    return lax.ppermute(value, axis, pairs)


def shifted_pairs(length, by, parity=None):
    return [
        (i, i + by)
        for i in range(length)
        if 0 <= i + by < length and (parity is None or (i + by) % 2 == parity)
    ]


def earlier_pieces(product, far, part, nb):
    length = lax.axis_size("seq")
    rounds = far // 2
    rows = product.shape[0]
    chain = [product]
    for r in range(1, rounds):
        chain.append(lax.ppermute(chain[-1], "seq", shifted_pairs(length, 2)))
    if part == nb:
        last_full = lax.ppermute(chain[-1], "seq", shifted_pairs(length, 2))
        tail = [(last_full, 0, rows)]
    else:
        last_full = lax.ppermute(chain[-1], "seq", shifted_pairs(length, 2, 1))
        last_part = lax.ppermute(
            chain[-1][(nb - part) * BLK :], "seq", shifted_pairs(length, 2, 0)
        )
        tail = [(last_part, 0, part * BLK), (last_full, (nb - part) * BLK, part * BLK)]
    offers = chain[1:] + [last_full]
    to_odd = [(i, i + 1) for i in range(0, length, 2)]
    to_even = [(i, i - 1) for i in range(1, length, 2)]
    odd = [
        [(lax.ppermute(chain[k], "seq", to_odd), 0, rows),
         (lax.ppermute(offers[k], "seq", to_even), 0, rows)]
        for k in range(rounds)
    ]
    pieces = [tail]
    for r in range(rounds, 0, -1):
        pieces.append(odd[r - 1])
        if r > 1:
            pieces.append([(chain[r - 1], 0, rows)])
    pieces.append([(product, 0, rows)])
    return pieces


def later_pieces(scaled, far, part, nb):
    length = lax.axis_size("seq")
    rounds = far // 2
    rows = scaled.shape[0]
    chain = [scaled]
    for r in range(1, rounds):
        chain.append(lax.ppermute(chain[-1], "seq", shifted_pairs(length, -2)))
    if part == nb:
        last_full = lax.ppermute(chain[-1], "seq", shifted_pairs(length, -2))
        tail = [(last_full, 0, rows)]
    else:
        last_full = lax.ppermute(chain[-1], "seq", shifted_pairs(length, -2, 0))
        last_part = lax.ppermute(chain[-1][: part * BLK], "seq", shifted_pairs(length, -2, 1))
        tail = [(last_part, 0, part * BLK), (last_full, 0, part * BLK)]
    offers = chain[1:] + [last_full]
    to_even = [(i, i - 1) for i in range(1, length, 2)]
    to_odd = [(i, i + 1) for i in range(0, length, 2)]
    odd = [
        [(lax.ppermute(chain[k], "seq", to_even), 0, rows),
         (lax.ppermute(offers[k], "seq", to_odd), 0, rows)]
        for k in range(rounds)
    ]
    pieces = [[(scaled, 0, rows)]]
    for r in range(1, rounds + 1):
        pieces.append(odd[r - 1])
        if r < rounds:
            pieces.append([(chain[r], 0, rows)])
    pieces.append(tail)
    return pieces


def flatten_pieces(pieces, arrays):
    layout = []
    for piece in pieces:
        terms = []
        for arr, start, rows in piece:
            for idx, known in enumerate(arrays):
                if known is arr:
                    break
            else:
                arrays.append(arr)
                idx = len(arrays) - 1
            terms.append((idx, start, rows))
        layout.append(terms)
    return layout


def assemble(halo, layout):
    pieces = []
    for terms in layout:
        total = None
        for idx, start, rows in terms:
            term = halo[idx][start : start + rows, :]
            total = term if total is None else total + term
        pieces.append(total)
    return jnp.concatenate(pieces, 0)


def make_grad_kernel(nb, width, conv_start, p_layout, n_halo):
    def kernel(*refs):
        cm_ref = refs[0]
        halo = refs[1 : 1 + n_halo]
        s_ref = refs[1 + n_halo]
        gd_ref = refs[2 + n_halo]
        pext = assemble(halo, p_layout)
        lane = lax.broadcasted_iota(jnp.int32, (BLK, BLK), 1)
        lo = lane < DH
        flip = (lane + lax.broadcasted_iota(jnp.int32, (BLK, BLK), 0) == BLK - 1).astype(
            jnp.bfloat16
        )
        gsum = jnp.zeros((2 * BLK, width), jnp.float32)
        for n in range(nb):
            cmask = cm_ref[n : n + 1, :]
            pw = pext[conv_start + n * BLK : conv_start + n * BLK + width]
            sr = jnp.dot(
                flip, s_ref[n * BLK : (n + 1) * BLK, :], preferred_element_type=jnp.float32
            ).astype(jnp.bfloat16)
            zero = jnp.zeros_like(sr)
            a = jnp.concatenate([jnp.where(lo, sr, zero), jnp.where(lo, zero, sr)], 0)
            g = lax.dot_general(
                a, pw, (((1,), (1,)), ((), ())), preferred_element_type=jnp.float32
            )
            gsum = gsum + g * cmask
        pad = jnp.zeros((BLK, BLK), jnp.float32)

        def diagonals(half):
            wide = jnp.concatenate([half, pad], 1)
            rolled = pltpu.roll(wide, 0, 1, stride=1, stride_axis=0)
            return rolled[:, :width].sum(0, keepdims=True)

        gd_ref[0] = jnp.concatenate([diagonals(gsum[:BLK]), diagonals(gsum[BLK:])], 0)

    return kernel


def make_conv_kernel(nb, width, span, conv_start, p_layout, s_layout, n_p, n_s):
    def kernel(*refs):
        qc_ref, qa_ref, cm_ref = refs[:3]
        halo_p = refs[3 : 3 + n_p]
        halo_s = refs[3 + n_p : 3 + n_p + n_s]
        q_ref, ct_ref, k_ref, v_ref = refs[3 + n_p + n_s : 7 + n_p + n_s]
        out_ref, gq_ref, gk_ref, gv_ref = refs[7 + n_p + n_s :]
        step = pl.program_id(0)
        pext = assemble(halo_p, p_layout)
        sext = assemble(halo_s, s_layout)
        lo = lax.broadcasted_iota(jnp.int32, (BLK, BLK), 1) < DH

        def table(ref, i, shift):
            row = ref[pl.ds(2 * step + i, 1), :]
            full = jnp.broadcast_to(row, (BLK, span))
            rolled = pltpu.roll(full, shift, 1, stride=1, stride_axis=0)
            return rolled[:, :width]

        tc = jnp.concatenate(
            [table(qc_ref, 0, span - (BLK - 1)), table(qc_ref, 1, span - (BLK - 1))], 0
        )
        ta = jnp.concatenate([table(qa_ref, 0, span - BLK), table(qa_ref, 1, span - BLK)], 0)
        for n in range(nb):
            rows = pl.ds(n * BLK, BLK)
            cmask = cm_ref[n : n + 1, :]
            amask = cm_ref[nb + n : nb + n + 1, :]
            pw = pext[conv_start + n * BLK : conv_start + n * BLK + width]
            sw = sext[n * BLK : n * BLK + width]
            conv2 = jnp.dot(
                (tc * cmask).astype(jnp.bfloat16), pw, preferred_element_type=jnp.float32
            )
            conv = jnp.where(lo, conv2[:BLK], conv2[BLK:])
            adj2 = jnp.dot(
                (ta * amask).astype(jnp.bfloat16), sw, preferred_element_type=jnp.float32
            )
            adj = jnp.where(lo, adj2[:BLK], adj2[BLK:])
            out_ref[rows, :] = (q_ref[rows, :].astype(jnp.float32) * conv).astype(jnp.bfloat16)
            gq_ref[rows, :] = (ct_ref[rows, :].astype(jnp.float32) * conv).astype(jnp.bfloat16)
            gk_ref[rows, :] = (adj * v_ref[rows, :].astype(jnp.float32)).astype(jnp.bfloat16)
            gv_ref[rows, :] = (adj * k_ref[rows, :].astype(jnp.float32)).astype(jnp.bfloat16)

    return kernel


def convolve_all(value_rows, key_rows, query_rows, cotangent, filter_taps, doc_blocks, lags):
    tok_rows, channels = value_rows.shape
    filters, taps_total = filter_taps.shape
    nb = tok_rows // BLK
    width = lags * BLK
    span = width + BLK
    base = (lags - 1) * BLK
    steps = channels // BLK
    far = -(-(lags - 1) // nb)
    part = (lags - 1) - (far - 1) * nb
    product = (key_rows.astype(jnp.float32) * value_rows.astype(jnp.float32)).astype(jnp.bfloat16)
    scaled = (cotangent.astype(jnp.float32) * query_rows.astype(jnp.float32)).astype(jnp.bfloat16)
    halo_p, halo_s = [], []
    p_layout = flatten_pieces(earlier_pieces(product, far, part, nb), halo_p)
    s_layout = flatten_pieces(later_pieces(scaled, far, part, nb), halo_s)
    conv_start = 0

    rounded = filter_taps.astype(jnp.bfloat16).astype(jnp.float32)
    kept = min(taps_total, span - BLK)
    qa = jnp.pad(rounded[:, :kept], ((0, 0), (BLK, span - BLK - kept)))
    qc = jnp.flip(qa, 1)

    margin = lags + nb
    padded = jnp.concatenate(
        [jnp.full((margin,), -1, jnp.int32), doc_blocks, jnp.full((margin,), -2, jnp.int32)], 0
    )
    shard = lax.axis_index("seq")
    window = lax.dynamic_slice_in_dim(padded, shard * nb + margin - (lags - 1), 2 * (lags - 1) + nb)
    own = jnp.stack([window[lags - 1 + n] for n in range(nb)])
    conv_docs = jnp.stack([window[n : n + lags] for n in range(nb)])
    adj_docs = jnp.stack([window[lags - 1 + n : lags - 1 + n + lags] for n in range(nb)])
    links = jnp.concatenate([conv_docs == own[:, None], adj_docs == own[:, None]], 0)
    cm = jnp.repeat(links.astype(jnp.float32), BLK, axis=1)

    whole = lambda shape: pl.BlockSpec(shape, lambda s: (0, 0))
    lanes = lambda r: pl.BlockSpec((r, BLK), lambda s: (0, s))
    params = pltpu.CompilerParams(
        dimension_semantics=("arbitrary",), vmem_limit_bytes=48 * 1024 * 1024
    )
    diag = pl.pallas_call(
        make_grad_kernel(nb, width, conv_start, p_layout, len(halo_p)),
        grid=(steps,),
        in_specs=[whole((2 * nb, width))]
        + [lanes(h.shape[0]) for h in halo_p]
        + [lanes(tok_rows)],
        out_specs=pl.BlockSpec((1, 2, width), lambda s: (s, 0, 0)),
        out_shape=jax.ShapeDtypeStruct((steps, 2, width), jnp.float32),
        compiler_params=params,
    )(cm, *halo_p, scaled)
    row_out = jax.ShapeDtypeStruct((tok_rows, channels), jnp.bfloat16)
    outs = pl.pallas_call(
        make_conv_kernel(
            nb, width, span, conv_start, p_layout, s_layout, len(halo_p), len(halo_s)
        ),
        grid=(steps,),
        in_specs=[whole((filters, span)), whole((filters, span)), whole((2 * nb, width))]
        + [lanes(h.shape[0]) for h in halo_p]
        + [lanes(h.shape[0]) for h in halo_s]
        + [lanes(tok_rows)] * 4,
        out_specs=[lanes(tok_rows)] * 4,
        out_shape=[row_out] * 4,
        compiler_params=params,
    )(qc, qa, cm, *halo_p, *halo_s, query_rows, cotangent, key_rows, value_rows)
    outs = list(outs) + [diag]
    output_rows, grad_query, grad_key, grad_value, diag = outs
    diag = diag.reshape(filters, width)
    top = min(taps_total, base + BLK)
    taps_grad = jnp.flip(diag[:, base + BLK - top : base + BLK], 1)
    if top < taps_total:
        taps_grad = jnp.pad(taps_grad, ((0, 0), (0, taps_total - top)))
    taps_grad = taps_grad * (1.0 / (tok_rows * lax.axis_size("seq")))
    grad_filter = doubled_total(taps_grad, ("head", "seq"))
    return output_rows, grad_query, grad_key, grad_value, grad_filter


def per_device(value_rows, key_rows, query_rows, cotangent, filter_taps, doc_blocks):
    tok_rows = value_rows.shape[0]
    taps_total = filter_taps.shape[1]
    full_lags = taps_total // BLK + 1
    short_lags = min(MOST, full_lags)
    args = (value_rows, key_rows, query_rows, cotangent, filter_taps, doc_blocks)
    nblk = doc_blocks.shape[0]
    apart = np.abs(np.arange(nblk)[:, None] - np.arange(nblk)[None, :])
    far_pairs = jnp.asarray((apart >= short_lags) & (apart < full_lags))
    same = doc_blocks[:, None] == doc_blocks[None, :]
    long_links = jnp.any(same & far_pairs)
    outs = lax.cond(
        long_links,
        lambda a: convolve_all(*a, full_lags),
        lambda a: convolve_all(*a, short_lags),
        args,
    )
    return tuple(outs)


def doubled_total(value, axes):
    for axis in axes:
        length = lax.axis_size(axis)
        bits = (length - 1).bit_length()
        for low in range(0, bits, 2):
            group = [1 << low] + ([1 << (low + 1)] if low + 1 < bits else [])
            swap = lambda m: lax.ppermute(value, axis, [(i, i ^ m) for i in range(length)])
            if len(group) == 1:
                value = value + swap(group[0])
            else:
                a, b = group
                value = (value + swap(a)) + (swap(b) + swap(a | b))
    return value


def solution(mesh):
    in_specs = (P("seq", "head"), P("seq", "head"), P("seq", "head"), P("seq", "head"), P(), P())
    out_specs = (P("seq", "head"), P("seq", "head"), P("seq", "head"), P("seq", "head"), P())
    return jax.shard_map(
        per_device, mesh=mesh, in_specs=in_specs, out_specs=out_specs, check_vma=False
    )
```

```python
import numpy as np
import jax
import jax.numpy as jnp
from jax import lax
from jax.experimental import pallas as pl
from jax.experimental.pallas import tpu as pltpu
from jax.sharding import PartitionSpec as P

DH = 64
BLK = 128
MOST = 12


def passed_along(value, axis, by):
    length = lax.axis_size(axis)
    pairs = [(i, i + by) for i in range(length) if 0 <= i + by < length]
    return lax.ppermute(value, axis, pairs)


def shifted_pairs(length, by, parity=None):
    return [
        (i, i + by)
        for i in range(length)
        if 0 <= i + by < length and (parity is None or (i + by) % 2 == parity)
    ]


def earlier_pieces(product, far, part, nb):
    length = lax.axis_size("seq")
    rounds = far // 2
    rows = product.shape[0]
    chain = [product]
    for r in range(1, rounds):
        chain.append(lax.ppermute(chain[-1], "seq", shifted_pairs(length, 2)))
    if part == nb:
        last_full = lax.ppermute(chain[-1], "seq", shifted_pairs(length, 2))
        tail = [(last_full, 0, rows)]
    else:
        last_full = lax.ppermute(chain[-1], "seq", shifted_pairs(length, 2, 1))
        last_part = lax.ppermute(
            chain[-1][(nb - part) * BLK :], "seq", shifted_pairs(length, 2, 0)
        )
        tail = [(last_part, 0, part * BLK), (last_full, (nb - part) * BLK, part * BLK)]
    offers = chain[1:] + [last_full]
    to_odd = [(i, i + 1) for i in range(0, length, 2)]
    to_even = [(i, i - 1) for i in range(1, length, 2)]
    odd = [
        [(lax.ppermute(chain[k], "seq", to_odd), 0, rows),
         (lax.ppermute(offers[k], "seq", to_even), 0, rows)]
        for k in range(rounds)
    ]
    pieces = [tail]
    for r in range(rounds, 0, -1):
        pieces.append(odd[r - 1])
        if r > 1:
            pieces.append([(chain[r - 1], 0, rows)])
    pieces.append([(product, 0, rows)])
    return pieces


def later_pieces(scaled, far, part, nb):
    length = lax.axis_size("seq")
    rounds = far // 2
    rows = scaled.shape[0]
    chain = [scaled]
    for r in range(1, rounds):
        chain.append(lax.ppermute(chain[-1], "seq", shifted_pairs(length, -2)))
    if part == nb:
        last_full = lax.ppermute(chain[-1], "seq", shifted_pairs(length, -2))
        tail = [(last_full, 0, rows)]
    else:
        last_full = lax.ppermute(chain[-1], "seq", shifted_pairs(length, -2, 0))
        last_part = lax.ppermute(chain[-1][: part * BLK], "seq", shifted_pairs(length, -2, 1))
        tail = [(last_part, 0, part * BLK), (last_full, 0, part * BLK)]
    offers = chain[1:] + [last_full]
    to_even = [(i, i - 1) for i in range(1, length, 2)]
    to_odd = [(i, i + 1) for i in range(0, length, 2)]
    odd = [
        [(lax.ppermute(chain[k], "seq", to_even), 0, rows),
         (lax.ppermute(offers[k], "seq", to_odd), 0, rows)]
        for k in range(rounds)
    ]
    pieces = [[(scaled, 0, rows)]]
    for r in range(1, rounds + 1):
        pieces.append(odd[r - 1])
        if r < rounds:
            pieces.append([(chain[r], 0, rows)])
    pieces.append(tail)
    return pieces


def flatten_pieces(pieces, arrays):
    layout = []
    for piece in pieces:
        terms = []
        for arr, start, rows in piece:
            for idx, known in enumerate(arrays):
                if known is arr:
                    break
            else:
                arrays.append(arr)
                idx = len(arrays) - 1
            terms.append((idx, start, rows))
        layout.append(terms)
    return layout


def assemble(halo, layout):
    pieces = []
    for terms in layout:
        total = None
        for idx, start, rows in terms:
            term = halo[idx][start : start + rows, :]
            total = term if total is None else total + term
        pieces.append(total)
    return jnp.concatenate(pieces, 0)


def make_grad_kernel(nb, width, conv_start, p_layout, n_halo):
    def kernel(*refs):
        cm_ref = refs[0]
        halo = refs[1 : 1 + n_halo]
        s_ref = refs[1 + n_halo]
        gd_ref = refs[2 + n_halo]
        pext = assemble(halo, p_layout)
        lane = lax.broadcasted_iota(jnp.int32, (BLK, BLK), 1)
        lo = lane < DH
        flip = (lane + lax.broadcasted_iota(jnp.int32, (BLK, BLK), 0) == BLK - 1).astype(
            jnp.bfloat16
        )
        gsum = jnp.zeros((2 * BLK, width), jnp.float32)
        for n in range(nb):
            cmask = cm_ref[n : n + 1, :]
            pw = pext[conv_start + n * BLK : conv_start + n * BLK + width]
            sr = jnp.dot(
                flip, s_ref[n * BLK : (n + 1) * BLK, :], preferred_element_type=jnp.float32
            ).astype(jnp.bfloat16)
            zero = jnp.zeros_like(sr)
            a = jnp.concatenate([jnp.where(lo, sr, zero), jnp.where(lo, zero, sr)], 0)
            g = lax.dot_general(
                a, pw, (((1,), (1,)), ((), ())), preferred_element_type=jnp.float32
            )
            gsum = gsum + g * cmask
        pad = jnp.zeros((BLK, BLK), jnp.float32)

        def diagonals(half):
            wide = jnp.concatenate([half, pad], 1)
            rolled = pltpu.roll(wide, 0, 1, stride=1, stride_axis=0)
            return rolled[:, :width].sum(0, keepdims=True)

        gd_ref[0] = jnp.concatenate([diagonals(gsum[:BLK]), diagonals(gsum[BLK:])], 0)

    return kernel


def make_conv_kernel(nb, width, span, conv_start, p_layout, s_layout, n_p, n_s):
    def kernel(*refs):
        qc_ref, qa_ref, cm_ref = refs[:3]
        halo_p = refs[3 : 3 + n_p]
        halo_s = refs[3 + n_p : 3 + n_p + n_s]
        q_ref, ct_ref, k_ref, v_ref = refs[3 + n_p + n_s : 7 + n_p + n_s]
        out_ref, gq_ref, gk_ref, gv_ref = refs[7 + n_p + n_s :]
        step = pl.program_id(0)
        pext = assemble(halo_p, p_layout)
        sext = assemble(halo_s, s_layout)
        lo = lax.broadcasted_iota(jnp.int32, (BLK, BLK), 1) < DH

        def table(ref, i, shift):
            row = ref[pl.ds(2 * step + i, 1), :]
            full = jnp.broadcast_to(row, (BLK, span))
            rolled = pltpu.roll(full, shift, 1, stride=1, stride_axis=0)
            return rolled[:, :width]

        tc = jnp.concatenate(
            [table(qc_ref, 0, span - (BLK - 1)), table(qc_ref, 1, span - (BLK - 1))], 0
        )
        ta = jnp.concatenate([table(qa_ref, 0, span - BLK), table(qa_ref, 1, span - BLK)], 0)
        for n in range(nb):
            rows = pl.ds(n * BLK, BLK)
            cmask = cm_ref[n : n + 1, :]
            amask = cm_ref[nb + n : nb + n + 1, :]
            pw = pext[conv_start + n * BLK : conv_start + n * BLK + width]
            sw = sext[n * BLK : n * BLK + width]
            conv2 = jnp.dot(
                (tc * cmask).astype(jnp.bfloat16), pw, preferred_element_type=jnp.float32
            )
            conv = jnp.where(lo, conv2[:BLK], conv2[BLK:])
            adj2 = jnp.dot(
                (ta * amask).astype(jnp.bfloat16), sw, preferred_element_type=jnp.float32
            )
            adj = jnp.where(lo, adj2[:BLK], adj2[BLK:])
            out_ref[rows, :] = (q_ref[rows, :].astype(jnp.float32) * conv).astype(jnp.bfloat16)
            gq_ref[rows, :] = (ct_ref[rows, :].astype(jnp.float32) * conv).astype(jnp.bfloat16)
            gk_ref[rows, :] = (adj * v_ref[rows, :].astype(jnp.float32)).astype(jnp.bfloat16)
            gv_ref[rows, :] = (adj * k_ref[rows, :].astype(jnp.float32)).astype(jnp.bfloat16)

    return kernel


def convolve_all(value_rows, key_rows, query_rows, cotangent, filter_taps, doc_blocks, lags):
    tok_rows, channels = value_rows.shape
    filters, taps_total = filter_taps.shape
    nb = tok_rows // BLK
    width = lags * BLK
    span = width + BLK
    base = (lags - 1) * BLK
    steps = channels // BLK
    far = -(-(lags - 1) // nb)
    part = (lags - 1) - (far - 1) * nb
    product = (key_rows.astype(jnp.float32) * value_rows.astype(jnp.float32)).astype(jnp.bfloat16)
    scaled = (cotangent.astype(jnp.float32) * query_rows.astype(jnp.float32)).astype(jnp.bfloat16)
    halo_p, halo_s = [], []
    p_layout = flatten_pieces(earlier_pieces(product, far, part, nb), halo_p)
    s_layout = flatten_pieces(later_pieces(scaled, far, part, nb), halo_s)
    conv_start = 0

    rounded = filter_taps.astype(jnp.bfloat16).astype(jnp.float32)
    kept = min(taps_total, span - BLK)
    qa = jnp.pad(rounded[:, :kept], ((0, 0), (BLK, span - BLK - kept)))
    qc = jnp.flip(qa, 1)

    margin = lags + nb
    padded = jnp.concatenate(
        [jnp.full((margin,), -1, jnp.int32), doc_blocks, jnp.full((margin,), -2, jnp.int32)], 0
    )
    shard = lax.axis_index("seq")
    window = lax.dynamic_slice_in_dim(padded, shard * nb + margin - (lags - 1), 2 * (lags - 1) + nb)
    own = jnp.stack([window[lags - 1 + n] for n in range(nb)])
    conv_docs = jnp.stack([window[n : n + lags] for n in range(nb)])
    adj_docs = jnp.stack([window[lags - 1 + n : lags - 1 + n + lags] for n in range(nb)])
    links = jnp.concatenate([conv_docs == own[:, None], adj_docs == own[:, None]], 0)
    cm = jnp.repeat(links.astype(jnp.float32), BLK, axis=1)

    whole = lambda shape: pl.BlockSpec(shape, lambda s: (0, 0))
    lanes = lambda r: pl.BlockSpec((r, BLK), lambda s: (0, s))
    params = pltpu.CompilerParams(
        dimension_semantics=("arbitrary",), vmem_limit_bytes=48 * 1024 * 1024
    )
    cm_g, scaled_g, halo_pg, _ = lax.optimization_barrier((cm, scaled, halo_p, halo_s))
    diag = pl.pallas_call(
        make_grad_kernel(nb, width, conv_start, p_layout, len(halo_p)),
        grid=(steps,),
        in_specs=[whole((2 * nb, width))]
        + [lanes(h.shape[0]) for h in halo_p]
        + [lanes(tok_rows)],
        out_specs=pl.BlockSpec((1, 2, width), lambda s: (s, 0, 0)),
        out_shape=jax.ShapeDtypeStruct((steps, 2, width), jnp.float32),
        compiler_params=params,
    )(cm_g, *halo_pg, scaled_g)
    row_out = jax.ShapeDtypeStruct((tok_rows, channels), jnp.bfloat16)
    outs = pl.pallas_call(
        make_conv_kernel(
            nb, width, span, conv_start, p_layout, s_layout, len(halo_p), len(halo_s)
        ),
        grid=(steps,),
        in_specs=[whole((filters, span)), whole((filters, span)), whole((2 * nb, width))]
        + [lanes(h.shape[0]) for h in halo_p]
        + [lanes(h.shape[0]) for h in halo_s]
        + [lanes(tok_rows)] * 4,
        out_specs=[lanes(tok_rows)] * 4,
        out_shape=[row_out] * 4,
        compiler_params=params,
    )(qc, qa, cm, *halo_p, *halo_s, query_rows, cotangent, key_rows, value_rows)
    outs = list(outs) + [diag]
    output_rows, grad_query, grad_key, grad_value, diag = outs
    diag = diag.reshape(filters, width)
    top = min(taps_total, base + BLK)
    taps_grad = jnp.flip(diag[:, base + BLK - top : base + BLK], 1)
    if top < taps_total:
        taps_grad = jnp.pad(taps_grad, ((0, 0), (0, taps_total - top)))
    taps_grad = taps_grad * (1.0 / (tok_rows * lax.axis_size("seq")))
    grad_filter = doubled_total(taps_grad, ("head", "seq"))
    return output_rows, grad_query, grad_key, grad_value, grad_filter


def per_device(value_rows, key_rows, query_rows, cotangent, filter_taps, doc_blocks):
    tok_rows = value_rows.shape[0]
    taps_total = filter_taps.shape[1]
    full_lags = taps_total // BLK + 1
    short_lags = min(MOST, full_lags)
    args = (value_rows, key_rows, query_rows, cotangent, filter_taps, doc_blocks)
    nblk = doc_blocks.shape[0]
    apart = np.abs(np.arange(nblk)[:, None] - np.arange(nblk)[None, :])
    far_pairs = jnp.asarray((apart >= short_lags) & (apart < full_lags))
    same = doc_blocks[:, None] == doc_blocks[None, :]
    long_links = jnp.any(same & far_pairs)
    outs = lax.cond(
        long_links,
        lambda a: convolve_all(*a, full_lags),
        lambda a: convolve_all(*a, short_lags),
        args,
    )
    return tuple(outs)


def doubled_total(value, axes):
    for axis in axes:
        length = lax.axis_size(axis)
        bits = (length - 1).bit_length()
        for low in range(0, bits, 2):
            group = [1 << low] + ([1 << (low + 1)] if low + 1 < bits else [])
            swap = lambda m: lax.ppermute(value, axis, [(i, i ^ m) for i in range(length)])
            if len(group) == 1:
                value = value + swap(group[0])
            else:
                a, b = group
                value = (value + swap(a)) + (swap(b) + swap(a | b))
    return value


def solution(mesh):
    in_specs = (P("seq", "head"), P("seq", "head"), P("seq", "head"), P("seq", "head"), P(), P())
    out_specs = (P("seq", "head"), P("seq", "head"), P("seq", "head"), P("seq", "head"), P())
    return jax.shard_map(
        per_device, mesh=mesh, in_specs=in_specs, out_specs=out_specs, check_vma=False
    )
```

```python
import numpy as np
import jax
import jax.numpy as jnp
from jax import lax
from jax.experimental import pallas as pl
from jax.experimental.pallas import tpu as pltpu
from jax.sharding import PartitionSpec as P

DH = 64
BLK = 128
MOST = 12


def passed_along(value, axis, by):
    length = lax.axis_size(axis)
    pairs = [(i, i + by) for i in range(length) if 0 <= i + by < length]
    return lax.ppermute(value, axis, pairs)


def shifted_pairs(length, by, parity=None):
    return [
        (i, i + by)
        for i in range(length)
        if 0 <= i + by < length and (parity is None or (i + by) % 2 == parity)
    ]


def halo_pieces(product, scaled, far, part, nb):
    length = lax.axis_size("seq")
    rounds = far // 2
    rows = product.shape[0]
    chain_p, chain_s = [product], [scaled]
    for r in range(rounds):
        chain_p.append(lax.ppermute(chain_p[-1], "seq", shifted_pairs(length, 2)))
        chain_s.append(lax.ppermute(chain_s[-1], "seq", shifted_pairs(length, -2)))
    to_odd = [(i, i + 1) for i in range(0, length, 2)]
    to_even = [(i, i - 1) for i in range(1, length, 2)]
    odd_p, odd_s = [], []
    for k in range(rounds):
        up = lax.ppermute(jnp.concatenate([chain_p[k], chain_s[k + 1]], 1), "seq", to_odd)
        down = lax.ppermute(jnp.concatenate([chain_p[k + 1], chain_s[k]], 1), "seq", to_even)
        odd_p.append([(up, 0, 0, rows), (down, 0, 0, rows)])
        odd_s.append([(up, 1, 0, rows), (down, 1, 0, rows)])
    p_pieces = [[(chain_p[rounds], 0, (nb - part) * BLK, part * BLK)]]
    for r in range(rounds, 0, -1):
        p_pieces.append(odd_p[r - 1])
        if r > 1:
            p_pieces.append([(chain_p[r - 1], 0, 0, rows)])
    p_pieces.append([(product, 0, 0, rows)])
    s_pieces = [[(scaled, 0, 0, rows)]]
    for r in range(1, rounds + 1):
        s_pieces.append(odd_s[r - 1])
        if r < rounds:
            s_pieces.append([(chain_s[r], 0, 0, rows)])
    s_pieces.append([(chain_s[rounds], 0, 0, part * BLK)])
    return p_pieces, s_pieces


def flatten_pieces(pieces, inputs):
    layout = []
    for piece in pieces:
        terms = []
        for arr, half, start, rows in piece:
            for idx, (known, known_half) in enumerate(inputs):
                if known is arr and known_half == half:
                    break
            else:
                inputs.append((arr, half))
                idx = len(inputs) - 1
            terms.append((idx, start, rows))
        layout.append(terms)
    return layout


def make_kernel(nb, lags, width, span, conv_start, p_layout, s_layout, n_halo):
    def kernel(*refs):
        qc_ref, qa_ref, cm_ref = refs[:3]
        halo = refs[3 : 3 + n_halo]
        q_ref, ct_ref, k_ref, v_ref = refs[3 + n_halo : 7 + n_halo]
        out_ref, gq_ref, gk_ref, gv_ref, gd_ref = refs[7 + n_halo :]
        step = pl.program_id(0)

        def assemble(layout):
            pieces = []
            for terms in layout:
                total = None
                for idx, start, rows in terms:
                    term = halo[idx][start : start + rows, :]
                    total = term if total is None else total + term
                pieces.append(total)
            return jnp.concatenate(pieces, 0)

        pext = assemble(p_layout)
        sext = assemble(s_layout)
        lane = lax.broadcasted_iota(jnp.int32, (BLK, BLK), 1)
        lo = lane < DH
        flip = (lane + lax.broadcasted_iota(jnp.int32, (BLK, BLK), 0) == BLK - 1).astype(
            jnp.bfloat16
        )

        def table(ref, i, shift):
            row = ref[pl.ds(2 * step + i, 1), :]
            full = jnp.broadcast_to(row, (BLK, span))
            rolled = pltpu.roll(full, shift, 1, stride=1, stride_axis=0)
            return rolled[:, :width]

        tc = jnp.concatenate(
            [table(qc_ref, 0, span - (BLK - 1)), table(qc_ref, 1, span - (BLK - 1))], 0
        )
        ta = jnp.concatenate([table(qa_ref, 0, span - BLK), table(qa_ref, 1, span - BLK)], 0)
        gsum = jnp.zeros((2 * BLK, width), jnp.float32)
        for n in range(nb):
            rows = pl.ds(n * BLK, BLK)
            cmask = cm_ref[n : n + 1, :]
            amask = cm_ref[nb + n : nb + n + 1, :]
            pw = pext[conv_start + n * BLK : conv_start + n * BLK + width]
            sw = sext[n * BLK : n * BLK + width]
            conv2 = jnp.dot(
                (tc * cmask).astype(jnp.bfloat16), pw, preferred_element_type=jnp.float32
            )
            conv = jnp.where(lo, conv2[:BLK], conv2[BLK:])
            adj2 = jnp.dot(
                (ta * amask).astype(jnp.bfloat16), sw, preferred_element_type=jnp.float32
            )
            adj = jnp.where(lo, adj2[:BLK], adj2[BLK:])
            out_ref[rows, :] = (q_ref[rows, :].astype(jnp.float32) * conv).astype(jnp.bfloat16)
            gq_ref[rows, :] = (ct_ref[rows, :].astype(jnp.float32) * conv).astype(jnp.bfloat16)
            gk_ref[rows, :] = (adj * v_ref[rows, :].astype(jnp.float32)).astype(jnp.bfloat16)
            gv_ref[rows, :] = (adj * k_ref[rows, :].astype(jnp.float32)).astype(jnp.bfloat16)
            sr = jnp.dot(
                flip, sext[n * BLK : (n + 1) * BLK], preferred_element_type=jnp.float32
            ).astype(jnp.bfloat16)
            zero = jnp.zeros_like(sr)
            a = jnp.concatenate([jnp.where(lo, sr, zero), jnp.where(lo, zero, sr)], 0)
            g = lax.dot_general(
                a, pw, (((1,), (1,)), ((), ())), preferred_element_type=jnp.float32
            )
            gsum = gsum + g * cmask
        pad = jnp.zeros((BLK, BLK), jnp.float32)

        def diagonals(half):
            wide = jnp.concatenate([half, pad], 1)
            rolled = pltpu.roll(wide, 0, 1, stride=1, stride_axis=0)
            return rolled[:, :width].sum(0, keepdims=True)

        gd_ref[0] = jnp.concatenate([diagonals(gsum[:BLK]), diagonals(gsum[BLK:])], 0)

    return kernel


def convolve_all(value_rows, key_rows, query_rows, cotangent, filter_taps, doc_blocks, lags):
    tok_rows, channels = value_rows.shape
    filters, taps_total = filter_taps.shape
    nb = tok_rows // BLK
    width = lags * BLK
    span = width + BLK
    base = (lags - 1) * BLK
    steps = channels // BLK
    far = -(-(lags - 1) // nb)
    part = (lags - 1) - (far - 1) * nb
    product = (key_rows.astype(jnp.float32) * value_rows.astype(jnp.float32)).astype(jnp.bfloat16)
    scaled = (cotangent.astype(jnp.float32) * query_rows.astype(jnp.float32)).astype(jnp.bfloat16)
    halo = []
    p_pieces, s_pieces = halo_pieces(product, scaled, far, part, nb)
    p_layout = flatten_pieces(p_pieces, halo)
    s_layout = flatten_pieces(s_pieces, halo)
    conv_start = 0

    rounded = filter_taps.astype(jnp.bfloat16).astype(jnp.float32)
    kept = min(taps_total, span - BLK)
    qa = jnp.pad(rounded[:, :kept], ((0, 0), (BLK, span - BLK - kept)))
    qc = jnp.flip(qa, 1)

    margin = lags + nb
    padded = jnp.concatenate(
        [jnp.full((margin,), -1, jnp.int32), doc_blocks, jnp.full((margin,), -2, jnp.int32)], 0
    )
    shard = lax.axis_index("seq")
    window = lax.dynamic_slice_in_dim(padded, shard * nb + margin - (lags - 1), 2 * (lags - 1) + nb)
    own = jnp.stack([window[lags - 1 + n] for n in range(nb)])
    conv_docs = jnp.stack([window[n : n + lags] for n in range(nb)])
    adj_docs = jnp.stack([window[lags - 1 + n : lags - 1 + n + lags] for n in range(nb)])
    links = jnp.concatenate([conv_docs == own[:, None], adj_docs == own[:, None]], 0)
    cm = jnp.repeat(links.astype(jnp.float32), BLK, axis=1)

    whole = lambda shape: pl.BlockSpec(shape, lambda s: (0, 0))
    lanes = lambda r: pl.BlockSpec((r, BLK), lambda s: (0, s))
    kernel = make_kernel(nb, lags, width, span, conv_start, p_layout, s_layout, len(halo))
    outs = pl.pallas_call(
        kernel,
        grid=(steps,),
        in_specs=[
            whole((filters, span)),
            whole((filters, span)),
            whole((2 * nb, width)),
            *[
                pl.BlockSpec((h.shape[0], BLK), lambda s, o=half * steps: (0, s + o))
                for h, half in halo
            ],
            lanes(tok_rows),
            lanes(tok_rows),
            lanes(tok_rows),
            lanes(tok_rows),
        ],
        out_specs=[
            lanes(tok_rows),
            lanes(tok_rows),
            lanes(tok_rows),
            lanes(tok_rows),
            pl.BlockSpec((1, 2, width), lambda s: (s, 0, 0)),
        ],
        out_shape=[
            jax.ShapeDtypeStruct((tok_rows, channels), jnp.bfloat16),
            jax.ShapeDtypeStruct((tok_rows, channels), jnp.bfloat16),
            jax.ShapeDtypeStruct((tok_rows, channels), jnp.bfloat16),
            jax.ShapeDtypeStruct((tok_rows, channels), jnp.bfloat16),
            jax.ShapeDtypeStruct((steps, 2, width), jnp.float32),
        ],
        compiler_params=pltpu.CompilerParams(
            dimension_semantics=("arbitrary",), vmem_limit_bytes=48 * 1024 * 1024
        ),
    )(qc, qa, cm, *[h for h, _ in halo], query_rows, cotangent, key_rows, value_rows)
    output_rows, grad_query, grad_key, grad_value, diag = outs
    diag = diag.reshape(filters, width)
    top = min(taps_total, base + BLK)
    taps_grad = jnp.flip(diag[:, base + BLK - top : base + BLK], 1)
    if top < taps_total:
        taps_grad = jnp.pad(taps_grad, ((0, 0), (0, taps_total - top)))
    return output_rows, grad_query, grad_key, grad_value, taps_grad


def per_device(value_rows, key_rows, query_rows, cotangent, filter_taps, doc_blocks):
    tok_rows = value_rows.shape[0]
    taps_total = filter_taps.shape[1]
    full_lags = taps_total // BLK + 1
    short_lags = min(MOST, full_lags)
    args = (value_rows, key_rows, query_rows, cotangent, filter_taps, doc_blocks)
    nblk = doc_blocks.shape[0]
    apart = np.abs(np.arange(nblk)[:, None] - np.arange(nblk)[None, :])
    far_pairs = jnp.asarray((apart >= short_lags) & (apart < full_lags))
    same = doc_blocks[:, None] == doc_blocks[None, :]
    long_links = jnp.any(same & far_pairs)
    outs = lax.cond(
        long_links,
        lambda a: convolve_all(*a, full_lags),
        lambda a: convolve_all(*a, short_lags),
        args,
    )
    output_rows, grad_query, grad_key, grad_value, taps_grad = outs
    taps_grad = taps_grad * (1.0 / (tok_rows * lax.axis_size("seq")))
    grad_filter = doubled_total(taps_grad, ("head", "seq"))
    return (output_rows, grad_query, grad_key, grad_value, grad_filter)


def doubled_total(value, axes):
    for axis in axes:
        length = lax.axis_size(axis)
        bits = (length - 1).bit_length()
        for low in range(0, bits, 2):
            group = [1 << low] + ([1 << (low + 1)] if low + 1 < bits else [])
            swap = lambda m: lax.ppermute(value, axis, [(i, i ^ m) for i in range(length)])
            if len(group) == 1:
                value = value + swap(group[0])
            else:
                a, b = group
                value = (value + swap(a)) + (swap(b) + swap(a | b))
    return value


def solution(mesh):
    in_specs = (P("seq", "head"), P("seq", "head"), P("seq", "head"), P("seq", "head"), P(), P())
    out_specs = (P("seq", "head"), P("seq", "head"), P("seq", "head"), P("seq", "head"), P())
    return jax.shard_map(
        per_device, mesh=mesh, in_specs=in_specs, out_specs=out_specs, check_vma=False
    )
```

```python
import numpy as np
import jax
import jax.numpy as jnp
from jax import lax
from jax.experimental import pallas as pl
from jax.experimental.pallas import tpu as pltpu
from jax.sharding import PartitionSpec as P

DH = 64
BLK = 128
MOST = 12


def passed_along(value, axis, by):
    length = lax.axis_size(axis)
    pairs = [(i, i + by) for i in range(length) if 0 <= i + by < length]
    return lax.ppermute(value, axis, pairs)


def shifted_pairs(length, by, parity=None):
    return [
        (i, i + by)
        for i in range(length)
        if 0 <= i + by < length and (parity is None or (i + by) % 2 == parity)
    ]


def halo_pieces(product, scaled, far, part, nb):
    length = lax.axis_size("seq")
    rounds = far // 2
    rows = product.shape[0]
    chain_p, chain_s = [product], [scaled]
    for r in range(rounds):
        chain_p.append(lax.ppermute(chain_p[-1], "seq", shifted_pairs(length, 2)))
        chain_s.append(lax.ppermute(chain_s[-1], "seq", shifted_pairs(length, -2)))
    to_odd = [(i, i + 1) for i in range(0, length, 2)]
    to_even = [(i, i - 1) for i in range(1, length, 2)]
    odd_p, odd_s = [], []
    for k in range(rounds):
        up = lax.ppermute(jnp.concatenate([chain_p[k], chain_s[k + 1]], 1), "seq", to_odd)
        down = lax.ppermute(jnp.concatenate([chain_p[k + 1], chain_s[k]], 1), "seq", to_even)
        odd_p.append([(up, 0, 0, rows), (down, 0, 0, rows)])
        odd_s.append([(up, 1, 0, rows), (down, 1, 0, rows)])
    p_pieces = [[(chain_p[rounds], 0, (nb - part) * BLK, part * BLK)]]
    for r in range(rounds, 0, -1):
        p_pieces.append(odd_p[r - 1])
        if r > 1:
            p_pieces.append([(chain_p[r - 1], 0, 0, rows)])
    p_pieces.append([(product, 0, 0, rows)])
    s_pieces = [[(scaled, 0, 0, rows)]]
    for r in range(1, rounds + 1):
        s_pieces.append(odd_s[r - 1])
        if r < rounds:
            s_pieces.append([(chain_s[r], 0, 0, rows)])
    s_pieces.append([(chain_s[rounds], 0, 0, part * BLK)])
    return p_pieces, s_pieces


def flatten_pieces(pieces, inputs):
    layout = []
    for piece in pieces:
        terms = []
        for arr, half, start, rows in piece:
            for idx, (known, known_half) in enumerate(inputs):
                if known is arr and known_half == half:
                    break
            else:
                inputs.append((arr, half))
                idx = len(inputs) - 1
            terms.append((idx, start, rows))
        layout.append(terms)
    return layout


def make_kernel(nb, lags, width, span, conv_start, p_layout, s_layout, n_halo, sub):
    def kernel(*refs):
        qc_ref, qa_ref, lk_ref = refs[:3]
        halo = refs[3 : 3 + n_halo]
        q_ref, ct_ref, k_ref, v_ref = refs[3 + n_halo : 7 + n_halo]
        out_ref, gq_ref, gk_ref, gv_ref, gd_ref = refs[7 + n_halo :]
        step = pl.program_id(0)
        lane = lax.broadcasted_iota(jnp.int32, (BLK, BLK), 1)
        lo = lane < DH
        flip = (lane + lax.broadcasted_iota(jnp.int32, (BLK, BLK), 0) == BLK - 1).astype(
            jnp.bfloat16
        )
        pad = jnp.zeros((BLK, BLK), jnp.float32)

        def assemble(layout, cols):
            pieces = []
            for terms in layout:
                total = None
                for idx, start, rows in terms:
                    term = halo[idx][start : start + rows, cols]
                    total = term if total is None else total + term
                pieces.append(total)
            return jnp.concatenate(pieces, 0)

        def masked(window, row):
            blocks = []
            for c in range(lags):
                block = window[c * BLK : (c + 1) * BLK]
                blocks.append(jnp.where(lk_ref[row, c] > 0, block, jnp.zeros_like(block)))
            return jnp.concatenate(blocks, 0)

        def table(ref, f, shift):
            row = ref[pl.ds(f, 1), :]
            full = jnp.broadcast_to(row, (BLK, span))
            rolled = pltpu.roll(full, shift, 1, stride=1, stride_axis=0)
            return rolled[:, :width]

        def diagonals(half):
            wide = jnp.concatenate([half, pad], 1)
            rolled = pltpu.roll(wide, 0, 1, stride=1, stride_axis=0)
            return rolled[:, :width].sum(0, keepdims=True)

        for j in range(sub):
            cols = slice(j * BLK, (j + 1) * BLK)
            f0 = 2 * (sub * step + j)
            pext = assemble(p_layout, cols)
            sext = assemble(s_layout, cols)
            tc = jnp.concatenate(
                [table(qc_ref, f0, span - (BLK - 1)), table(qc_ref, f0 + 1, span - (BLK - 1))], 0
            ).astype(jnp.bfloat16)
            ta = jnp.concatenate(
                [table(qa_ref, f0, span - BLK), table(qa_ref, f0 + 1, span - BLK)], 0
            ).astype(jnp.bfloat16)
            gsum = jnp.zeros((2 * BLK, width), jnp.float32)
            for n in range(nb):
                rows = pl.ds(n * BLK, BLK)
                lanes_j = pl.ds(j * BLK, BLK)
                pw = masked(pext[conv_start + n * BLK : conv_start + n * BLK + width], n)
                sw = masked(sext[n * BLK : n * BLK + width], nb + n)
                conv2 = jnp.dot(tc, pw, preferred_element_type=jnp.float32)
                conv = jnp.where(lo, conv2[:BLK], conv2[BLK:])
                adj2 = jnp.dot(ta, sw, preferred_element_type=jnp.float32)
                adj = jnp.where(lo, adj2[:BLK], adj2[BLK:])
                q = q_ref[rows, lanes_j].astype(jnp.float32)
                out_ref[rows, lanes_j] = (q * conv).astype(jnp.bfloat16)
                ct = ct_ref[rows, lanes_j].astype(jnp.float32)
                gq_ref[rows, lanes_j] = (ct * conv).astype(jnp.bfloat16)
                v = v_ref[rows, lanes_j].astype(jnp.float32)
                gk_ref[rows, lanes_j] = (adj * v).astype(jnp.bfloat16)
                k = k_ref[rows, lanes_j].astype(jnp.float32)
                gv_ref[rows, lanes_j] = (adj * k).astype(jnp.bfloat16)
                sr = jnp.dot(
                    flip, sext[n * BLK : (n + 1) * BLK], preferred_element_type=jnp.float32
                ).astype(jnp.bfloat16)
                zero = jnp.zeros_like(sr)
                a = jnp.concatenate([jnp.where(lo, sr, zero), jnp.where(lo, zero, sr)], 0)
                gsum = gsum + lax.dot_general(
                    a, pw, (((1,), (1,)), ((), ())), preferred_element_type=jnp.float32
                )
            gd_ref[0, 2 * j : 2 * j + 2, :] = jnp.concatenate(
                [diagonals(gsum[:BLK]), diagonals(gsum[BLK:])], 0
            )

    return kernel


def convolve_all(value_rows, key_rows, query_rows, cotangent, filter_taps, doc_blocks, lags):
    tok_rows, channels = value_rows.shape
    filters, taps_total = filter_taps.shape
    nb = tok_rows // BLK
    width = lags * BLK
    span = width + BLK
    base = (lags - 1) * BLK
    sub = 2
    steps = channels // (BLK * sub)
    far = -(-(lags - 1) // nb)
    part = (lags - 1) - (far - 1) * nb
    product = (key_rows.astype(jnp.float32) * value_rows.astype(jnp.float32)).astype(jnp.bfloat16)
    scaled = (cotangent.astype(jnp.float32) * query_rows.astype(jnp.float32)).astype(jnp.bfloat16)
    halo = []
    p_pieces, s_pieces = halo_pieces(product, scaled, far, part, nb)
    p_layout = flatten_pieces(p_pieces, halo)
    s_layout = flatten_pieces(s_pieces, halo)
    conv_start = 0

    rounded = filter_taps.astype(jnp.bfloat16).astype(jnp.float32)
    kept = min(taps_total, span - BLK)
    qa = jnp.pad(rounded[:, :kept], ((0, 0), (BLK, span - BLK - kept)))
    qc = jnp.flip(qa, 1)

    margin = lags + nb
    padded = jnp.concatenate(
        [jnp.full((margin,), -1, jnp.int32), doc_blocks, jnp.full((margin,), -2, jnp.int32)], 0
    )
    shard = lax.axis_index("seq")
    window = lax.dynamic_slice_in_dim(padded, shard * nb + margin - (lags - 1), 2 * (lags - 1) + nb)
    own = jnp.stack([window[lags - 1 + n] for n in range(nb)])
    conv_docs = jnp.stack([window[n : n + lags] for n in range(nb)])
    adj_docs = jnp.stack([window[lags - 1 + n : lags - 1 + n + lags] for n in range(nb)])
    links = jnp.concatenate([conv_docs == own[:, None], adj_docs == own[:, None]], 0)
    links = links.astype(jnp.int32)

    whole = lambda shape: pl.BlockSpec(shape, lambda s: (0, 0))
    lanes = lambda r: pl.BlockSpec((r, BLK * sub), lambda s: (0, s))
    kernel = make_kernel(
        nb, lags, width, span, conv_start, p_layout, s_layout, len(halo), sub
    )
    outs = pl.pallas_call(
        kernel,
        grid=(steps,),
        in_specs=[
            whole((filters, span)),
            whole((filters, span)),
            pl.BlockSpec(memory_space=pltpu.SMEM),
            *[
                pl.BlockSpec((h.shape[0], BLK * sub), lambda s, o=half * steps: (0, s + o))
                for h, half in halo
            ],
            lanes(tok_rows),
            lanes(tok_rows),
            lanes(tok_rows),
            lanes(tok_rows),
        ],
        out_specs=[
            lanes(tok_rows),
            lanes(tok_rows),
            lanes(tok_rows),
            lanes(tok_rows),
            pl.BlockSpec((1, 2 * sub, width), lambda s: (s, 0, 0)),
        ],
        out_shape=[
            jax.ShapeDtypeStruct((tok_rows, channels), jnp.bfloat16),
            jax.ShapeDtypeStruct((tok_rows, channels), jnp.bfloat16),
            jax.ShapeDtypeStruct((tok_rows, channels), jnp.bfloat16),
            jax.ShapeDtypeStruct((tok_rows, channels), jnp.bfloat16),
            jax.ShapeDtypeStruct((steps, 2 * sub, width), jnp.float32),
        ],
        compiler_params=pltpu.CompilerParams(
            dimension_semantics=("arbitrary",), vmem_limit_bytes=48 * 1024 * 1024
        ),
    )(qc, qa, links, *[h for h, _ in halo], query_rows, cotangent, key_rows, value_rows)
    output_rows, grad_query, grad_key, grad_value, diag = outs
    diag = diag.reshape(filters, width)
    top = min(taps_total, base + BLK)
    taps_grad = jnp.flip(diag[:, base + BLK - top : base + BLK], 1)
    if top < taps_total:
        taps_grad = jnp.pad(taps_grad, ((0, 0), (0, taps_total - top)))
    return output_rows, grad_query, grad_key, grad_value, taps_grad


def per_device(value_rows, key_rows, query_rows, cotangent, filter_taps, doc_blocks):
    tok_rows = value_rows.shape[0]
    taps_total = filter_taps.shape[1]
    full_lags = taps_total // BLK + 1
    short_lags = min(MOST, full_lags)
    args = (value_rows, key_rows, query_rows, cotangent, filter_taps, doc_blocks)
    nblk = doc_blocks.shape[0]
    apart = np.abs(np.arange(nblk)[:, None] - np.arange(nblk)[None, :])
    far_pairs = jnp.asarray((apart >= short_lags) & (apart < full_lags))
    same = doc_blocks[:, None] == doc_blocks[None, :]
    long_links = jnp.any(same & far_pairs)
    outs = lax.cond(
        long_links,
        lambda a: convolve_all(*a, full_lags),
        lambda a: convolve_all(*a, short_lags),
        args,
    )
    output_rows, grad_query, grad_key, grad_value, taps_grad = outs
    taps_grad = taps_grad * (1.0 / (tok_rows * lax.axis_size("seq")))
    grad_filter = doubled_total(taps_grad, ("head", "seq"))
    return (output_rows, grad_query, grad_key, grad_value, grad_filter)


def doubled_total(value, axes):
    for axis in axes:
        length = lax.axis_size(axis)
        bits = (length - 1).bit_length()
        for low in range(0, bits, 2):
            group = [1 << low] + ([1 << (low + 1)] if low + 1 < bits else [])
            swap = lambda m: lax.ppermute(value, axis, [(i, i ^ m) for i in range(length)])
            if len(group) == 1:
                value = value + swap(group[0])
            else:
                a, b = group
                value = (value + swap(a)) + (swap(b) + swap(a | b))
    return value


def solution(mesh):
    in_specs = (P("seq", "head"), P("seq", "head"), P("seq", "head"), P("seq", "head"), P(), P())
    out_specs = (P("seq", "head"), P("seq", "head"), P("seq", "head"), P("seq", "head"), P())
    return jax.shard_map(
        per_device, mesh=mesh, in_specs=in_specs, out_specs=out_specs, check_vma=False
    )
```

```python
import numpy as np
import jax
import jax.numpy as jnp
from jax import lax
from jax.experimental import pallas as pl
from jax.experimental.pallas import tpu as pltpu
from jax.sharding import PartitionSpec as P

DH = 64
BLK = 128
MOST = 12


def passed_along(value, axis, by):
    length = lax.axis_size(axis)
    pairs = [(i, i + by) for i in range(length) if 0 <= i + by < length]
    return lax.ppermute(value, axis, pairs)


def shifted_pairs(length, by, parity=None):
    return [
        (i, i + by)
        for i in range(length)
        if 0 <= i + by < length and (parity is None or (i + by) % 2 == parity)
    ]


def halo_pieces(product, scaled, far, part, nb):
    length = lax.axis_size("seq")
    rounds = far // 2
    rows = product.shape[0]
    chain_p, chain_s = [product], [scaled]
    for r in range(rounds):
        chain_p.append(lax.ppermute(chain_p[-1], "seq", shifted_pairs(length, 2)))
        chain_s.append(lax.ppermute(chain_s[-1], "seq", shifted_pairs(length, -2)))
    to_odd = [(i, i + 1) for i in range(0, length, 2)]
    to_even = [(i, i - 1) for i in range(1, length, 2)]
    odd_p, odd_s = [], []
    for k in range(rounds):
        up = jnp.concatenate(lax.optimization_barrier((chain_p[k], chain_s[k + 1])), 1)
        down = jnp.concatenate(lax.optimization_barrier((chain_p[k + 1], chain_s[k])), 1)
        up = lax.ppermute(up, "seq", to_odd)
        down = lax.ppermute(down, "seq", to_even)
        odd_p.append([(up, 0, 0, rows), (down, 0, 0, rows)])
        odd_s.append([(up, 1, 0, rows), (down, 1, 0, rows)])
    p_pieces = [[(chain_p[rounds], 0, (nb - part) * BLK, part * BLK)]]
    for r in range(rounds, 0, -1):
        p_pieces.append(odd_p[r - 1])
        if r > 1:
            p_pieces.append([(chain_p[r - 1], 0, 0, rows)])
    p_pieces.append([(product, 0, 0, rows)])
    s_pieces = [[(scaled, 0, 0, rows)]]
    for r in range(1, rounds + 1):
        s_pieces.append(odd_s[r - 1])
        if r < rounds:
            s_pieces.append([(chain_s[r], 0, 0, rows)])
    s_pieces.append([(chain_s[rounds], 0, 0, part * BLK)])
    return p_pieces, s_pieces


def flatten_pieces(pieces, inputs):
    layout = []
    for piece in pieces:
        terms = []
        for arr, half, start, rows in piece:
            for idx, (known, known_half) in enumerate(inputs):
                if known is arr and known_half == half:
                    break
            else:
                inputs.append((arr, half))
                idx = len(inputs) - 1
            terms.append((idx, start, rows))
        layout.append(terms)
    return layout


def make_kernel(nb, lags, width, span, conv_start, p_layout, s_layout, n_halo, sub):
    def kernel(*refs):
        qc_ref, qa_ref, lk_ref = refs[:3]
        halo = refs[3 : 3 + n_halo]
        q_ref, ct_ref, k_ref, v_ref = refs[3 + n_halo : 7 + n_halo]
        out_ref, gq_ref, gk_ref, gv_ref, gd_ref = refs[7 + n_halo :]
        step = pl.program_id(0)
        lane = lax.broadcasted_iota(jnp.int32, (BLK, BLK), 1)
        lo = lane < DH
        flip = (lane + lax.broadcasted_iota(jnp.int32, (BLK, BLK), 0) == BLK - 1).astype(
            jnp.bfloat16
        )
        pad = jnp.zeros((BLK, BLK), jnp.float32)

        def assemble(layout, cols):
            pieces = []
            for terms in layout:
                total = None
                for idx, start, rows in terms:
                    term = halo[idx][start : start + rows, cols]
                    total = term if total is None else total + term
                pieces.append(total)
            return jnp.concatenate(pieces, 0)

        def masked(window, row):
            blocks = []
            for c in range(lags):
                block = window[c * BLK : (c + 1) * BLK]
                blocks.append(jnp.where(lk_ref[row, c] > 0, block, jnp.zeros_like(block)))
            return jnp.concatenate(blocks, 0)

        def table(ref, f, shift):
            row = ref[pl.ds(f, 1), :]
            full = jnp.broadcast_to(row, (BLK, span))
            rolled = pltpu.roll(full, shift, 1, stride=1, stride_axis=0)
            return rolled[:, :width]

        def diagonals(half):
            wide = jnp.concatenate([half, pad], 1)
            rolled = pltpu.roll(wide, 0, 1, stride=1, stride_axis=0)
            return rolled[:, :width].sum(0, keepdims=True)

        for j in range(sub):
            cols = slice(j * BLK, (j + 1) * BLK)
            f0 = 2 * (sub * step + j)
            pext = assemble(p_layout, cols)
            sext = assemble(s_layout, cols)
            tc = jnp.concatenate(
                [table(qc_ref, f0, span - (BLK - 1)), table(qc_ref, f0 + 1, span - (BLK - 1))], 0
            ).astype(jnp.bfloat16)
            ta = jnp.concatenate(
                [table(qa_ref, f0, span - BLK), table(qa_ref, f0 + 1, span - BLK)], 0
            ).astype(jnp.bfloat16)
            gsum = jnp.zeros((2 * BLK, width), jnp.float32)
            for n in range(nb):
                rows = pl.ds(n * BLK, BLK)
                lanes_j = pl.ds(j * BLK, BLK)
                pw = masked(pext[conv_start + n * BLK : conv_start + n * BLK + width], n)
                sw = masked(sext[n * BLK : n * BLK + width], nb + n)
                conv2 = jnp.dot(tc, pw, preferred_element_type=jnp.float32)
                conv = jnp.where(lo, conv2[:BLK], conv2[BLK:])
                adj2 = jnp.dot(ta, sw, preferred_element_type=jnp.float32)
                adj = jnp.where(lo, adj2[:BLK], adj2[BLK:])
                q = q_ref[rows, lanes_j].astype(jnp.float32)
                out_ref[rows, lanes_j] = (q * conv).astype(jnp.bfloat16)
                ct = ct_ref[rows, lanes_j].astype(jnp.float32)
                gq_ref[rows, lanes_j] = (ct * conv).astype(jnp.bfloat16)
                v = v_ref[rows, lanes_j].astype(jnp.float32)
                gk_ref[rows, lanes_j] = (adj * v).astype(jnp.bfloat16)
                k = k_ref[rows, lanes_j].astype(jnp.float32)
                gv_ref[rows, lanes_j] = (adj * k).astype(jnp.bfloat16)
                sr = jnp.dot(
                    flip, sext[n * BLK : (n + 1) * BLK], preferred_element_type=jnp.float32
                ).astype(jnp.bfloat16)
                zero = jnp.zeros_like(sr)
                a = jnp.concatenate([jnp.where(lo, sr, zero), jnp.where(lo, zero, sr)], 0)
                gsum = gsum + lax.dot_general(
                    a, pw, (((1,), (1,)), ((), ())), preferred_element_type=jnp.float32
                )
            gd_ref[0, 2 * j : 2 * j + 2, :] = jnp.concatenate(
                [diagonals(gsum[:BLK]), diagonals(gsum[BLK:])], 0
            )

    return kernel


def convolve_all(value_rows, key_rows, query_rows, cotangent, filter_taps, doc_blocks, lags):
    tok_rows, channels = value_rows.shape
    filters, taps_total = filter_taps.shape
    nb = tok_rows // BLK
    width = lags * BLK
    span = width + BLK
    base = (lags - 1) * BLK
    sub = 2
    steps = channels // (BLK * sub)
    far = -(-(lags - 1) // nb)
    part = (lags - 1) - (far - 1) * nb
    product = (key_rows.astype(jnp.float32) * value_rows.astype(jnp.float32)).astype(jnp.bfloat16)
    scaled = (cotangent.astype(jnp.float32) * query_rows.astype(jnp.float32)).astype(jnp.bfloat16)
    halo = []
    p_pieces, s_pieces = halo_pieces(product, scaled, far, part, nb)
    p_layout = flatten_pieces(p_pieces, halo)
    s_layout = flatten_pieces(s_pieces, halo)
    conv_start = 0

    rounded = filter_taps.astype(jnp.bfloat16).astype(jnp.float32)
    kept = min(taps_total, span - BLK)
    qa = jnp.pad(rounded[:, :kept], ((0, 0), (BLK, span - BLK - kept)))
    qc = jnp.flip(qa, 1)

    margin = lags + nb
    padded = jnp.concatenate(
        [jnp.full((margin,), -1, jnp.int32), doc_blocks, jnp.full((margin,), -2, jnp.int32)], 0
    )
    shard = lax.axis_index("seq")
    window = lax.dynamic_slice_in_dim(padded, shard * nb + margin - (lags - 1), 2 * (lags - 1) + nb)
    own = jnp.stack([window[lags - 1 + n] for n in range(nb)])
    conv_docs = jnp.stack([window[n : n + lags] for n in range(nb)])
    adj_docs = jnp.stack([window[lags - 1 + n : lags - 1 + n + lags] for n in range(nb)])
    links = jnp.concatenate([conv_docs == own[:, None], adj_docs == own[:, None]], 0)
    links = links.astype(jnp.int32)

    whole = lambda shape: pl.BlockSpec(shape, lambda s: (0, 0))
    lanes = lambda r: pl.BlockSpec((r, BLK * sub), lambda s: (0, s))
    kernel = make_kernel(
        nb, lags, width, span, conv_start, p_layout, s_layout, len(halo), sub
    )
    outs = pl.pallas_call(
        kernel,
        grid=(steps,),
        in_specs=[
            whole((filters, span)),
            whole((filters, span)),
            pl.BlockSpec(memory_space=pltpu.SMEM),
            *[
                pl.BlockSpec((h.shape[0], BLK * sub), lambda s, o=half * steps: (0, s + o))
                for h, half in halo
            ],
            lanes(tok_rows),
            lanes(tok_rows),
            lanes(tok_rows),
            lanes(tok_rows),
        ],
        out_specs=[
            lanes(tok_rows),
            lanes(tok_rows),
            lanes(tok_rows),
            lanes(tok_rows),
            pl.BlockSpec((1, 2 * sub, width), lambda s: (s, 0, 0)),
        ],
        out_shape=[
            jax.ShapeDtypeStruct((tok_rows, channels), jnp.bfloat16),
            jax.ShapeDtypeStruct((tok_rows, channels), jnp.bfloat16),
            jax.ShapeDtypeStruct((tok_rows, channels), jnp.bfloat16),
            jax.ShapeDtypeStruct((tok_rows, channels), jnp.bfloat16),
            jax.ShapeDtypeStruct((steps, 2 * sub, width), jnp.float32),
        ],
        compiler_params=pltpu.CompilerParams(
            dimension_semantics=("arbitrary",), vmem_limit_bytes=48 * 1024 * 1024
        ),
    )(qc, qa, links, *[h for h, _ in halo], query_rows, cotangent, key_rows, value_rows)
    output_rows, grad_query, grad_key, grad_value, diag = outs
    diag = diag.reshape(filters, width)
    top = min(taps_total, base + BLK)
    taps_grad = jnp.flip(diag[:, base + BLK - top : base + BLK], 1)
    if top < taps_total:
        taps_grad = jnp.pad(taps_grad, ((0, 0), (0, taps_total - top)))
    return output_rows, grad_query, grad_key, grad_value, taps_grad


def per_device(value_rows, key_rows, query_rows, cotangent, filter_taps, doc_blocks):
    tok_rows = value_rows.shape[0]
    taps_total = filter_taps.shape[1]
    full_lags = taps_total // BLK + 1
    short_lags = min(MOST, full_lags)
    args = (value_rows, key_rows, query_rows, cotangent, filter_taps, doc_blocks)
    nblk = doc_blocks.shape[0]
    apart = np.abs(np.arange(nblk)[:, None] - np.arange(nblk)[None, :])
    far_pairs = jnp.asarray((apart >= short_lags) & (apart < full_lags))
    same = doc_blocks[:, None] == doc_blocks[None, :]
    long_links = jnp.any(same & far_pairs)
    outs = lax.cond(
        long_links,
        lambda a: convolve_all(*a, full_lags),
        lambda a: convolve_all(*a, short_lags),
        args,
    )
    output_rows, grad_query, grad_key, grad_value, taps_grad = outs
    taps_grad = taps_grad * (1.0 / (tok_rows * lax.axis_size("seq")))
    grad_filter = doubled_total(taps_grad, ("head", "seq"))
    return (output_rows, grad_query, grad_key, grad_value, grad_filter)


def doubled_total(value, axes):
    for axis in axes:
        length = lax.axis_size(axis)
        bits = (length - 1).bit_length()
        for low in range(0, bits, 2):
            group = [1 << low] + ([1 << (low + 1)] if low + 1 < bits else [])
            swap = lambda m: lax.ppermute(value, axis, [(i, i ^ m) for i in range(length)])
            if len(group) == 1:
                value = value + swap(group[0])
            else:
                a, b = group
                value = (value + swap(a)) + (swap(b) + swap(a | b))
    return value


def solution(mesh):
    in_specs = (P("seq", "head"), P("seq", "head"), P("seq", "head"), P("seq", "head"), P(), P())
    out_specs = (P("seq", "head"), P("seq", "head"), P("seq", "head"), P("seq", "head"), P())
    return jax.shard_map(
        per_device, mesh=mesh, in_specs=in_specs, out_specs=out_specs, check_vma=False
    )
```

```python
import numpy as np
import jax
import jax.numpy as jnp
from jax import lax
from jax.experimental import pallas as pl
from jax.experimental.pallas import tpu as pltpu
from jax.sharding import PartitionSpec as P

DH = 64
BLK = 128
MOST = 12


def passed_along(value, axis, by):
    length = lax.axis_size(axis)
    pairs = [(i, i + by) for i in range(length) if 0 <= i + by < length]
    return lax.ppermute(value, axis, pairs)


def shifted_pairs(length, by, parity=None):
    return [
        (i, i + by)
        for i in range(length)
        if 0 <= i + by < length and (parity is None or (i + by) % 2 == parity)
    ]


def halo_pieces(product, scaled, far, part, nb):
    length = lax.axis_size("seq")
    rounds = far // 2
    rows = product.shape[0]
    chain_p, chain_s = [product], [scaled]
    for r in range(rounds):
        chain_p.append(lax.ppermute(chain_p[-1], "seq", shifted_pairs(length, 2)))
        chain_s.append(lax.ppermute(chain_s[-1], "seq", shifted_pairs(length, -2)))
    to_odd = [(i, i + 1) for i in range(0, length, 2)]
    to_even = [(i, i - 1) for i in range(1, length, 2)]
    odd_p, odd_s = [], []
    for k in range(rounds):
        up = jnp.concatenate(lax.optimization_barrier((chain_p[k], chain_s[k + 1])), 1)
        down = jnp.concatenate(lax.optimization_barrier((chain_p[k + 1], chain_s[k])), 1)
        up = lax.ppermute(up, "seq", to_odd)
        down = lax.ppermute(down, "seq", to_even)
        odd_p.append([(up, 0, 0, rows), (down, 0, 0, rows)])
        odd_s.append([(up, 1, 0, rows), (down, 1, 0, rows)])
    p_pieces = [[(chain_p[rounds], 0, (nb - part) * BLK, part * BLK)]]
    for r in range(rounds, 0, -1):
        p_pieces.append(odd_p[r - 1])
        if r > 1:
            p_pieces.append([(chain_p[r - 1], 0, 0, rows)])
    p_pieces.append([(product, 0, 0, rows)])
    s_pieces = [[(scaled, 0, 0, rows)]]
    for r in range(1, rounds + 1):
        s_pieces.append(odd_s[r - 1])
        if r < rounds:
            s_pieces.append([(chain_s[r], 0, 0, rows)])
    s_pieces.append([(chain_s[rounds], 0, 0, part * BLK)])
    return p_pieces, s_pieces


def flatten_pieces(pieces, inputs):
    layout = []
    for piece in pieces:
        terms = []
        for arr, half, start, rows in piece:
            for idx, (known, known_half) in enumerate(inputs):
                if known is arr and known_half == half:
                    break
            else:
                inputs.append((arr, half))
                idx = len(inputs) - 1
            terms.append((idx, start, rows))
        layout.append(terms)
    return layout


def make_kernel(nb, lags, width, span, conv_start, p_layout, s_layout, n_halo, sub):
    def kernel(*refs):
        qc_ref, qa_ref, lk_ref = refs[:3]
        halo = refs[3 : 3 + n_halo]
        q_ref, ct_ref, k_ref, v_ref = refs[3 + n_halo : 7 + n_halo]
        out_ref, gq_ref, gk_ref, gv_ref, gd_ref = refs[7 + n_halo :]
        step = pl.program_id(0)
        lane = lax.broadcasted_iota(jnp.int32, (BLK, BLK), 1)
        lo = lane < DH
        flip = (lane + lax.broadcasted_iota(jnp.int32, (BLK, BLK), 0) == BLK - 1).astype(
            jnp.bfloat16
        )
        pad = jnp.zeros((BLK, BLK), jnp.float32)

        def assemble(layout, cols):
            pieces = []
            for terms in layout:
                total = None
                for idx, start, rows in terms:
                    term = halo[idx][start : start + rows, cols]
                    total = term if total is None else total + term
                pieces.append(total)
            return jnp.concatenate(pieces, 0)

        def masked(window, row):
            blocks = []
            for c in range(lags):
                block = window[c * BLK : (c + 1) * BLK]
                blocks.append(jnp.where(lk_ref[row, c] > 0, block, jnp.zeros_like(block)))
            return jnp.concatenate(blocks, 0)

        def table(ref, f, shift):
            row = ref[pl.ds(f, 1), :]
            full = jnp.broadcast_to(row, (BLK, span))
            rolled = pltpu.roll(full, shift, 1, stride=1, stride_axis=0)
            return rolled[:, :width]

        def diagonals(half):
            wide = jnp.concatenate([half, pad], 1)
            rolled = pltpu.roll(wide, 0, 1, stride=1, stride_axis=0)
            return rolled[:, :width].sum(0, keepdims=True)

        for j in range(sub):
            cols = slice(j * BLK, (j + 1) * BLK)
            f0 = 2 * (sub * step + j)
            pext = assemble(p_layout, cols)
            sext = assemble(s_layout, cols)
            tc = jnp.concatenate(
                [table(qc_ref, f0, span - (BLK - 1)), table(qc_ref, f0 + 1, span - (BLK - 1))], 0
            ).astype(jnp.bfloat16)
            ta = jnp.concatenate(
                [table(qa_ref, f0, span - BLK), table(qa_ref, f0 + 1, span - BLK)], 0
            ).astype(jnp.bfloat16)
            gsum = jnp.zeros((2 * BLK, width), jnp.float32)
            for n in range(nb):
                rows = pl.ds(n * BLK, BLK)
                lanes_j = pl.ds(j * BLK, BLK)
                pw = masked(pext[conv_start + n * BLK : conv_start + n * BLK + width], n)
                sw = masked(sext[n * BLK : n * BLK + width], nb + n)
                conv2 = jnp.dot(tc, pw, preferred_element_type=jnp.float32)
                conv = jnp.where(lo, conv2[:BLK], conv2[BLK:])
                adj2 = jnp.dot(ta, sw, preferred_element_type=jnp.float32)
                adj = jnp.where(lo, adj2[:BLK], adj2[BLK:])
                q = q_ref[rows, lanes_j].astype(jnp.float32)
                out_ref[rows, lanes_j] = (q * conv).astype(jnp.bfloat16)
                ct = ct_ref[rows, lanes_j].astype(jnp.float32)
                gq_ref[rows, lanes_j] = (ct * conv).astype(jnp.bfloat16)
                v = v_ref[rows, lanes_j].astype(jnp.float32)
                gk_ref[rows, lanes_j] = (adj * v).astype(jnp.bfloat16)
                k = k_ref[rows, lanes_j].astype(jnp.float32)
                gv_ref[rows, lanes_j] = (adj * k).astype(jnp.bfloat16)
                sr = jnp.dot(
                    flip, sext[n * BLK : (n + 1) * BLK], preferred_element_type=jnp.float32
                ).astype(jnp.bfloat16)
                zero = jnp.zeros_like(sr)
                a = jnp.concatenate([jnp.where(lo, sr, zero), jnp.where(lo, zero, sr)], 0)
                gsum = gsum + lax.dot_general(
                    a, pw, (((1,), (1,)), ((), ())), preferred_element_type=jnp.float32
                )
            gd_ref[0, 2 * j : 2 * j + 2, :] = jnp.concatenate(
                [diagonals(gsum[:BLK]), diagonals(gsum[BLK:])], 0
            )

    return kernel


def convolve_all(value_rows, key_rows, query_rows, cotangent, filter_taps, doc_blocks, lags):
    tok_rows, channels = value_rows.shape
    filters, taps_total = filter_taps.shape
    nb = tok_rows // BLK
    width = lags * BLK
    span = width + BLK
    base = (lags - 1) * BLK
    sub = 2
    steps = channels // (BLK * sub)
    far = -(-(lags - 1) // nb)
    part = (lags - 1) - (far - 1) * nb
    product = (key_rows.astype(jnp.float32) * value_rows.astype(jnp.float32)).astype(jnp.bfloat16)
    scaled = (cotangent.astype(jnp.float32) * query_rows.astype(jnp.float32)).astype(jnp.bfloat16)
    halo = []
    p_pieces, s_pieces = halo_pieces(product, scaled, far, part, nb)
    p_layout = flatten_pieces(p_pieces, halo)
    s_layout = flatten_pieces(s_pieces, halo)
    conv_start = 0

    rounded = filter_taps.astype(jnp.bfloat16).astype(jnp.float32)
    kept = min(taps_total, span - BLK)
    qa = jnp.pad(rounded[:, :kept], ((0, 0), (BLK, span - BLK - kept)))
    qc = jnp.flip(qa, 1)

    margin = lags + nb
    padded = jnp.concatenate(
        [jnp.full((margin,), -1, jnp.int32), doc_blocks, jnp.full((margin,), -2, jnp.int32)], 0
    )
    shard = lax.axis_index("seq")
    window = lax.dynamic_slice_in_dim(padded, shard * nb + margin - (lags - 1), 2 * (lags - 1) + nb)
    own = jnp.stack([window[lags - 1 + n] for n in range(nb)])
    conv_docs = jnp.stack([window[n : n + lags] for n in range(nb)])
    adj_docs = jnp.stack([window[lags - 1 + n : lags - 1 + n + lags] for n in range(nb)])
    links = jnp.concatenate([conv_docs == own[:, None], adj_docs == own[:, None]], 0)
    links = links.astype(jnp.int32)

    whole = lambda shape: pl.BlockSpec(shape, lambda s: (0, 0))
    lanes = lambda r: pl.BlockSpec((r, BLK * sub), lambda s: (0, s))
    kernel = make_kernel(
        nb, lags, width, span, conv_start, p_layout, s_layout, len(halo), sub
    )
    outs = pl.pallas_call(
        kernel,
        grid=(steps,),
        in_specs=[
            whole((filters, span)),
            whole((filters, span)),
            pl.BlockSpec(memory_space=pltpu.SMEM),
            *[
                pl.BlockSpec((h.shape[0], BLK * sub), lambda s, o=half * steps: (0, s + o))
                for h, half in halo
            ],
            lanes(tok_rows),
            lanes(tok_rows),
            lanes(tok_rows),
            lanes(tok_rows),
        ],
        out_specs=[
            lanes(tok_rows),
            lanes(tok_rows),
            lanes(tok_rows),
            lanes(tok_rows),
            pl.BlockSpec((1, 2 * sub, width), lambda s: (s, 0, 0)),
        ],
        out_shape=[
            jax.ShapeDtypeStruct((tok_rows, channels), jnp.bfloat16),
            jax.ShapeDtypeStruct((tok_rows, channels), jnp.bfloat16),
            jax.ShapeDtypeStruct((tok_rows, channels), jnp.bfloat16),
            jax.ShapeDtypeStruct((tok_rows, channels), jnp.bfloat16),
            jax.ShapeDtypeStruct((steps, 2 * sub, width), jnp.float32),
        ],
        compiler_params=pltpu.CompilerParams(
            dimension_semantics=("arbitrary",), vmem_limit_bytes=48 * 1024 * 1024
        ),
    )(qc, qa, links, *[h for h, _ in halo], query_rows, cotangent, key_rows, value_rows)
    output_rows, grad_query, grad_key, grad_value, diag = outs
    diag = diag.reshape(filters, width)
    top = min(taps_total, base + BLK)
    taps_grad = jnp.flip(diag[:, base + BLK - top : base + BLK], 1)
    taps_grad = taps_grad * (1.0 / (tok_rows * lax.axis_size("seq")))
    grad_filter = doubled_total(taps_grad, ("head", "seq"))
    if top < taps_total:
        grad_filter = jnp.pad(grad_filter, ((0, 0), (0, taps_total - top)))
    return output_rows, grad_query, grad_key, grad_value, grad_filter


def per_device(value_rows, key_rows, query_rows, cotangent, filter_taps, doc_blocks):
    tok_rows = value_rows.shape[0]
    taps_total = filter_taps.shape[1]
    full_lags = taps_total // BLK + 1
    short_lags = min(MOST, full_lags)
    args = (value_rows, key_rows, query_rows, cotangent, filter_taps, doc_blocks)
    nblk = doc_blocks.shape[0]
    apart = np.abs(np.arange(nblk)[:, None] - np.arange(nblk)[None, :])
    far_pairs = jnp.asarray((apart >= short_lags) & (apart < full_lags))
    same = doc_blocks[:, None] == doc_blocks[None, :]
    long_links = jnp.any(same & far_pairs)
    outs = lax.cond(
        long_links,
        lambda a: convolve_all(*a, full_lags),
        lambda a: convolve_all(*a, short_lags),
        args,
    )
    return tuple(outs)


def doubled_total(value, axes):
    for axis in axes:
        length = lax.axis_size(axis)
        bits = (length - 1).bit_length()
        for low in range(0, bits, 2):
            group = [1 << low] + ([1 << (low + 1)] if low + 1 < bits else [])
            swap = lambda m: lax.ppermute(value, axis, [(i, i ^ m) for i in range(length)])
            if len(group) == 1:
                value = value + swap(group[0])
            else:
                a, b = group
                value = (value + swap(a)) + (swap(b) + swap(a | b))
    return value


def solution(mesh):
    in_specs = (P("seq", "head"), P("seq", "head"), P("seq", "head"), P("seq", "head"), P(), P())
    out_specs = (P("seq", "head"), P("seq", "head"), P("seq", "head"), P("seq", "head"), P())
    return jax.shard_map(
        per_device, mesh=mesh, in_specs=in_specs, out_specs=out_specs, check_vma=False
    )
```

```python
import numpy as np
import jax
import jax.numpy as jnp
from jax import lax
from jax.experimental import pallas as pl
from jax.experimental.pallas import tpu as pltpu
from jax.sharding import PartitionSpec as P

DH = 64
BLK = 128
MOST = 12


def passed_along(value, axis, by):
    length = lax.axis_size(axis)
    pairs = [(i, i + by) for i in range(length) if 0 <= i + by < length]
    return lax.ppermute(value, axis, pairs)


def shifted_pairs(length, by, parity=None):
    return [
        (i, i + by)
        for i in range(length)
        if 0 <= i + by < length and (parity is None or (i + by) % 2 == parity)
    ]


def halo_pieces(product, scaled, far, part, nb):
    length = lax.axis_size("seq")
    rounds = far // 2
    rows = product.shape[0]
    chain_p, chain_s = [product], [scaled]
    for r in range(rounds):
        chain_p.append(lax.ppermute(chain_p[-1], "seq", shifted_pairs(length, 2)))
        chain_s.append(lax.ppermute(chain_s[-1], "seq", shifted_pairs(length, -2)))
    to_odd = [(i, i + 1) for i in range(0, length, 2)]
    to_even = [(i, i - 1) for i in range(1, length, 2)]
    odd_p, odd_s = [], []
    for k in range(rounds):
        up = jnp.concatenate(lax.optimization_barrier((chain_p[k], chain_s[k + 1])), 1)
        down = jnp.concatenate(lax.optimization_barrier((chain_p[k + 1], chain_s[k])), 1)
        up = lax.ppermute(up, "seq", to_odd)
        down = lax.ppermute(down, "seq", to_even)
        odd_p.append([(up, 0, 0, rows), (down, 0, 0, rows)])
        odd_s.append([(up, 1, 0, rows), (down, 1, 0, rows)])
    p_pieces = [[(chain_p[rounds], 0, (nb - part) * BLK, part * BLK)]]
    for r in range(rounds, 0, -1):
        p_pieces.append(odd_p[r - 1])
        if r > 1:
            p_pieces.append([(chain_p[r - 1], 0, 0, rows)])
    p_pieces.append([(product, 0, 0, rows)])
    s_pieces = [[(scaled, 0, 0, rows)]]
    for r in range(1, rounds + 1):
        s_pieces.append(odd_s[r - 1])
        if r < rounds:
            s_pieces.append([(chain_s[r], 0, 0, rows)])
    s_pieces.append([(chain_s[rounds], 0, 0, part * BLK)])
    return p_pieces, s_pieces


def flatten_pieces(pieces, inputs):
    layout = []
    for piece in pieces:
        terms = []
        for arr, half, start, rows in piece:
            for idx, (known, known_half) in enumerate(inputs):
                if known is arr and known_half == half:
                    break
            else:
                inputs.append((arr, half))
                idx = len(inputs) - 1
            terms.append((idx, start, rows))
        layout.append(terms)
    return layout


def make_kernel(nb, lags, width, span, conv_start, p_layout, s_layout, n_halo, sub):
    def kernel(*refs):
        qc_ref, qa_ref, lk_ref = refs[:3]
        halo = refs[3 : 3 + n_halo]
        q_ref, ct_ref, k_ref, v_ref = refs[3 + n_halo : 7 + n_halo]
        out_ref, gq_ref, gk_ref, gv_ref, gd_ref = refs[7 + n_halo :]
        step = pl.program_id(0)
        lane = lax.broadcasted_iota(jnp.int32, (BLK, BLK), 1)
        lo = lane < DH
        flip = (lane + lax.broadcasted_iota(jnp.int32, (BLK, BLK), 0) == BLK - 1).astype(
            jnp.bfloat16
        )
        pad = jnp.zeros((BLK, BLK), jnp.float32)

        def assemble(layout, cols):
            pieces = []
            for terms in layout:
                total = None
                for idx, start, rows in terms:
                    term = halo[idx][start : start + rows, cols]
                    total = term if total is None else total + term
                pieces.append(total)
            return jnp.concatenate(pieces, 0)

        def masked(window, row):
            blocks = []
            for c in range(lags):
                block = window[c * BLK : (c + 1) * BLK]
                blocks.append(jnp.where(lk_ref[row, c] > 0, block, jnp.zeros_like(block)))
            return jnp.concatenate(blocks, 0)

        def table(ref, f, shift):
            row = ref[pl.ds(f, 1), :]
            full = jnp.broadcast_to(row, (BLK, span))
            rolled = pltpu.roll(full, shift, 1, stride=1, stride_axis=0)
            return rolled[:, :width]

        def diagonals(half):
            wide = jnp.concatenate([half, pad], 1)
            rolled = pltpu.roll(wide, 0, 1, stride=1, stride_axis=0)
            return rolled[:, :width].sum(0, keepdims=True)

        for j in range(sub):
            cols = slice(j * BLK, (j + 1) * BLK)
            f0 = 2 * (sub * step + j)
            pext = assemble(p_layout, cols)
            sext = assemble(s_layout, cols)
            tc = jnp.concatenate(
                [table(qc_ref, f0, span - (BLK - 1)), table(qc_ref, f0 + 1, span - (BLK - 1))], 0
            ).astype(jnp.bfloat16)
            ta = jnp.concatenate(
                [table(qa_ref, f0, span - BLK), table(qa_ref, f0 + 1, span - BLK)], 0
            ).astype(jnp.bfloat16)
            gsum = jnp.zeros((2 * BLK, width), jnp.float32)
            for n in range(nb):
                rows = pl.ds(n * BLK, BLK)
                lanes_j = pl.ds(j * BLK, BLK)
                pw = masked(pext[conv_start + n * BLK : conv_start + n * BLK + width], n)
                sw = masked(sext[n * BLK : n * BLK + width], nb + n)
                conv2 = jnp.dot(tc, pw, preferred_element_type=jnp.float32)
                conv = jnp.where(lo, conv2[:BLK], conv2[BLK:])
                adj2 = jnp.dot(ta, sw, preferred_element_type=jnp.float32)
                adj = jnp.where(lo, adj2[:BLK], adj2[BLK:])
                q = q_ref[rows, lanes_j].astype(jnp.float32)
                out_ref[rows, lanes_j] = (q * conv).astype(jnp.bfloat16)
                ct = ct_ref[rows, lanes_j].astype(jnp.float32)
                gq_ref[rows, lanes_j] = (ct * conv).astype(jnp.bfloat16)
                v = v_ref[rows, lanes_j].astype(jnp.float32)
                gk_ref[rows, lanes_j] = (adj * v).astype(jnp.bfloat16)
                k = k_ref[rows, lanes_j].astype(jnp.float32)
                gv_ref[rows, lanes_j] = (adj * k).astype(jnp.bfloat16)
                sr = jnp.dot(
                    flip, sext[n * BLK : (n + 1) * BLK], preferred_element_type=jnp.float32
                ).astype(jnp.bfloat16)
                zero = jnp.zeros_like(sr)
                a = jnp.concatenate([jnp.where(lo, sr, zero), jnp.where(lo, zero, sr)], 0)
                gsum = gsum + lax.dot_general(
                    a, pw, (((1,), (1,)), ((), ())), preferred_element_type=jnp.float32
                )
            gd_ref[0, 2 * j : 2 * j + 2, :] = jnp.concatenate(
                [diagonals(gsum[:BLK]), diagonals(gsum[BLK:])], 0
            )

    return kernel


def convolve_all(value_rows, key_rows, query_rows, cotangent, filter_taps, doc_blocks, lags):
    tok_rows, channels = value_rows.shape
    filters, taps_total = filter_taps.shape
    nb = tok_rows // BLK
    width = lags * BLK
    span = width + BLK
    base = (lags - 1) * BLK
    sub = 4
    steps = channels // (BLK * sub)
    far = -(-(lags - 1) // nb)
    part = (lags - 1) - (far - 1) * nb
    product = (key_rows.astype(jnp.float32) * value_rows.astype(jnp.float32)).astype(jnp.bfloat16)
    scaled = (cotangent.astype(jnp.float32) * query_rows.astype(jnp.float32)).astype(jnp.bfloat16)
    halo = []
    p_pieces, s_pieces = halo_pieces(product, scaled, far, part, nb)
    p_layout = flatten_pieces(p_pieces, halo)
    s_layout = flatten_pieces(s_pieces, halo)
    conv_start = 0

    rounded = filter_taps.astype(jnp.bfloat16).astype(jnp.float32)
    kept = min(taps_total, span - BLK)
    qa = jnp.pad(rounded[:, :kept], ((0, 0), (BLK, span - BLK - kept)))
    qc = jnp.flip(qa, 1)

    margin = lags + nb
    padded = jnp.concatenate(
        [jnp.full((margin,), -1, jnp.int32), doc_blocks, jnp.full((margin,), -2, jnp.int32)], 0
    )
    shard = lax.axis_index("seq")
    window = lax.dynamic_slice_in_dim(padded, shard * nb + margin - (lags - 1), 2 * (lags - 1) + nb)
    own = jnp.stack([window[lags - 1 + n] for n in range(nb)])
    conv_docs = jnp.stack([window[n : n + lags] for n in range(nb)])
    adj_docs = jnp.stack([window[lags - 1 + n : lags - 1 + n + lags] for n in range(nb)])
    links = jnp.concatenate([conv_docs == own[:, None], adj_docs == own[:, None]], 0)
    links = links.astype(jnp.int32)

    whole = lambda shape: pl.BlockSpec(shape, lambda s: (0, 0))
    lanes = lambda r: pl.BlockSpec((r, BLK * sub), lambda s: (0, s))
    kernel = make_kernel(
        nb, lags, width, span, conv_start, p_layout, s_layout, len(halo), sub
    )
    outs = pl.pallas_call(
        kernel,
        grid=(steps,),
        in_specs=[
            whole((filters, span)),
            whole((filters, span)),
            pl.BlockSpec(memory_space=pltpu.SMEM),
            *[
                pl.BlockSpec((h.shape[0], BLK * sub), lambda s, o=half * steps: (0, s + o))
                for h, half in halo
            ],
            lanes(tok_rows),
            lanes(tok_rows),
            lanes(tok_rows),
            lanes(tok_rows),
        ],
        out_specs=[
            lanes(tok_rows),
            lanes(tok_rows),
            lanes(tok_rows),
            lanes(tok_rows),
            pl.BlockSpec((1, 2 * sub, width), lambda s: (s, 0, 0)),
        ],
        out_shape=[
            jax.ShapeDtypeStruct((tok_rows, channels), jnp.bfloat16),
            jax.ShapeDtypeStruct((tok_rows, channels), jnp.bfloat16),
            jax.ShapeDtypeStruct((tok_rows, channels), jnp.bfloat16),
            jax.ShapeDtypeStruct((tok_rows, channels), jnp.bfloat16),
            jax.ShapeDtypeStruct((steps, 2 * sub, width), jnp.float32),
        ],
        compiler_params=pltpu.CompilerParams(
            dimension_semantics=("arbitrary",), vmem_limit_bytes=48 * 1024 * 1024
        ),
    )(qc, qa, links, *[h for h, _ in halo], query_rows, cotangent, key_rows, value_rows)
    output_rows, grad_query, grad_key, grad_value, diag = outs
    diag = diag.reshape(filters, width)
    top = min(taps_total, base + BLK)
    taps_grad = jnp.flip(diag[:, base + BLK - top : base + BLK], 1)
    taps_grad = taps_grad * (1.0 / (tok_rows * lax.axis_size("seq")))
    grad_filter = doubled_total(taps_grad, ("head", "seq"))
    if top < taps_total:
        grad_filter = jnp.pad(grad_filter, ((0, 0), (0, taps_total - top)))
    return output_rows, grad_query, grad_key, grad_value, grad_filter


def per_device(value_rows, key_rows, query_rows, cotangent, filter_taps, doc_blocks):
    tok_rows = value_rows.shape[0]
    taps_total = filter_taps.shape[1]
    full_lags = taps_total // BLK + 1
    short_lags = min(MOST, full_lags)
    args = (value_rows, key_rows, query_rows, cotangent, filter_taps, doc_blocks)
    nblk = doc_blocks.shape[0]
    apart = np.abs(np.arange(nblk)[:, None] - np.arange(nblk)[None, :])
    far_pairs = jnp.asarray((apart >= short_lags) & (apart < full_lags))
    same = doc_blocks[:, None] == doc_blocks[None, :]
    long_links = jnp.any(same & far_pairs)
    outs = lax.cond(
        long_links,
        lambda a: convolve_all(*a, full_lags),
        lambda a: convolve_all(*a, short_lags),
        args,
    )
    return tuple(outs)


def doubled_total(value, axes):
    for axis in axes:
        length = lax.axis_size(axis)
        bits = (length - 1).bit_length()
        for low in range(0, bits, 2):
            group = [1 << low] + ([1 << (low + 1)] if low + 1 < bits else [])
            swap = lambda m: lax.ppermute(value, axis, [(i, i ^ m) for i in range(length)])
            if len(group) == 1:
                value = value + swap(group[0])
            else:
                a, b = group
                value = (value + swap(a)) + (swap(b) + swap(a | b))
    return value


def solution(mesh):
    in_specs = (P("seq", "head"), P("seq", "head"), P("seq", "head"), P("seq", "head"), P(), P())
    out_specs = (P("seq", "head"), P("seq", "head"), P("seq", "head"), P("seq", "head"), P())
    return jax.shard_map(
        per_device, mesh=mesh, in_specs=in_specs, out_specs=out_specs, check_vma=False
    )
```

```python
import numpy as np
import jax
import jax.numpy as jnp
from jax import lax
from jax.experimental import pallas as pl
from jax.experimental.pallas import tpu as pltpu
from jax.sharding import PartitionSpec as P

DH = 64
BLK = 128
MOST = 12


def passed_along(value, axis, by):
    length = lax.axis_size(axis)
    pairs = [(i, i + by) for i in range(length) if 0 <= i + by < length]
    return lax.ppermute(value, axis, pairs)


def shifted_pairs(length, by, parity=None):
    return [
        (i, i + by)
        for i in range(length)
        if 0 <= i + by < length and (parity is None or (i + by) % 2 == parity)
    ]


def halo_pieces(product, scaled, far, part, nb):
    length = lax.axis_size("seq")
    rounds = far // 2
    rows = product.shape[0]
    chain_p, chain_s = [product], [scaled]
    for r in range(rounds):
        chain_p.append(lax.ppermute(chain_p[-1], "seq", shifted_pairs(length, 2)))
        chain_s.append(lax.ppermute(chain_s[-1], "seq", shifted_pairs(length, -2)))
    to_odd = [(i, i + 1) for i in range(0, length, 2)]
    to_even = [(i, i - 1) for i in range(1, length, 2)]
    odd_p, odd_s = [], []
    for k in range(rounds):
        up = jnp.concatenate(lax.optimization_barrier((chain_p[k], chain_s[k + 1])), 1)
        down = jnp.concatenate(lax.optimization_barrier((chain_p[k + 1], chain_s[k])), 1)
        up = lax.ppermute(up, "seq", to_odd)
        down = lax.ppermute(down, "seq", to_even)
        odd_p.append([(up, 0, 0, rows), (down, 0, 0, rows)])
        odd_s.append([(up, 1, 0, rows), (down, 1, 0, rows)])
    p_pieces = [[(chain_p[rounds], 0, (nb - part) * BLK, part * BLK)]]
    for r in range(rounds, 0, -1):
        p_pieces.append(odd_p[r - 1])
        if r > 1:
            p_pieces.append([(chain_p[r - 1], 0, 0, rows)])
    p_pieces.append([(product, 0, 0, rows)])
    s_pieces = [[(scaled, 0, 0, rows)]]
    for r in range(1, rounds + 1):
        s_pieces.append(odd_s[r - 1])
        if r < rounds:
            s_pieces.append([(chain_s[r], 0, 0, rows)])
    s_pieces.append([(chain_s[rounds], 0, 0, part * BLK)])
    return p_pieces, s_pieces


def flatten_pieces(pieces, inputs):
    layout = []
    for piece in pieces:
        terms = []
        for arr, half, start, rows in piece:
            for idx, (known, known_half) in enumerate(inputs):
                if known is arr and known_half == half:
                    break
            else:
                inputs.append((arr, half))
                idx = len(inputs) - 1
            terms.append((idx, start, rows))
        layout.append(terms)
    return layout


def make_kernel(nb, lags, width, span, conv_start, p_layout, s_layout, n_halo, sub):
    def kernel(*refs):
        qc_ref, qa_ref, lk_ref = refs[:3]
        halo = refs[3 : 3 + n_halo]
        q_ref, ct_ref, k_ref, v_ref = refs[3 + n_halo : 7 + n_halo]
        out_ref, gq_ref, gk_ref, gv_ref, gd_ref = refs[7 + n_halo :]
        step = pl.program_id(0)
        lane = lax.broadcasted_iota(jnp.int32, (BLK, BLK), 1)
        lo = lane < DH
        flip = (lane + lax.broadcasted_iota(jnp.int32, (BLK, BLK), 0) == BLK - 1).astype(
            jnp.bfloat16
        )
        pad = jnp.zeros((BLK, BLK), jnp.float32)

        def assemble(layout, cols):
            pieces = []
            for terms in layout:
                total = None
                for idx, start, rows in terms:
                    term = halo[idx][start : start + rows, cols]
                    total = term if total is None else total + term
                pieces.append(total)
            return jnp.concatenate(pieces, 0)

        def masked(window, row):
            blocks = []
            for c in range(lags):
                block = window[c * BLK : (c + 1) * BLK]
                blocks.append(jnp.where(lk_ref[row, c] > 0, block, jnp.zeros_like(block)))
            return jnp.concatenate(blocks, 0)

        def table(ref, f, shift):
            row = ref[pl.ds(f, 1), :]
            full = jnp.broadcast_to(row, (BLK, span))
            rolled = pltpu.roll(full, shift, 1, stride=1, stride_axis=0)
            return rolled[:, :width]

        def diagonals(half):
            wide = jnp.concatenate([half, pad], 1)
            rolled = pltpu.roll(wide, 0, 1, stride=1, stride_axis=0)
            return rolled[:, :width].sum(0, keepdims=True)

        for j in range(sub):
            cols = slice(j * BLK, (j + 1) * BLK)
            f0 = 2 * (sub * step + j)
            pext = assemble(p_layout, cols)
            sext = assemble(s_layout, cols)
            tc = jnp.concatenate(
                [table(qc_ref, f0, span - (BLK - 1)), table(qc_ref, f0 + 1, span - (BLK - 1))], 0
            ).astype(jnp.bfloat16)
            ta = jnp.concatenate(
                [table(qa_ref, f0, span - BLK), table(qa_ref, f0 + 1, span - BLK)], 0
            ).astype(jnp.bfloat16)
            gsum = jnp.zeros((2 * BLK, width), jnp.float32)
            for n in range(nb):
                rows = pl.ds(n * BLK, BLK)
                lanes_j = pl.ds(j * BLK, BLK)
                pw = masked(pext[conv_start + n * BLK : conv_start + n * BLK + width], n)
                sw = masked(sext[n * BLK : n * BLK + width], nb + n)
                conv2 = jnp.dot(tc, pw, preferred_element_type=jnp.float32)
                conv = jnp.where(lo, conv2[:BLK], conv2[BLK:])
                adj2 = jnp.dot(ta, sw, preferred_element_type=jnp.float32)
                adj = jnp.where(lo, adj2[:BLK], adj2[BLK:])
                q = q_ref[rows, lanes_j].astype(jnp.float32)
                out_ref[rows, lanes_j] = (q * conv).astype(jnp.bfloat16)
                ct = ct_ref[rows, lanes_j].astype(jnp.float32)
                gq_ref[rows, lanes_j] = (ct * conv).astype(jnp.bfloat16)
                v = v_ref[rows, lanes_j].astype(jnp.float32)
                gk_ref[rows, lanes_j] = (adj * v).astype(jnp.bfloat16)
                k = k_ref[rows, lanes_j].astype(jnp.float32)
                gv_ref[rows, lanes_j] = (adj * k).astype(jnp.bfloat16)
                sr = jnp.dot(
                    flip, sext[n * BLK : (n + 1) * BLK], preferred_element_type=jnp.float32
                ).astype(jnp.bfloat16)
                zero = jnp.zeros_like(sr)
                a = jnp.concatenate([jnp.where(lo, sr, zero), jnp.where(lo, zero, sr)], 0)
                gsum = gsum + lax.dot_general(
                    a, pw, (((1,), (1,)), ((), ())), preferred_element_type=jnp.float32
                )
            gd_ref[0, 2 * j : 2 * j + 2, :] = jnp.concatenate(
                [diagonals(gsum[:BLK]), diagonals(gsum[BLK:])], 0
            )

    return kernel


def tables_and_links(filter_taps, doc_blocks, nb, lags):
    taps_total = filter_taps.shape[1]
    span = (lags + 1) * BLK
    rounded = filter_taps.astype(jnp.bfloat16).astype(jnp.float32)
    kept = min(taps_total, span - BLK)
    qa = jnp.pad(rounded[:, :kept], ((0, 0), (BLK, span - BLK - kept)))
    qc = jnp.flip(qa, 1)

    margin = lags + nb
    padded = jnp.concatenate(
        [jnp.full((margin,), -1, jnp.int32), doc_blocks, jnp.full((margin,), -2, jnp.int32)], 0
    )
    shard = lax.axis_index("seq")
    window = lax.dynamic_slice_in_dim(padded, shard * nb + margin - (lags - 1), 2 * (lags - 1) + nb)
    own = jnp.stack([window[lags - 1 + n] for n in range(nb)])
    conv_docs = jnp.stack([window[n : n + lags] for n in range(nb)])
    adj_docs = jnp.stack([window[lags - 1 + n : lags - 1 + n + lags] for n in range(nb)])
    links = jnp.concatenate([conv_docs == own[:, None], adj_docs == own[:, None]], 0)
    links = links.astype(jnp.int32)

    return qc, qa, links


def convolve_all(value_rows, key_rows, query_rows, cotangent, filter_taps, qc, qa, links, lags):
    tok_rows, channels = value_rows.shape
    filters, taps_total = filter_taps.shape
    nb = tok_rows // BLK
    width = lags * BLK
    span = width + BLK
    base = (lags - 1) * BLK
    sub = 2
    steps = channels // (BLK * sub)
    far = -(-(lags - 1) // nb)
    part = (lags - 1) - (far - 1) * nb
    product = (key_rows.astype(jnp.float32) * value_rows.astype(jnp.float32)).astype(jnp.bfloat16)
    scaled = (cotangent.astype(jnp.float32) * query_rows.astype(jnp.float32)).astype(jnp.bfloat16)
    halo = []
    p_pieces, s_pieces = halo_pieces(product, scaled, far, part, nb)
    p_layout = flatten_pieces(p_pieces, halo)
    s_layout = flatten_pieces(s_pieces, halo)
    conv_start = 0

    whole = lambda shape: pl.BlockSpec(shape, lambda s: (0, 0))
    lanes = lambda r: pl.BlockSpec((r, BLK * sub), lambda s: (0, s))
    kernel = make_kernel(
        nb, lags, width, span, conv_start, p_layout, s_layout, len(halo), sub
    )
    outs = pl.pallas_call(
        kernel,
        grid=(steps,),
        in_specs=[
            whole((filters, span)),
            whole((filters, span)),
            pl.BlockSpec(memory_space=pltpu.SMEM),
            *[
                pl.BlockSpec((h.shape[0], BLK * sub), lambda s, o=half * steps: (0, s + o))
                for h, half in halo
            ],
            lanes(tok_rows),
            lanes(tok_rows),
            lanes(tok_rows),
            lanes(tok_rows),
        ],
        out_specs=[
            lanes(tok_rows),
            lanes(tok_rows),
            lanes(tok_rows),
            lanes(tok_rows),
            pl.BlockSpec((1, 2 * sub, width), lambda s: (s, 0, 0)),
        ],
        out_shape=[
            jax.ShapeDtypeStruct((tok_rows, channels), jnp.bfloat16),
            jax.ShapeDtypeStruct((tok_rows, channels), jnp.bfloat16),
            jax.ShapeDtypeStruct((tok_rows, channels), jnp.bfloat16),
            jax.ShapeDtypeStruct((tok_rows, channels), jnp.bfloat16),
            jax.ShapeDtypeStruct((steps, 2 * sub, width), jnp.float32),
        ],
        compiler_params=pltpu.CompilerParams(
            dimension_semantics=("arbitrary",), vmem_limit_bytes=48 * 1024 * 1024
        ),
    )(qc, qa, links, *[h for h, _ in halo], query_rows, cotangent, key_rows, value_rows)
    output_rows, grad_query, grad_key, grad_value, diag = outs
    diag = diag.reshape(filters, width)
    top = min(taps_total, base + BLK)
    taps_grad = jnp.flip(diag[:, base + BLK - top : base + BLK], 1)
    taps_grad = taps_grad * (1.0 / (tok_rows * lax.axis_size("seq")))
    grad_filter = doubled_total(taps_grad, ("head", "seq"))
    if top < taps_total:
        grad_filter = jnp.pad(grad_filter, ((0, 0), (0, taps_total - top)))
    return output_rows, grad_query, grad_key, grad_value, grad_filter


def per_device(value_rows, key_rows, query_rows, cotangent, filter_taps, doc_blocks):
    tok_rows = value_rows.shape[0]
    taps_total = filter_taps.shape[1]
    full_lags = taps_total // BLK + 1
    short_lags = min(MOST, full_lags)
    nb = tok_rows // BLK
    rows = (value_rows, key_rows, query_rows, cotangent, filter_taps)
    full_args = rows + tables_and_links(filter_taps, doc_blocks, nb, full_lags)
    short_args = rows + tables_and_links(filter_taps, doc_blocks, nb, short_lags)
    nblk = doc_blocks.shape[0]
    apart = np.abs(np.arange(nblk)[:, None] - np.arange(nblk)[None, :])
    far_pairs = jnp.asarray((apart >= short_lags) & (apart < full_lags))
    same = doc_blocks[:, None] == doc_blocks[None, :]
    long_links = jnp.any(same & far_pairs)
    outs = lax.cond(
        long_links,
        lambda a, b: convolve_all(*a, full_lags),
        lambda a, b: convolve_all(*b, short_lags),
        full_args,
        short_args,
    )
    return tuple(outs)


def doubled_total(value, axes):
    for axis in axes:
        length = lax.axis_size(axis)
        bits = (length - 1).bit_length()
        for low in range(0, bits, 2):
            group = [1 << low] + ([1 << (low + 1)] if low + 1 < bits else [])
            swap = lambda m: lax.ppermute(value, axis, [(i, i ^ m) for i in range(length)])
            if len(group) == 1:
                value = value + swap(group[0])
            else:
                a, b = group
                value = (value + swap(a)) + (swap(b) + swap(a | b))
    return value


def solution(mesh):
    in_specs = (P("seq", "head"), P("seq", "head"), P("seq", "head"), P("seq", "head"), P(), P())
    out_specs = (P("seq", "head"), P("seq", "head"), P("seq", "head"), P("seq", "head"), P())
    return jax.shard_map(
        per_device, mesh=mesh, in_specs=in_specs, out_specs=out_specs, check_vma=False
    )
```

```python
import numpy as np
import jax
import jax.numpy as jnp
from jax import lax
from jax.experimental import pallas as pl
from jax.experimental.pallas import tpu as pltpu
from jax.sharding import PartitionSpec as P

DH = 64
BLK = 128
MOST = 12


def passed_along(value, axis, by):
    length = lax.axis_size(axis)
    pairs = [(i, i + by) for i in range(length) if 0 <= i + by < length]
    return lax.ppermute(value, axis, pairs)


def shifted_pairs(length, by, parity=None):
    return [
        (i, i + by)
        for i in range(length)
        if 0 <= i + by < length and (parity is None or (i + by) % 2 == parity)
    ]


def halo_pieces(product, scaled, far, part, nb):
    length = lax.axis_size("seq")
    rounds = far // 2
    rows = product.shape[0]
    chain_p, chain_s = [product], [scaled]
    for r in range(rounds):
        chain_p.append(lax.ppermute(chain_p[-1], "seq", shifted_pairs(length, 2)))
        chain_s.append(lax.ppermute(chain_s[-1], "seq", shifted_pairs(length, -2)))
    to_odd = [(i, i + 1) for i in range(0, length, 2)]
    to_even = [(i, i - 1) for i in range(1, length, 2)]
    odd_p, odd_s = [], []
    for k in range(rounds):
        up = jnp.concatenate(lax.optimization_barrier((chain_p[k], chain_s[k + 1])), 1)
        down = jnp.concatenate(lax.optimization_barrier((chain_p[k + 1], chain_s[k])), 1)
        up = lax.ppermute(up, "seq", to_odd)
        down = lax.ppermute(down, "seq", to_even)
        odd_p.append([(up, 0, 0, rows), (down, 0, 0, rows)])
        odd_s.append([(up, 1, 0, rows), (down, 1, 0, rows)])
    p_pieces = [[(chain_p[rounds], 0, (nb - part) * BLK, part * BLK)]]
    for r in range(rounds, 0, -1):
        p_pieces.append(odd_p[r - 1])
        if r > 1:
            p_pieces.append([(chain_p[r - 1], 0, 0, rows)])
    p_pieces.append([(product, 0, 0, rows)])
    s_pieces = [[(scaled, 0, 0, rows)]]
    for r in range(1, rounds + 1):
        s_pieces.append(odd_s[r - 1])
        if r < rounds:
            s_pieces.append([(chain_s[r], 0, 0, rows)])
    s_pieces.append([(chain_s[rounds], 0, 0, part * BLK)])
    return p_pieces, s_pieces


def flatten_pieces(pieces, inputs):
    layout = []
    for piece in pieces:
        terms = []
        for arr, half, start, rows in piece:
            for idx, (known, known_half) in enumerate(inputs):
                if known is arr and known_half == half:
                    break
            else:
                inputs.append((arr, half))
                idx = len(inputs) - 1
            terms.append((idx, start, rows))
        layout.append(terms)
    return layout


def make_kernel(nb, lags, width, span, conv_start, p_layout, s_layout, n_halo, sub):
    def kernel(*refs):
        qc_ref, qa_ref, lk_ref = refs[:3]
        halo = refs[3 : 3 + n_halo]
        q_ref, ct_ref, k_ref, v_ref = refs[3 + n_halo : 7 + n_halo]
        out_ref, gq_ref, gk_ref, gv_ref, gd_ref = refs[7 + n_halo :]
        step = pl.program_id(0)
        lane = lax.broadcasted_iota(jnp.int32, (BLK, BLK), 1)
        lo = lane < DH
        flip = (lane + lax.broadcasted_iota(jnp.int32, (BLK, BLK), 0) == BLK - 1).astype(
            jnp.bfloat16
        )
        pad = jnp.zeros((BLK, BLK), jnp.float32)

        def assemble(layout, cols):
            pieces = []
            for terms in layout:
                total = None
                for idx, start, rows in terms:
                    term = halo[idx][start : start + rows, cols]
                    total = term if total is None else total + term
                pieces.append(total)
            return jnp.concatenate(pieces, 0)

        def masked(window, row):
            blocks = []
            for c in range(lags):
                block = window[c * BLK : (c + 1) * BLK]
                blocks.append(jnp.where(lk_ref[row, c] > 0, block, jnp.zeros_like(block)))
            return jnp.concatenate(blocks, 0)

        def table(ref, f, shift):
            row = ref[pl.ds(f, 1), :]
            full = jnp.broadcast_to(row, (BLK, span))
            rolled = pltpu.roll(full, shift, 1, stride=1, stride_axis=0)
            return rolled[:, :width]

        def diagonals(half):
            wide = jnp.concatenate([half, pad], 1)
            rolled = pltpu.roll(wide, 0, 1, stride=1, stride_axis=0)
            return rolled[:, :width].sum(0, keepdims=True)

        for j in range(sub):
            cols = slice(j * BLK, (j + 1) * BLK)
            f0 = 2 * (sub * step + j)
            pext = assemble(p_layout, cols)
            sext = assemble(s_layout, cols)
            tc = jnp.concatenate(
                [table(qc_ref, f0, span - (BLK - 1)), table(qc_ref, f0 + 1, span - (BLK - 1))], 0
            ).astype(jnp.bfloat16)
            ta = jnp.concatenate(
                [table(qa_ref, f0, span - BLK), table(qa_ref, f0 + 1, span - BLK)], 0
            ).astype(jnp.bfloat16)
            gsum = jnp.zeros((2 * BLK, width), jnp.float32)
            for n in range(nb):
                rows = pl.ds(n * BLK, BLK)
                lanes_j = pl.ds(j * BLK, BLK)
                pw = masked(pext[conv_start + n * BLK : conv_start + n * BLK + width], n)
                sw = masked(sext[n * BLK : n * BLK + width], nb + n)
                conv2 = jnp.dot(tc, pw, preferred_element_type=jnp.float32)
                conv = jnp.where(lo, conv2[:BLK], conv2[BLK:])
                adj2 = jnp.dot(ta, sw, preferred_element_type=jnp.float32)
                adj = jnp.where(lo, adj2[:BLK], adj2[BLK:])
                q = q_ref[rows, lanes_j].astype(jnp.float32)
                out_ref[rows, lanes_j] = (q * conv).astype(jnp.bfloat16)
                ct = ct_ref[rows, lanes_j].astype(jnp.float32)
                gq_ref[rows, lanes_j] = (ct * conv).astype(jnp.bfloat16)
                v = v_ref[rows, lanes_j].astype(jnp.float32)
                gk_ref[rows, lanes_j] = (adj * v).astype(jnp.bfloat16)
                k = k_ref[rows, lanes_j].astype(jnp.float32)
                gv_ref[rows, lanes_j] = (adj * k).astype(jnp.bfloat16)
                sr = jnp.dot(
                    flip, sext[n * BLK : (n + 1) * BLK], preferred_element_type=jnp.float32
                ).astype(jnp.bfloat16)
                zero = jnp.zeros_like(sr)
                a = jnp.concatenate([jnp.where(lo, sr, zero), jnp.where(lo, zero, sr)], 0)
                gsum = gsum + lax.dot_general(
                    a, pw, (((1,), (1,)), ((), ())), preferred_element_type=jnp.float32
                )
            gd_ref[0, 2 * j : 2 * j + 2, :] = jnp.concatenate(
                [diagonals(gsum[:BLK]), diagonals(gsum[BLK:])], 0
            )

    return kernel


def tables_and_links(filter_taps, doc_blocks, nb, lags):
    taps_total = filter_taps.shape[1]
    span = (lags + 1) * BLK
    rounded = filter_taps.astype(jnp.bfloat16).astype(jnp.float32)
    kept = min(taps_total, span - BLK)
    qa = jnp.pad(rounded[:, :kept], ((0, 0), (BLK, span - BLK - kept)))
    qc = jnp.flip(qa, 1)

    margin = lags + nb
    padded = jnp.concatenate(
        [jnp.full((margin,), -1, jnp.int32), doc_blocks, jnp.full((margin,), -2, jnp.int32)], 0
    )
    shard = lax.axis_index("seq")
    window = lax.dynamic_slice_in_dim(padded, shard * nb + margin - (lags - 1), 2 * (lags - 1) + nb)
    own = jnp.stack([window[lags - 1 + n] for n in range(nb)])
    conv_docs = jnp.stack([window[n : n + lags] for n in range(nb)])
    adj_docs = jnp.stack([window[lags - 1 + n : lags - 1 + n + lags] for n in range(nb)])
    links = jnp.concatenate([conv_docs == own[:, None], adj_docs == own[:, None]], 0)
    links = links.astype(jnp.int32)

    return qc, qa, links


def convolve_all(value_rows, key_rows, query_rows, cotangent, filter_taps, qc, qa, links, lags):
    tok_rows, channels = value_rows.shape
    filters, taps_total = filter_taps.shape
    nb = tok_rows // BLK
    width = lags * BLK
    span = width + BLK
    base = (lags - 1) * BLK
    sub = 2
    steps = channels // (BLK * sub)
    far = -(-(lags - 1) // nb)
    part = (lags - 1) - (far - 1) * nb
    product = (key_rows.astype(jnp.float32) * value_rows.astype(jnp.float32)).astype(jnp.bfloat16)
    scaled = (cotangent.astype(jnp.float32) * query_rows.astype(jnp.float32)).astype(jnp.bfloat16)
    halo = []
    p_pieces, s_pieces = halo_pieces(product, scaled, far, part, nb)
    p_layout = flatten_pieces(p_pieces, halo)
    s_layout = flatten_pieces(s_pieces, halo)
    conv_start = 0

    whole = lambda shape: pl.BlockSpec(shape, lambda s: (0, 0))
    lanes = lambda r: pl.BlockSpec((r, BLK * sub), lambda s: (0, s))
    kernel = make_kernel(
        nb, lags, width, span, conv_start, p_layout, s_layout, len(halo), sub
    )
    outs = pl.pallas_call(
        kernel,
        grid=(steps,),
        in_specs=[
            whole((filters, span)),
            whole((filters, span)),
            pl.BlockSpec(memory_space=pltpu.SMEM),
            *[
                pl.BlockSpec((h.shape[0], BLK * sub), lambda s, o=half * steps: (0, s + o))
                for h, half in halo
            ],
            lanes(tok_rows),
            lanes(tok_rows),
            lanes(tok_rows),
            lanes(tok_rows),
        ],
        out_specs=[
            lanes(tok_rows),
            lanes(tok_rows),
            lanes(tok_rows),
            lanes(tok_rows),
            pl.BlockSpec((1, 2 * sub, width), lambda s: (s, 0, 0)),
        ],
        out_shape=[
            jax.ShapeDtypeStruct((tok_rows, channels), jnp.bfloat16),
            jax.ShapeDtypeStruct((tok_rows, channels), jnp.bfloat16),
            jax.ShapeDtypeStruct((tok_rows, channels), jnp.bfloat16),
            jax.ShapeDtypeStruct((tok_rows, channels), jnp.bfloat16),
            jax.ShapeDtypeStruct((steps, 2 * sub, width), jnp.float32),
        ],
        compiler_params=pltpu.CompilerParams(
            dimension_semantics=("arbitrary",), vmem_limit_bytes=48 * 1024 * 1024
        ),
    )(qc, qa, links, *[h for h, _ in halo], query_rows, cotangent, key_rows, value_rows)
    output_rows, grad_query, grad_key, grad_value, diag = outs
    diag = diag.reshape(filters, width)
    top = min(taps_total, base + BLK)
    taps_grad = jnp.flip(diag[:, base + BLK - top : base + BLK], 1)
    taps_grad = taps_grad * (1.0 / (tok_rows * lax.axis_size("seq")))
    grad_filter = doubled_total(taps_grad, ("head", "seq"))
    if top < taps_total:
        grad_filter = jnp.pad(grad_filter, ((0, 0), (0, taps_total - top)))
    return output_rows, grad_query, grad_key, grad_value, grad_filter


def per_device(value_rows, key_rows, query_rows, cotangent, filter_taps, doc_blocks):
    tok_rows = value_rows.shape[0]
    taps_total = filter_taps.shape[1]
    full_lags = taps_total // BLK + 1
    short_lags = min(MOST, full_lags)
    nb = tok_rows // BLK
    rows = (value_rows, key_rows, query_rows, cotangent, filter_taps)
    short_args = rows + tables_and_links(filter_taps, doc_blocks, nb, short_lags)
    nblk = doc_blocks.shape[0]
    apart = np.abs(np.arange(nblk)[:, None] - np.arange(nblk)[None, :])
    far_pairs = jnp.asarray((apart >= short_lags) & (apart < full_lags))
    same = doc_blocks[:, None] == doc_blocks[None, :]
    long_links = jnp.any(same & far_pairs)
    outs = lax.cond(
        long_links,
        lambda a, b: convolve_all(
            *a[:-1], *tables_and_links(a[4], a[-1], nb, full_lags), full_lags
        ),
        lambda a, b: convolve_all(*b, short_lags),
        rows + (doc_blocks,),
        short_args,
    )
    return tuple(outs)


def doubled_total(value, axes):
    for axis in axes:
        length = lax.axis_size(axis)
        bits = (length - 1).bit_length()
        for low in range(0, bits, 2):
            group = [1 << low] + ([1 << (low + 1)] if low + 1 < bits else [])
            swap = lambda m: lax.ppermute(value, axis, [(i, i ^ m) for i in range(length)])
            if len(group) == 1:
                value = value + swap(group[0])
            else:
                a, b = group
                value = (value + swap(a)) + (swap(b) + swap(a | b))
    return value


def solution(mesh):
    in_specs = (P("seq", "head"), P("seq", "head"), P("seq", "head"), P("seq", "head"), P(), P())
    out_specs = (P("seq", "head"), P("seq", "head"), P("seq", "head"), P("seq", "head"), P())
    return jax.shard_map(
        per_device, mesh=mesh, in_specs=in_specs, out_specs=out_specs, check_vma=False
    )
```

```python
import numpy as np
import jax
import jax.numpy as jnp
from jax import lax
from jax.experimental import pallas as pl
from jax.experimental.pallas import tpu as pltpu
from jax.sharding import PartitionSpec as P

DH = 64
BLK = 128
MOST = 12


def passed_along(value, axis, by):
    length = lax.axis_size(axis)
    pairs = [(i, i + by) for i in range(length) if 0 <= i + by < length]
    return lax.ppermute(value, axis, pairs)


def shifted_pairs(length, by, parity=None):
    return [
        (i, i + by)
        for i in range(length)
        if 0 <= i + by < length and (parity is None or (i + by) % 2 == parity)
    ]


def halo_pieces(product, scaled, first_p, first_s, far, part, nb):
    length = lax.axis_size("seq")
    rounds = far // 2
    rows = product.shape[0]
    chain_p, chain_s = [product, first_p], [scaled, first_s]
    for r in range(1, rounds):
        chain_p.append(lax.ppermute(chain_p[-1], "seq", shifted_pairs(length, 2)))
        chain_s.append(lax.ppermute(chain_s[-1], "seq", shifted_pairs(length, -2)))
    to_odd = [(i, i + 1) for i in range(0, length, 2)]
    to_even = [(i, i - 1) for i in range(1, length, 2)]
    odd_p, odd_s = [], []
    for k in range(rounds):
        up = jnp.concatenate(lax.optimization_barrier((chain_p[k], chain_s[k + 1])), 1)
        down = jnp.concatenate(lax.optimization_barrier((chain_p[k + 1], chain_s[k])), 1)
        up = lax.ppermute(up, "seq", to_odd)
        down = lax.ppermute(down, "seq", to_even)
        odd_p.append([(up, 0, 0, rows), (down, 0, 0, rows)])
        odd_s.append([(up, 1, 0, rows), (down, 1, 0, rows)])
    p_pieces = [[(chain_p[rounds], 0, (nb - part) * BLK, part * BLK)]]
    for r in range(rounds, 0, -1):
        p_pieces.append(odd_p[r - 1])
        if r > 1:
            p_pieces.append([(chain_p[r - 1], 0, 0, rows)])
    p_pieces.append([(product, 0, 0, rows)])
    s_pieces = [[(scaled, 0, 0, rows)]]
    for r in range(1, rounds + 1):
        s_pieces.append(odd_s[r - 1])
        if r < rounds:
            s_pieces.append([(chain_s[r], 0, 0, rows)])
    s_pieces.append([(chain_s[rounds], 0, 0, part * BLK)])
    return p_pieces, s_pieces


def flatten_pieces(pieces, inputs):
    layout = []
    for piece in pieces:
        terms = []
        for arr, half, start, rows in piece:
            for idx, (known, known_half) in enumerate(inputs):
                if known is arr and known_half == half:
                    break
            else:
                inputs.append((arr, half))
                idx = len(inputs) - 1
            terms.append((idx, start, rows))
        layout.append(terms)
    return layout


def make_kernel(nb, lags, width, span, conv_start, p_layout, s_layout, n_halo, sub):
    def kernel(*refs):
        qc_ref, qa_ref, lk_ref = refs[:3]
        halo = refs[3 : 3 + n_halo]
        q_ref, ct_ref, k_ref, v_ref = refs[3 + n_halo : 7 + n_halo]
        out_ref, gq_ref, gk_ref, gv_ref, gd_ref = refs[7 + n_halo :]
        step = pl.program_id(0)
        lane = lax.broadcasted_iota(jnp.int32, (BLK, BLK), 1)
        lo = lane < DH
        flip = (lane + lax.broadcasted_iota(jnp.int32, (BLK, BLK), 0) == BLK - 1).astype(
            jnp.bfloat16
        )
        pad = jnp.zeros((BLK, BLK), jnp.float32)

        def assemble(layout, cols):
            pieces = []
            for terms in layout:
                total = None
                for idx, start, rows in terms:
                    term = halo[idx][start : start + rows, cols]
                    total = term if total is None else total + term
                pieces.append(total)
            return jnp.concatenate(pieces, 0)

        def masked(window, row):
            blocks = []
            for c in range(lags):
                block = window[c * BLK : (c + 1) * BLK]
                blocks.append(jnp.where(lk_ref[row, c] > 0, block, jnp.zeros_like(block)))
            return jnp.concatenate(blocks, 0)

        def table(ref, f, shift):
            row = ref[pl.ds(f, 1), :]
            full = jnp.broadcast_to(row, (BLK, span))
            rolled = pltpu.roll(full, shift, 1, stride=1, stride_axis=0)
            return rolled[:, :width]

        def diagonals(half):
            wide = jnp.concatenate([half, pad], 1)
            rolled = pltpu.roll(wide, 0, 1, stride=1, stride_axis=0)
            return rolled[:, :width].sum(0, keepdims=True)

        for j in range(sub):
            cols = slice(j * BLK, (j + 1) * BLK)
            f0 = 2 * (sub * step + j)
            pext = assemble(p_layout, cols)
            sext = assemble(s_layout, cols)
            tc = jnp.concatenate(
                [table(qc_ref, f0, span - (BLK - 1)), table(qc_ref, f0 + 1, span - (BLK - 1))], 0
            ).astype(jnp.bfloat16)
            ta = jnp.concatenate(
                [table(qa_ref, f0, span - BLK), table(qa_ref, f0 + 1, span - BLK)], 0
            ).astype(jnp.bfloat16)
            gsum = jnp.zeros((2 * BLK, width), jnp.float32)
            for n in range(nb):
                rows = pl.ds(n * BLK, BLK)
                lanes_j = pl.ds(j * BLK, BLK)
                pw = masked(pext[conv_start + n * BLK : conv_start + n * BLK + width], n)
                sw = masked(sext[n * BLK : n * BLK + width], nb + n)
                conv2 = jnp.dot(tc, pw, preferred_element_type=jnp.float32)
                conv = jnp.where(lo, conv2[:BLK], conv2[BLK:])
                adj2 = jnp.dot(ta, sw, preferred_element_type=jnp.float32)
                adj = jnp.where(lo, adj2[:BLK], adj2[BLK:])
                q = q_ref[rows, lanes_j].astype(jnp.float32)
                out_ref[rows, lanes_j] = (q * conv).astype(jnp.bfloat16)
                ct = ct_ref[rows, lanes_j].astype(jnp.float32)
                gq_ref[rows, lanes_j] = (ct * conv).astype(jnp.bfloat16)
                v = v_ref[rows, lanes_j].astype(jnp.float32)
                gk_ref[rows, lanes_j] = (adj * v).astype(jnp.bfloat16)
                k = k_ref[rows, lanes_j].astype(jnp.float32)
                gv_ref[rows, lanes_j] = (adj * k).astype(jnp.bfloat16)
                sr = jnp.dot(
                    flip, sext[n * BLK : (n + 1) * BLK], preferred_element_type=jnp.float32
                ).astype(jnp.bfloat16)
                zero = jnp.zeros_like(sr)
                a = jnp.concatenate([jnp.where(lo, sr, zero), jnp.where(lo, zero, sr)], 0)
                gsum = gsum + lax.dot_general(
                    a, pw, (((1,), (1,)), ((), ())), preferred_element_type=jnp.float32
                )
            gd_ref[0, 2 * j : 2 * j + 2, :] = jnp.concatenate(
                [diagonals(gsum[:BLK]), diagonals(gsum[BLK:])], 0
            )

    return kernel


def tables_and_links(filter_taps, doc_blocks, nb, lags):
    taps_total = filter_taps.shape[1]
    span = (lags + 1) * BLK
    rounded = filter_taps.astype(jnp.bfloat16).astype(jnp.float32)
    kept = min(taps_total, span - BLK)
    qa = jnp.pad(rounded[:, :kept], ((0, 0), (BLK, span - BLK - kept)))
    qc = jnp.flip(qa, 1)

    margin = lags + nb
    padded = jnp.concatenate(
        [jnp.full((margin,), -1, jnp.int32), doc_blocks, jnp.full((margin,), -2, jnp.int32)], 0
    )
    shard = lax.axis_index("seq")
    window = lax.dynamic_slice_in_dim(padded, shard * nb + margin - (lags - 1), 2 * (lags - 1) + nb)
    own = jnp.stack([window[lags - 1 + n] for n in range(nb)])
    conv_docs = jnp.stack([window[n : n + lags] for n in range(nb)])
    adj_docs = jnp.stack([window[lags - 1 + n : lags - 1 + n + lags] for n in range(nb)])
    links = jnp.concatenate([conv_docs == own[:, None], adj_docs == own[:, None]], 0)
    links = links.astype(jnp.int32)

    return qc, qa, links


def convolve_all(
    value_rows, key_rows, query_rows, cotangent, product, scaled, first_p, first_s,
    filter_taps, qc, qa, links, lags,
):
    tok_rows, channels = value_rows.shape
    filters, taps_total = filter_taps.shape
    nb = tok_rows // BLK
    width = lags * BLK
    span = width + BLK
    base = (lags - 1) * BLK
    sub = 2
    steps = channels // (BLK * sub)
    far = -(-(lags - 1) // nb)
    part = (lags - 1) - (far - 1) * nb
    halo = []
    p_pieces, s_pieces = halo_pieces(product, scaled, first_p, first_s, far, part, nb)
    p_layout = flatten_pieces(p_pieces, halo)
    s_layout = flatten_pieces(s_pieces, halo)
    conv_start = 0

    whole = lambda shape: pl.BlockSpec(shape, lambda s: (0, 0))
    lanes = lambda r: pl.BlockSpec((r, BLK * sub), lambda s: (0, s))
    kernel = make_kernel(
        nb, lags, width, span, conv_start, p_layout, s_layout, len(halo), sub
    )
    outs = pl.pallas_call(
        kernel,
        grid=(steps,),
        in_specs=[
            whole((filters, span)),
            whole((filters, span)),
            pl.BlockSpec(memory_space=pltpu.SMEM),
            *[
                pl.BlockSpec((h.shape[0], BLK * sub), lambda s, o=half * steps: (0, s + o))
                for h, half in halo
            ],
            lanes(tok_rows),
            lanes(tok_rows),
            lanes(tok_rows),
            lanes(tok_rows),
        ],
        out_specs=[
            lanes(tok_rows),
            lanes(tok_rows),
            lanes(tok_rows),
            lanes(tok_rows),
            pl.BlockSpec((1, 2 * sub, width), lambda s: (s, 0, 0)),
        ],
        out_shape=[
            jax.ShapeDtypeStruct((tok_rows, channels), jnp.bfloat16),
            jax.ShapeDtypeStruct((tok_rows, channels), jnp.bfloat16),
            jax.ShapeDtypeStruct((tok_rows, channels), jnp.bfloat16),
            jax.ShapeDtypeStruct((tok_rows, channels), jnp.bfloat16),
            jax.ShapeDtypeStruct((steps, 2 * sub, width), jnp.float32),
        ],
        compiler_params=pltpu.CompilerParams(
            dimension_semantics=("arbitrary",), vmem_limit_bytes=48 * 1024 * 1024
        ),
    )(qc, qa, links, *[h for h, _ in halo], query_rows, cotangent, key_rows, value_rows)
    output_rows, grad_query, grad_key, grad_value, diag = outs
    diag = diag.reshape(filters, width)
    top = min(taps_total, base + BLK)
    taps_grad = jnp.flip(diag[:, base + BLK - top : base + BLK], 1)
    taps_grad = taps_grad * (1.0 / (tok_rows * lax.axis_size("seq")))
    grad_filter = doubled_total(taps_grad, ("head", "seq"))
    if top < taps_total:
        grad_filter = jnp.pad(grad_filter, ((0, 0), (0, taps_total - top)))
    return output_rows, grad_query, grad_key, grad_value, grad_filter


def per_device(value_rows, key_rows, query_rows, cotangent, filter_taps, doc_blocks):
    tok_rows = value_rows.shape[0]
    taps_total = filter_taps.shape[1]
    full_lags = taps_total // BLK + 1
    short_lags = min(MOST, full_lags)
    nb = tok_rows // BLK
    product = (key_rows.astype(jnp.float32) * value_rows.astype(jnp.float32)).astype(jnp.bfloat16)
    scaled = (cotangent.astype(jnp.float32) * query_rows.astype(jnp.float32)).astype(jnp.bfloat16)
    length = lax.axis_size("seq")
    first_p = lax.ppermute(product, "seq", shifted_pairs(length, 2))
    first_s = lax.ppermute(scaled, "seq", shifted_pairs(length, -2))
    rows = (value_rows, key_rows, query_rows, cotangent, product, scaled, first_p, first_s,
            filter_taps)
    short_args = rows + tables_and_links(filter_taps, doc_blocks, nb, short_lags)
    nblk = doc_blocks.shape[0]
    apart = np.abs(np.arange(nblk)[:, None] - np.arange(nblk)[None, :])
    far_pairs = jnp.asarray((apart >= short_lags) & (apart < full_lags))
    same = doc_blocks[:, None] == doc_blocks[None, :]
    long_links = jnp.any(same & far_pairs)
    outs = lax.cond(
        long_links,
        lambda a, b: convolve_all(
            *a[:-1], *tables_and_links(a[8], a[-1], nb, full_lags), full_lags
        ),
        lambda a, b: convolve_all(*b, short_lags),
        rows + (doc_blocks,),
        short_args,
    )
    return tuple(outs)


def doubled_total(value, axes):
    for axis in axes:
        length = lax.axis_size(axis)
        bits = (length - 1).bit_length()
        for low in range(0, bits, 2):
            group = [1 << low] + ([1 << (low + 1)] if low + 1 < bits else [])
            swap = lambda m: lax.ppermute(value, axis, [(i, i ^ m) for i in range(length)])
            if len(group) == 1:
                value = value + swap(group[0])
            else:
                a, b = group
                value = (value + swap(a)) + (swap(b) + swap(a | b))
    return value


def solution(mesh):
    in_specs = (P("seq", "head"), P("seq", "head"), P("seq", "head"), P("seq", "head"), P(), P())
    out_specs = (P("seq", "head"), P("seq", "head"), P("seq", "head"), P("seq", "head"), P())
    return jax.shard_map(
        per_device, mesh=mesh, in_specs=in_specs, out_specs=out_specs, check_vma=False
    )
```

```python
import numpy as np
import jax
import jax.numpy as jnp
from jax import lax
from jax.experimental import pallas as pl
from jax.experimental.pallas import tpu as pltpu
from jax.sharding import PartitionSpec as P

DH = 64
BLK = 128
MOST = 12


def passed_along(value, axis, by):
    length = lax.axis_size(axis)
    pairs = [(i, i + by) for i in range(length) if 0 <= i + by < length]
    return lax.ppermute(value, axis, pairs)


def shifted_pairs(length, by, parity=None):
    return [
        (i, i + by)
        for i in range(length)
        if 0 <= i + by < length and (parity is None or (i + by) % 2 == parity)
    ]


def halo_pieces(product, scaled, far, part, nb):
    length = lax.axis_size("seq")
    rounds = far // 2
    rows = product.shape[0]
    chain_p, chain_s = [product], [scaled]
    for r in range(rounds):
        chain_p.append(lax.ppermute(chain_p[-1], "seq", shifted_pairs(length, 2)))
        chain_s.append(lax.ppermute(chain_s[-1], "seq", shifted_pairs(length, -2)))
    to_odd = [(i, i + 1) for i in range(0, length, 2)]
    to_even = [(i, i - 1) for i in range(1, length, 2)]
    odd_p, odd_s = [], []
    for k in range(rounds):
        up = jnp.concatenate(lax.optimization_barrier((chain_p[k], chain_s[k + 1])), 1)
        down = jnp.concatenate(lax.optimization_barrier((chain_p[k + 1], chain_s[k])), 1)
        up = lax.ppermute(up, "seq", to_odd)
        down = lax.ppermute(down, "seq", to_even)
        odd_p.append([(up, 0, 0, rows), (down, 0, 0, rows)])
        odd_s.append([(up, 1, 0, rows), (down, 1, 0, rows)])
    p_pieces = [[(chain_p[rounds], 0, (nb - part) * BLK, part * BLK)]]
    for r in range(rounds, 0, -1):
        p_pieces.append(odd_p[r - 1])
        if r > 1:
            p_pieces.append([(chain_p[r - 1], 0, 0, rows)])
    p_pieces.append([(product, 0, 0, rows)])
    s_pieces = [[(scaled, 0, 0, rows)]]
    for r in range(1, rounds + 1):
        s_pieces.append(odd_s[r - 1])
        if r < rounds:
            s_pieces.append([(chain_s[r], 0, 0, rows)])
    s_pieces.append([(chain_s[rounds], 0, 0, part * BLK)])
    return p_pieces, s_pieces


def flatten_pieces(pieces, inputs):
    layout = []
    for piece in pieces:
        terms = []
        for arr, half, start, rows in piece:
            for idx, (known, known_half) in enumerate(inputs):
                if known is arr and known_half == half:
                    break
            else:
                inputs.append((arr, half))
                idx = len(inputs) - 1
            terms.append((idx, start, rows))
        layout.append(terms)
    return layout


def make_kernel(nb, lags, width, span, conv_start, p_layout, s_layout, n_halo, sub):
    def kernel(*refs):
        qc_ref, qa_ref, lk_ref = refs[:3]
        halo = refs[3 : 3 + n_halo]
        q_ref, ct_ref, k_ref, v_ref = refs[3 + n_halo : 7 + n_halo]
        out_ref, gq_ref, gk_ref, gv_ref, gd_ref = refs[7 + n_halo :]
        step = pl.program_id(0)
        lane = lax.broadcasted_iota(jnp.int32, (BLK, BLK), 1)
        lo = lane < DH
        flip = (lane + lax.broadcasted_iota(jnp.int32, (BLK, BLK), 0) == BLK - 1).astype(
            jnp.bfloat16
        )
        pad = jnp.zeros((BLK, BLK), jnp.float32)

        def assemble(layout, cols):
            pieces = []
            for terms in layout:
                total = None
                for idx, start, rows in terms:
                    term = halo[idx][start : start + rows, cols]
                    total = term if total is None else total + term
                pieces.append(total)
            return jnp.concatenate(pieces, 0)

        def masked(window, row):
            blocks = []
            for c in range(lags):
                block = window[c * BLK : (c + 1) * BLK]
                blocks.append(jnp.where(lk_ref[row, c] > 0, block, jnp.zeros_like(block)))
            return jnp.concatenate(blocks, 0)

        def table(ref, f, shift):
            row = ref[pl.ds(f, 1), :]
            full = jnp.broadcast_to(row, (BLK, span))
            rolled = pltpu.roll(full, shift, 1, stride=1, stride_axis=0)
            return rolled[:, :width]

        def diagonals(half):
            wide = jnp.concatenate([half, pad], 1)
            rolled = pltpu.roll(wide, 0, 1, stride=1, stride_axis=0)
            return rolled[:, :width].sum(0, keepdims=True)

        for j in range(sub):
            cols = slice(j * BLK, (j + 1) * BLK)
            f0 = 2 * (sub * step + j)
            pext = assemble(p_layout, cols)
            sext = assemble(s_layout, cols)
            tc = jnp.concatenate(
                [table(qc_ref, f0, span - (BLK - 1)), table(qc_ref, f0 + 1, span - (BLK - 1))], 0
            ).astype(jnp.bfloat16)
            ta = jnp.concatenate(
                [table(qa_ref, f0, span - BLK), table(qa_ref, f0 + 1, span - BLK)], 0
            ).astype(jnp.bfloat16)
            gsum = jnp.zeros((2 * BLK, width), jnp.float32)
            for n in range(nb):
                rows = pl.ds(n * BLK, BLK)
                lanes_j = pl.ds(j * BLK, BLK)
                pw = masked(pext[conv_start + n * BLK : conv_start + n * BLK + width], n)
                sw = masked(sext[n * BLK : n * BLK + width], nb + n)
                conv2 = jnp.dot(tc, pw, preferred_element_type=jnp.float32)
                conv = jnp.where(lo, conv2[:BLK], conv2[BLK:])
                adj2 = jnp.dot(ta, sw, preferred_element_type=jnp.float32)
                adj = jnp.where(lo, adj2[:BLK], adj2[BLK:])
                q = q_ref[rows, lanes_j].astype(jnp.float32)
                out_ref[rows, lanes_j] = (q * conv).astype(jnp.bfloat16)
                ct = ct_ref[rows, lanes_j].astype(jnp.float32)
                gq_ref[rows, lanes_j] = (ct * conv).astype(jnp.bfloat16)
                v = v_ref[rows, lanes_j].astype(jnp.float32)
                gk_ref[rows, lanes_j] = (adj * v).astype(jnp.bfloat16)
                k = k_ref[rows, lanes_j].astype(jnp.float32)
                gv_ref[rows, lanes_j] = (adj * k).astype(jnp.bfloat16)
                sr = jnp.dot(
                    flip, sext[n * BLK : (n + 1) * BLK], preferred_element_type=jnp.float32
                ).astype(jnp.bfloat16)
                zero = jnp.zeros_like(sr)
                a = jnp.concatenate([jnp.where(lo, sr, zero), jnp.where(lo, zero, sr)], 0)
                gsum = gsum + lax.dot_general(
                    a, pw, (((1,), (1,)), ((), ())), preferred_element_type=jnp.float32
                )
            gd_ref[0, 2 * j : 2 * j + 2, :] = jnp.concatenate(
                [diagonals(gsum[:BLK]), diagonals(gsum[BLK:])], 0
            )

    return kernel


def tables_and_links(filter_taps, doc_blocks, nb, lags):
    taps_total = filter_taps.shape[1]
    span = (lags + 1) * BLK
    rounded = filter_taps.astype(jnp.bfloat16).astype(jnp.float32)
    kept = min(taps_total, span - BLK)
    qa = jnp.pad(rounded[:, :kept], ((0, 0), (BLK, span - BLK - kept)))
    qc = jnp.flip(qa, 1)

    margin = lags + nb
    padded = jnp.concatenate(
        [jnp.full((margin,), -1, jnp.int32), doc_blocks, jnp.full((margin,), -2, jnp.int32)], 0
    )
    shard = lax.axis_index("seq")
    window = lax.dynamic_slice_in_dim(padded, shard * nb + margin - (lags - 1), 2 * (lags - 1) + nb)
    own = jnp.stack([window[lags - 1 + n] for n in range(nb)])
    conv_docs = jnp.stack([window[n : n + lags] for n in range(nb)])
    adj_docs = jnp.stack([window[lags - 1 + n : lags - 1 + n + lags] for n in range(nb)])
    links = jnp.concatenate([conv_docs == own[:, None], adj_docs == own[:, None]], 0)
    links = links.astype(jnp.int32)

    return qc, qa, links


def convolve_all(value_rows, key_rows, query_rows, cotangent, filter_taps, qc, qa, links, lags):
    tok_rows, channels = value_rows.shape
    filters, taps_total = filter_taps.shape
    nb = tok_rows // BLK
    width = lags * BLK
    span = width + BLK
    base = (lags - 1) * BLK
    sub = 2
    steps = channels // (BLK * sub)
    far = -(-(lags - 1) // nb)
    part = (lags - 1) - (far - 1) * nb
    product = (key_rows.astype(jnp.float32) * value_rows.astype(jnp.float32)).astype(jnp.bfloat16)
    scaled = (cotangent.astype(jnp.float32) * query_rows.astype(jnp.float32)).astype(jnp.bfloat16)
    halo = []
    p_pieces, s_pieces = halo_pieces(product, scaled, far, part, nb)
    p_layout = flatten_pieces(p_pieces, halo)
    s_layout = flatten_pieces(s_pieces, halo)
    conv_start = 0

    whole = lambda shape: pl.BlockSpec(shape, lambda s: (0, 0))
    lanes = lambda r: pl.BlockSpec((r, BLK * sub), lambda s: (0, s))
    kernel = make_kernel(
        nb, lags, width, span, conv_start, p_layout, s_layout, len(halo), sub
    )
    outs = pl.pallas_call(
        kernel,
        grid=(steps,),
        in_specs=[
            whole((filters, span)),
            whole((filters, span)),
            pl.BlockSpec(memory_space=pltpu.SMEM),
            *[
                pl.BlockSpec((h.shape[0], BLK * sub), lambda s, o=half * steps: (0, s + o))
                for h, half in halo
            ],
            lanes(tok_rows),
            lanes(tok_rows),
            lanes(tok_rows),
            lanes(tok_rows),
        ],
        out_specs=[
            lanes(tok_rows),
            lanes(tok_rows),
            lanes(tok_rows),
            lanes(tok_rows),
            pl.BlockSpec((1, 2 * sub, width), lambda s: (s, 0, 0)),
        ],
        out_shape=[
            jax.ShapeDtypeStruct((tok_rows, channels), jnp.bfloat16),
            jax.ShapeDtypeStruct((tok_rows, channels), jnp.bfloat16),
            jax.ShapeDtypeStruct((tok_rows, channels), jnp.bfloat16),
            jax.ShapeDtypeStruct((tok_rows, channels), jnp.bfloat16),
            jax.ShapeDtypeStruct((steps, 2 * sub, width), jnp.float32),
        ],
        compiler_params=pltpu.CompilerParams(
            dimension_semantics=("arbitrary",), vmem_limit_bytes=48 * 1024 * 1024
        ),
    )(qc, qa, links, *[h for h, _ in halo], query_rows, cotangent, key_rows, value_rows)
    output_rows, grad_query, grad_key, grad_value, diag = outs
    diag = diag.reshape(filters, width)
    top = min(taps_total, base + BLK)
    taps_grad = jnp.flip(diag[:, base + BLK - top : base + BLK], 1)
    taps_grad = taps_grad * (1.0 / (tok_rows * lax.axis_size("seq")))
    grad_filter = doubled_total(taps_grad, ("seq", "head"))
    if top < taps_total:
        grad_filter = jnp.pad(grad_filter, ((0, 0), (0, taps_total - top)))
    return output_rows, grad_query, grad_key, grad_value, grad_filter


def per_device(value_rows, key_rows, query_rows, cotangent, filter_taps, doc_blocks):
    tok_rows = value_rows.shape[0]
    taps_total = filter_taps.shape[1]
    full_lags = taps_total // BLK + 1
    short_lags = min(MOST, full_lags)
    nb = tok_rows // BLK
    rows = (value_rows, key_rows, query_rows, cotangent, filter_taps)
    short_args = rows + tables_and_links(filter_taps, doc_blocks, nb, short_lags)
    nblk = doc_blocks.shape[0]
    apart = np.abs(np.arange(nblk)[:, None] - np.arange(nblk)[None, :])
    far_pairs = jnp.asarray((apart >= short_lags) & (apart < full_lags))
    same = doc_blocks[:, None] == doc_blocks[None, :]
    long_links = jnp.any(same & far_pairs)
    outs = lax.cond(
        long_links,
        lambda a, b: convolve_all(
            *a[:-1], *tables_and_links(a[4], a[-1], nb, full_lags), full_lags
        ),
        lambda a, b: convolve_all(*b, short_lags),
        rows + (doc_blocks,),
        short_args,
    )
    return tuple(outs)


def doubled_total(value, axes):
    for axis in axes:
        length = lax.axis_size(axis)
        bits = (length - 1).bit_length()
        for low in range(0, bits, 2):
            group = [1 << low] + ([1 << (low + 1)] if low + 1 < bits else [])
            swap = lambda m: lax.ppermute(value, axis, [(i, i ^ m) for i in range(length)])
            if len(group) == 1:
                value = value + swap(group[0])
            else:
                a, b = group
                value = (value + swap(a)) + (swap(b) + swap(a | b))
    return value


def solution(mesh):
    in_specs = (P("seq", "head"), P("seq", "head"), P("seq", "head"), P("seq", "head"), P(), P())
    out_specs = (P("seq", "head"), P("seq", "head"), P("seq", "head"), P("seq", "head"), P())
    return jax.shard_map(
        per_device, mesh=mesh, in_specs=in_specs, out_specs=out_specs, check_vma=False
    )
```
